256 devices in a mesh: ctx: 64 (over z, y, x_lo), tp: 4 (over x_hi, core).
Axes of the slice: x: 4 (x_hi: 2, x_lo: 2; x = x_hi * 2 + x_lo), y: 4, z: 8, core: 2. Of those that a mesh axis runs over, the one named last changes fastest.
Arguments:
- hidden_in: bfloat16 [8192, 4096], P('ctx', 'tp'), may hold values from -6 to 6
- w_query: bfloat16 [4096, 2048], P(None, 'tp'), may hold values from -8 to 8, as said below
- w_key: bfloat16 [4096, 2048], P(None, 'tp'), may hold values from -8 to 8, as said below
- w_value: bfloat16 [4096, 2048], P(None, 'tp'), may hold values from -0.09375 to 0.09375
- query_gain: float32 [2048], P('tp'), may hold values from 0.1 to 1.9
- key_gain: float32 [2048], P('tp'), may hold values from 0.1 to 1.9
- prompt_lengths: int32 [4], replicated, may hold values from 1 to 4096, 8192 in all
Outputs:
- attn_out: bfloat16 [8192, 2048], P('ctx', 'tp')
- key_cache: bfloat16 [8192, 2048], P('ctx', 'tp')
- value_cache: bfloat16 [8192, 2048], P('ctx', 'tp')
The draws below stay inside these ranges and needn't reach their ends.
Inputs may be any that keep to these rules, and one draw needn't show every extreme that they name: `prompt_lengths`: lengths of the 4 prompts in order; they sum to 8192 and the longest holds exactly half of 8192. `w_query`: a projection matrix of 4096 rows. `w_key`: a projection matrix of 4096 rows.
All inputs are finite; a program needn't handle non-finite values.
Results may differ from the reference program's by a relative error of at most 0.0075.
Values may be sent and summed in bfloat16 or wider, within the bound.
No kernel may reach another device: no remote copies, remote signals or barrier semaphores. Data moves between devices by JAX's collectives and lax.ppermute only.
A program may use at most 128 MiB of HBM per device.

```python
import math
import jax
import jax.numpy as jnp
import numpy as np
from jax import lax

D = 4096
HEADS = 16
HD = 128
REQS = 4
TOK_DEV = 128
TOKENS = 8192
N_CTX = 64


def paired_weights(key):
    base = jax.random.fold_in(key, 31)
    key_first = jax.random.fold_in(base, 0)
    key_second = jax.random.fold_in(base, 1)
    key_scale = jax.random.fold_in(base, 3)
    columns = HEADS * HD
    w_first = jnp.clip(jax.random.normal(key_first, (D, columns), jnp.float32), -3.0, 3.0) * D ** (-0.5)
    w_second = jnp.clip(jax.random.normal(key_second, (D, columns), jnp.float32), -3.0, 3.0) * D ** (-0.5)
    spread = jnp.exp(jax.random.uniform(key_scale, (2, HEADS), jnp.float32, -0.7, 0.7))
    query_part = w_first * jnp.repeat(spread[0], HD)[None, :]
    key_part = w_second * jnp.repeat(spread[1], HD)[None, :]
    return (query_part, key_part)


def draw_w_query(key, part):
    return paired_weights(key)[0].astype(jnp.bfloat16)


def draw_w_key(key, part):
    return paired_weights(key)[1].astype(jnp.bfloat16)


def block_levels(rng, shape, pieces, low, top_value):
    def one(dim, parts):
        draws = jax.random.uniform(jax.random.fold_in(jax.random.fold_in(rng, 6), dim), (parts,), jnp.float32, low / len(pieces), top_value / len(pieces))
        return jnp.repeat(jnp.exp(draws), shape[dim] // parts).reshape((-1,) + (1,) * (len(shape) - dim - 1))

    factor_of = one(*pieces[0])
    for cut in pieces[1:]:
        factor_of = factor_of * one(*cut)
    return factor_of


def profile(amount, total, limit, slope):
    portions = [(1 << 20) // math.isqrt(standing ** slope) + 1 for standing in range(2, amount + 1)]
    surplus, holding = total - limit - (amount - 1), [1] * (amount - 1)
    while surplus > 0:
        candidates = [i for i in range(amount - 1) if holding[i] < limit]
        mass, left = sum([portions[i] for i in candidates]), surplus
        for i in candidates:
            extra = min(limit - holding[i], max(1, left * portions[i] // mass), surplus)
            holding[i] = holding[i] + extra
            surplus = surplus - extra
    return np.array([limit] + holding)


def uneven_parts(key, number_of, total, reach, lean):
    if number_of == 2:
        one = jax.random.randint(key, (), max(1, total - reach), min(reach, total - 1) + 1)
        return jnp.stack([one, total - one])
    lengths = jnp.asarray(profile(number_of, total, reach, lean), jnp.int32)
    pairs = (number_of - 1) // 2
    donor, sink = lengths[1:1 + 2 * pairs:2], lengths[2:2 + 2 * pairs:2]
    slack = jnp.minimum(donor - 1, reach - sink)
    shifted = jax.random.randint(jax.random.fold_in(key, 1), (pairs,), 0, 1 << 20) % (slack + 1)
    lengths = lengths.at[1:1 + 2 * pairs:2].set(donor - shifted).at[2:2 + 2 * pairs:2].set(sink + shifted)
    return lengths[jax.random.permutation(jax.random.fold_in(key, 2), number_of)]


def centred(own_key, dims, deviation, bound, cuts=(), kind=jnp.bfloat16):
    entries = jax.random.normal(own_key, dims, jnp.float32) * deviation
    if len(cuts) > 0:
        entries = block_levels(own_key, dims, cuts, -0.22, 0.18) * entries
    return jnp.clip(entries, min=-bound, max=bound).astype(kind)


def setup_inputs(seed: int = 0) -> dict:
    keys = jax.random.split(jax.random.key(seed), 8)
    return {
        "hidden_in": centred(keys[0], (TOKENS, D), 1.0, 6.0, ((0, 64), (1, 4))),
        "w_query": draw_w_query(jax.random.fold_in(keys[7], 71), 0),
        "w_key": draw_w_key(jax.random.fold_in(keys[7], 71), 0),
        "w_value": centred(keys[3], (D, HEADS * HD), D ** -0.5, 0.09375, ((1, 4),)),
        "query_gain": jnp.clip(1.0 + 0.18 * jax.random.normal(keys[4], (HEADS * HD,), jnp.float32), 0.1, 1.9),
        "key_gain": jnp.clip(1.0 + 0.18 * jax.random.normal(keys[5], (HEADS * HD,), jnp.float32), 0.1, 1.9),
        "prompt_lengths": uneven_parts(keys[6], REQS, TOKENS, TOKENS // 2, 2).astype(jnp.int32),
    }


def normalize(matrix, gains):
    return matrix * lax.rsqrt(lax.optimization_barrier(jnp.mean(matrix * matrix, axis=-1, keepdims=True)) + 1e-06) * gains

def rotate(matrix, position):
    row_count, columns = matrix.shape
    head_count = columns // HD
    rot_half = HD // 2
    shaped = matrix.reshape(row_count, head_count, HD)
    inverse_freq = 500000.0 ** (-2.0 * jnp.arange(rot_half, dtype=jnp.float32) / HD)
    angles = position.astype(jnp.float32)[:, None] * inverse_freq[None, :]
    cosine = jnp.cos(angles)[:, None, :]
    sine_part = jnp.sin(angles)[:, None, :]
    first_part = shaped[..., :rot_half]
    second_part = shaped[..., rot_half:]
    turned = jnp.concatenate([first_part * cosine - second_part * sine_part, second_part * cosine + first_part * sine_part], axis=-1)
    return turned.reshape(row_count, columns).astype(jnp.bfloat16)

def reference(hidden_in, w_query, w_key, w_value, query_gain, key_gain, prompt_lengths):
    half_rows = TOK_DEV // 2
    columns = HEADS * HD
    blocks = hidden_in.reshape(N_CTX, 2, half_rows, D)
    natural = jnp.concatenate([blocks[:, 0].reshape(N_CTX * half_rows, D), blocks[::-1, 1].reshape(N_CTX * half_rows, D)], axis=0)
    queries = jnp.dot(natural, w_query, preferred_element_type=jnp.float32)
    keys_proj = jnp.dot(natural, w_key, preferred_element_type=jnp.float32)
    values = jnp.dot(natural, w_value, preferred_element_type=jnp.float32).astype(jnp.bfloat16)
    token_ids = jnp.arange(TOKENS, dtype=jnp.int32)
    req_ends = jnp.cumsum(prompt_lengths).astype(jnp.int32)
    starts = (req_ends - prompt_lengths).astype(jnp.int32)
    request = lax.optimization_barrier(jnp.sum((token_ids[:, None] >= req_ends[None, :]).astype(jnp.int32), axis=1))
    onehot = request[:, None] == jnp.arange(REQS, dtype=jnp.int32)[None, :]
    position = (token_ids - lax.optimization_barrier(jnp.sum(jnp.where(onehot, starts[None, :], 0), axis=1))).astype(jnp.int32)
    query_rot = rotate(normalize(queries, query_gain), position)
    key_rot = rotate(normalize(keys_proj, key_gain), position)
    score_scale = HD ** (-0.5)
    q_block = math.gcd(TOKENS, 1024)
    outputs = []
    for block_index in range(TOKENS // q_block):
        row_start = block_index * q_block
        row_end = row_start + q_block
        visible = (request[row_start:row_end, None] == request[None, :row_end]) & (token_ids[None, :row_end] <= token_ids[row_start:row_end, None])
        query_heads = query_rot[row_start:row_end].reshape(q_block, HEADS, HD).transpose(1, 0, 2)
        key_heads = key_rot[:row_end].reshape(row_end, HEADS, HD).transpose(1, 0, 2)
        value_heads = values[:row_end].reshape(row_end, HEADS, HD).transpose(1, 0, 2)

        def one_head(operands, visible=visible):
            query_one, key_one, value_one = operands
            scores = jnp.dot(query_one, key_one.T, preferred_element_type=jnp.float32) * score_scale
            masked = jnp.where(visible, scores, -1e+30)
            row_peak = lax.optimization_barrier(jnp.max(masked, axis=1, keepdims=True))
            weights = jnp.where(visible, jnp.exp(masked - row_peak), 0.0)
            totals = lax.optimization_barrier(jnp.sum(weights, axis=1, keepdims=True))
            mixed = jnp.dot(weights.astype(jnp.bfloat16), value_one, preferred_element_type=jnp.float32)
            return mixed / totals
        per_head = lax.map(one_head, (query_heads, key_heads, value_heads))
        outputs.append(per_head.transpose(1, 0, 2).reshape(q_block, columns))
    attended = jnp.concatenate(outputs, axis=0).astype(jnp.bfloat16)
    out_blocks = attended.reshape(2 * N_CTX, half_rows, columns)
    mirrored = jnp.stack([out_blocks[:N_CTX], out_blocks[N_CTX:][::-1]], axis=1).reshape(TOKENS, columns)
    key_cache = key_rot.reshape(TOK_DEV, N_CTX, columns).transpose(1, 0, 2).reshape(TOKENS, columns)
    value_cache = values.reshape(TOK_DEV, N_CTX, columns).transpose(1, 0, 2).reshape(TOKENS, columns)
    return (mirrored, key_cache, value_cache)
```

```python
import functools

import jax
import jax.numpy as jnp
from jax import lax
from jax.experimental import pallas as pl
from jax.experimental.pallas import tpu as pltpu
from jax.sharding import Mesh
from jax.sharding import PartitionSpec as P

HD = 128
KB = 256
CL = ("ylo", "xlo")
CTX = ("z", "yhi", "ylo", "xlo")


def rotate(matrix, position):
    row_count, columns = matrix.shape
    head_count = columns // HD
    rot_half = HD // 2
    shaped = matrix.reshape(row_count, head_count, HD)
    inverse_freq = 500000.0 ** (-2.0 * jnp.arange(rot_half, dtype=jnp.float32) / HD)
    angles = position.astype(jnp.float32)[:, None] * inverse_freq[None, :]
    cosine = jnp.cos(angles)[:, None, :]
    sine_part = jnp.sin(angles)[:, None, :]
    first_part = shaped[..., :rot_half]
    second_part = shaped[..., rot_half:]
    turned = jnp.concatenate(
        [
            first_part * cosine - second_part * sine_part,
            second_part * cosine + first_part * sine_part,
        ],
        axis=-1,
    )
    return turned.reshape(row_count, columns).astype(jnp.bfloat16)


def request_start(token_ids, prompt_lengths):
    req_ends = jnp.cumsum(prompt_lengths)
    starts = req_ends - prompt_lengths
    request = jnp.sum((token_ids[:, None] >= req_ends[None, :]).astype(jnp.int32), axis=1)
    onehot = request[:, None] == jnp.arange(prompt_lengths.shape[0], dtype=jnp.int32)[None, :]
    return jnp.sum(jnp.where(onehot, starts[None, :], 0), axis=1)


def attn_kernel(info_ref, q_ref, kv_ref, qtok_ref, qlo_ref, o_ref):
    blk = pl.program_id(0)
    lo = info_ref[2 * blk]
    hi = info_ref[2 * blk + 1]
    shift = info_ref[4]
    groups = info_ref[5]
    nblocks = 2 * groups
    q = q_ref[...]
    qtok = qtok_ref[...]
    qlo = qlo_ref[...]
    rows = q.shape[0]
    scale = HD ** (-0.5)

    def body(kb, carry):
        peak, total, acc = carry
        upper = kb >= groups
        group = jnp.where(upper, nblocks - 1 - kb, kb)
        slot = (group - shift + groups) % groups
        start = pl.multiple_of((slot * 2 + upper.astype(jnp.int32)) * KB, KB)
        block = kv_ref[pl.ds(start, KB), :]
        keys = block[:, :HD]
        vals = block[:, HD:]
        scores = (
            lax.dot_general(q, keys, (((1,), (1,)), ((), ())), preferred_element_type=jnp.float32)
            * scale
        )
        ktok = kb * KB + lax.broadcasted_iota(jnp.int32, (1, KB), 1)
        visible = (ktok >= qlo) & (ktok <= qtok)
        masked = jnp.where(visible, scores, -1e30)
        new_peak = jnp.maximum(peak, jnp.max(masked, axis=1, keepdims=True))
        weights = jnp.where(visible, jnp.exp(masked - new_peak), 0.0)
        factor = jnp.exp(peak - new_peak)
        total = total * factor + jnp.sum(weights, axis=1, keepdims=True)
        acc = acc * factor + jnp.dot(
            weights.astype(jnp.bfloat16), vals, preferred_element_type=jnp.float32
        )
        return new_peak, total, acc

    start_state = (
        jnp.full((rows, 1), -1e30, jnp.float32),
        jnp.zeros((rows, 1), jnp.float32),
        jnp.zeros((rows, HD), jnp.float32),
    )
    _, total, acc = lax.fori_loop(lo, hi + 1, body, start_state)
    o_ref[...] = (acc / total).astype(o_ref.dtype)


def attention(info, q, kv, qtok, qlo):
    rows = q.shape[0]
    half = rows // 2
    return pl.pallas_call(
        attn_kernel,
        out_shape=jax.ShapeDtypeStruct((rows, HD), jnp.bfloat16),
        grid_spec=pltpu.PrefetchScalarGridSpec(
            num_scalar_prefetch=1,
            grid=(2,),
            in_specs=[
                pl.BlockSpec((half, HD), lambda i, info: (i, 0)),
                pl.BlockSpec(kv.shape, lambda i, info: (0, 0)),
                pl.BlockSpec((half, 1), lambda i, info: (i, 0)),
                pl.BlockSpec((half, 1), lambda i, info: (i, 0)),
            ],
            out_specs=pl.BlockSpec((half, HD), lambda i, info: (i, 0)),
        ),
    )(info, q, kv, qtok, qlo)


def z_ring(part, n):
    fwd = [part]
    bwd = [part]
    steps = n // 2
    for step in range(1, steps + 1):
        if step < steps:
            fwd.append(lax.ppermute(fwd[-1], "z", [(i, (i + 1) % n) for i in range(n)]))
            bwd.append(lax.ppermute(bwd[-1], "z", [(i, (i - 1) % n) for i in range(n)]))
        else:
            cut = part.shape[0] // 2
            far_a = lax.ppermute(fwd[-1][:cut], "z", [(i, (i + 1) % n) for i in range(n)])
            far_b = lax.ppermute(bwd[-1][cut:], "z", [(i, (i - 1) % n) for i in range(n)])
    ordered = bwd[: steps] + [far_a, far_b] + fwd[1:steps][::-1]
    return jnp.concatenate(ordered, axis=0)


def per_device(hidden_in, w_query, w_key, w_value, query_gain, key_gain, prompt_lengths):
    tok_rows = hidden_in.shape[0]
    half_rows = tok_rows // 2
    local_width = w_query.shape[1]
    head_count = local_width // HD
    nz = lax.axis_size("z")
    nyh = lax.axis_size("yhi")
    ncl = lax.axis_size("ylo") * lax.axis_size("xlo")
    z_idx = lax.axis_index("z")
    cg = z_idx * nyh + lax.axis_index("yhi")
    cl = lax.axis_index("ylo") * lax.axis_size("xlo") + lax.axis_index("xlo")
    groups = nz * nyh
    ctx_count = groups * ncl
    own = cg * ncl + cl

    pieces = lax.all_gather(hidden_in, "tp", axis=1, tiled=True)
    queries = jnp.dot(pieces, w_query, preferred_element_type=jnp.float32)
    keys_proj = jnp.dot(pieces, w_key, preferred_element_type=jnp.float32)
    values = jnp.dot(pieces, w_value, preferred_element_type=jnp.float32).astype(jnp.bfloat16)
    query_sq, key_sq = lax.psum(
        (jnp.sum(queries * queries, axis=1), jnp.sum(keys_proj * keys_proj, axis=1)), "tp"
    )
    full_width = local_width * lax.axis_size("tp")
    query_normed = queries * lax.rsqrt(query_sq[:, None] / full_width + 1e-06) * query_gain
    key_normed = keys_proj * lax.rsqrt(key_sq[:, None] / full_width + 1e-06) * key_gain
    local_rows = jnp.arange(tok_rows, dtype=jnp.int32)
    block_of = jnp.where(local_rows < half_rows, own, 2 * ctx_count - 1 - own)
    token_ids = block_of * half_rows + local_rows % half_rows
    position = token_ids - request_start(token_ids, prompt_lengths)
    query_rot = rotate(query_normed, position)
    key_rot = rotate(key_normed, position)

    packed = jnp.concatenate(
        [
            query_rot.reshape(tok_rows, head_count, HD),
            key_rot.reshape(tok_rows, head_count, HD),
            values.reshape(tok_rows, head_count, HD),
        ],
        axis=2,
    )
    got = lax.all_to_all(packed, CL, split_axis=1, concat_axis=0, tiled=True)
    got = got.reshape(ncl, tok_rows, 3 * HD)
    lower = got[:, :half_rows].reshape(ncl * half_rows, 3 * HD)
    upper = got[::-1, half_rows:].reshape(ncl * half_rows, 3 * HD)
    mine = jnp.concatenate([lower, upper], axis=0)
    q_head = mine[:, :HD]
    kv_mine = mine[:, HD:]

    kv_pair = lax.all_gather(kv_mine, "yhi", axis=0, tiled=True)
    kv_all = z_ring(kv_pair, nz)

    span = ncl * half_rows
    total_tokens = 2 * ctx_count * half_rows
    r = jnp.arange(span, dtype=jnp.int32)
    q_tokens = jnp.concatenate([cg * span + r, total_tokens - (cg + 1) * span + r])
    q_lo = request_start(q_tokens, prompt_lengths)
    info = jnp.stack(
        [
            q_lo[0] // KB,
            cg,
            q_lo[span] // KB,
            2 * groups - 1 - cg,
            (z_idx * nyh) % groups,
            jnp.asarray(groups, jnp.int32),
        ]
    ).astype(jnp.int32)
    out_head = attention(info, q_head, kv_all, q_tokens[:, None], q_lo[:, None])

    out_lower = out_head[:span].reshape(ncl, half_rows, HD)
    out_upper = out_head[span:].reshape(ncl, half_rows, HD)[::-1]
    out_send = jnp.stack([out_lower, out_upper], axis=1).reshape(ncl, tok_rows, HD)

    picked = kv_all.reshape(groups, 2, ncl, half_rows, 2 * HD)
    picked = lax.dynamic_slice_in_dim(picked, cg * ncl, ncl, axis=3)
    doubled = jnp.concatenate([picked, picked], axis=0)
    natural = lax.dynamic_slice_in_dim(doubled, (groups - (z_idx * nyh) % groups) % groups, groups, axis=0)
    cache_lower = natural[:, 0].reshape(groups * ncl, ncl, 2 * HD)
    cache_upper = natural[::-1, 1].reshape(groups * ncl, ncl, 2 * HD)
    cache = jnp.concatenate([cache_lower, cache_upper], axis=0).transpose(1, 0, 2)
    send = jnp.concatenate([out_send, cache], axis=2)
    recv = lax.all_to_all(send, CL, split_axis=0, concat_axis=0, tiled=True)
    recv = recv.transpose(1, 0, 2)
    attn_out = recv[:, :, :HD].reshape(tok_rows, local_width)
    key_cache = recv[:, :, HD : 2 * HD].reshape(tok_rows, local_width)
    value_cache = recv[:, :, 2 * HD :].reshape(tok_rows, local_width)
    return attn_out, key_cache, value_cache


def solution(mesh):
    ctx_size = mesh.shape["ctx"]
    tp_size = mesh.shape["tp"]
    nz = 8
    split = Mesh(
        mesh.devices.reshape(nz, 2, 2, ctx_size // (nz * 4), tp_size), ("z", "yhi", "ylo", "xlo", "tp")
    )
    rows = P(CTX, "tp")
    placed = (rows, P(None, "tp"), P(None, "tp"), P(None, "tp"), P("tp"), P("tp"), P())
    return jax.shard_map(
        per_device,
        mesh=split,
        in_specs=placed,
        out_specs=(rows, rows, rows),
        check_vma=False,
    )
```

```python
import functools

import jax
import jax.numpy as jnp
from jax import lax
from jax.experimental import pallas as pl
from jax.experimental.pallas import tpu as pltpu
from jax.sharding import Mesh
from jax.sharding import PartitionSpec as P

HD = 128
KB = 256
CL = ("ylo", "xlo")
CTX = ("z", "yhi", "ylo", "xlo")
TP = ("xhi", "core")


def rotate(matrix, position):
    row_count, columns = matrix.shape
    head_count = columns // HD
    rot_half = HD // 2
    shaped = matrix.reshape(row_count, head_count, HD)
    inverse_freq = 500000.0 ** (-2.0 * jnp.arange(rot_half, dtype=jnp.float32) / HD)
    angles = position.astype(jnp.float32)[:, None] * inverse_freq[None, :]
    cosine = jnp.cos(angles)[:, None, :]
    sine_part = jnp.sin(angles)[:, None, :]
    first_part = shaped[..., :rot_half]
    second_part = shaped[..., rot_half:]
    turned = jnp.concatenate(
        [
            first_part * cosine - second_part * sine_part,
            second_part * cosine + first_part * sine_part,
        ],
        axis=-1,
    )
    return turned.reshape(row_count, columns).astype(jnp.bfloat16)


def request_start(token_ids, prompt_lengths):
    req_ends = jnp.cumsum(prompt_lengths)
    starts = req_ends - prompt_lengths
    request = jnp.sum((token_ids[:, None] >= req_ends[None, :]).astype(jnp.int32), axis=1)
    onehot = request[:, None] == jnp.arange(prompt_lengths.shape[0], dtype=jnp.int32)[None, :]
    return jnp.sum(jnp.where(onehot, starts[None, :], 0), axis=1)


def attn_kernel(info_ref, q_ref, kv_ref, qtok_ref, qlo_ref, o_ref):
    blk = pl.program_id(0)
    lo = info_ref[2 * blk]
    hi = info_ref[2 * blk + 1]
    shift = info_ref[4]
    groups = info_ref[5]
    nblocks = 2 * groups
    q = q_ref[...]
    qtok = qtok_ref[...]
    qlo = qlo_ref[...]
    rows = q.shape[0]
    scale = HD ** (-0.5)

    def body(kb, carry):
        peak, total, acc = carry
        upper = kb >= groups
        group = jnp.where(upper, nblocks - 1 - kb, kb)
        slot = (group - shift + groups) % groups
        start = pl.multiple_of((slot * 2 + upper.astype(jnp.int32)) * KB, KB)
        block = kv_ref[pl.ds(start, KB), :]
        keys = block[:, :HD]
        vals = block[:, HD:]
        scores = (
            lax.dot_general(q, keys, (((1,), (1,)), ((), ())), preferred_element_type=jnp.float32)
            * scale
        )
        ktok = kb * KB + lax.broadcasted_iota(jnp.int32, (1, KB), 1)
        visible = (ktok >= qlo) & (ktok <= qtok)
        masked = jnp.where(visible, scores, -1e30)
        new_peak = jnp.maximum(peak, jnp.max(masked, axis=1, keepdims=True))
        weights = jnp.where(visible, jnp.exp(masked - new_peak), 0.0)
        factor = jnp.exp(peak - new_peak)
        total = total * factor + jnp.sum(weights, axis=1, keepdims=True)
        acc = acc * factor + jnp.dot(
            weights.astype(jnp.bfloat16), vals, preferred_element_type=jnp.float32
        )
        return new_peak, total, acc

    start_state = (
        jnp.full((rows, 1), -1e30, jnp.float32),
        jnp.zeros((rows, 1), jnp.float32),
        jnp.zeros((rows, HD), jnp.float32),
    )
    _, total, acc = lax.fori_loop(lo, hi + 1, body, start_state)
    o_ref[...] = (acc / total).astype(o_ref.dtype)


def attention(info, q, kv, qtok, qlo):
    rows = q.shape[0]
    half = rows // 2
    return pl.pallas_call(
        attn_kernel,
        out_shape=jax.ShapeDtypeStruct((rows, HD), jnp.bfloat16),
        grid_spec=pltpu.PrefetchScalarGridSpec(
            num_scalar_prefetch=1,
            grid=(2,),
            in_specs=[
                pl.BlockSpec((half, HD), lambda i, info: (i, 0)),
                pl.BlockSpec(kv.shape, lambda i, info: (0, 0)),
                pl.BlockSpec((half, 1), lambda i, info: (i, 0)),
                pl.BlockSpec((half, 1), lambda i, info: (i, 0)),
            ],
            out_specs=pl.BlockSpec((half, HD), lambda i, info: (i, 0)),
        ),
    )(info, q, kv, qtok, qlo)


def z_ring(part, n):
    fwd = [part]
    bwd = [part]
    steps = n // 2
    for step in range(1, steps + 1):
        if step < steps:
            fwd.append(lax.ppermute(fwd[-1], "z", [(i, (i + 1) % n) for i in range(n)]))
            bwd.append(lax.ppermute(bwd[-1], "z", [(i, (i - 1) % n) for i in range(n)]))
        else:
            cut = part.shape[0] // 2
            far_a = lax.ppermute(fwd[-1][:cut], "z", [(i, (i + 1) % n) for i in range(n)])
            far_b = lax.ppermute(bwd[-1][cut:], "z", [(i, (i - 1) % n) for i in range(n)])
    ordered = bwd[: steps] + [far_a, far_b] + fwd[1:steps][::-1]
    return jnp.concatenate(ordered, axis=0)


def per_device(hidden_in, w_query, w_key, w_value, query_gain, key_gain, prompt_lengths):
    tok_rows = hidden_in.shape[0]
    half_rows = tok_rows // 2
    local_width = w_query.shape[1]
    head_count = local_width // HD
    nz = lax.axis_size("z")
    nyh = lax.axis_size("yhi")
    ncl = lax.axis_size("ylo") * lax.axis_size("xlo")
    z_idx = lax.axis_index("z")
    cg = z_idx * nyh + lax.axis_index("yhi")
    cl = lax.axis_index("ylo") * lax.axis_size("xlo") + lax.axis_index("xlo")
    groups = nz * nyh
    ctx_count = groups * ncl
    own = cg * ncl + cl

    xh = lax.axis_index("xhi")
    core = lax.axis_index("core")
    swap = [(0, 1), (1, 0)]
    across = lax.ppermute(hidden_in, "xhi", swap)
    pair = jnp.where(xh == 0, jnp.concatenate([hidden_in, across], axis=1), jnp.concatenate([across, hidden_in], axis=1))
    other = lax.ppermute(pair, "core", swap)
    width = hidden_in.shape[1]
    mine_first = jnp.concatenate([pair[:, :width], other[:, :width], pair[:, width:], other[:, width:]], axis=1)
    theirs_first = jnp.concatenate([other[:, :width], pair[:, :width], other[:, width:], pair[:, width:]], axis=1)
    pieces = jnp.where(core == 0, mine_first, theirs_first)
    queries = jnp.dot(pieces, w_query, preferred_element_type=jnp.float32)
    keys_proj = jnp.dot(pieces, w_key, preferred_element_type=jnp.float32)
    values = jnp.dot(pieces, w_value, preferred_element_type=jnp.float32).astype(jnp.bfloat16)
    squares = jnp.stack([jnp.sum(queries * queries, axis=1), jnp.sum(keys_proj * keys_proj, axis=1)])
    squares = squares + lax.ppermute(squares, "xhi", swap)
    squares = squares + lax.ppermute(squares, "core", swap)
    query_sq = squares[0]
    key_sq = squares[1]
    full_width = local_width * lax.axis_size("xhi") * lax.axis_size("core")
    query_normed = queries * lax.rsqrt(query_sq[:, None] / full_width + 1e-06) * query_gain
    key_normed = keys_proj * lax.rsqrt(key_sq[:, None] / full_width + 1e-06) * key_gain
    local_rows = jnp.arange(tok_rows, dtype=jnp.int32)
    block_of = jnp.where(local_rows < half_rows, own, 2 * ctx_count - 1 - own)
    token_ids = block_of * half_rows + local_rows % half_rows
    position = token_ids - request_start(token_ids, prompt_lengths)
    query_rot = rotate(query_normed, position)
    key_rot = rotate(key_normed, position)

    packed = jnp.concatenate(
        [
            query_rot.reshape(tok_rows, head_count, HD),
            key_rot.reshape(tok_rows, head_count, HD),
            values.reshape(tok_rows, head_count, HD),
        ],
        axis=2,
    )
    got = lax.all_to_all(packed, CL, split_axis=1, concat_axis=0, tiled=True)
    got = got.reshape(ncl, tok_rows, 3 * HD)
    lower = got[:, :half_rows].reshape(ncl * half_rows, 3 * HD)
    upper = got[::-1, half_rows:].reshape(ncl * half_rows, 3 * HD)
    mine = jnp.concatenate([lower, upper], axis=0)
    q_head = mine[:, :HD]
    kv_mine = mine[:, HD:]

    yh = lax.axis_index("yhi")
    kv_other = lax.ppermute(kv_mine, "yhi", swap)
    kv_pair = jnp.where(yh == 0, jnp.concatenate([kv_mine, kv_other], axis=0), jnp.concatenate([kv_other, kv_mine], axis=0))
    kv_all = z_ring(kv_pair, nz)

    span = ncl * half_rows
    total_tokens = 2 * ctx_count * half_rows
    r = jnp.arange(span, dtype=jnp.int32)
    q_tokens = jnp.concatenate([cg * span + r, total_tokens - (cg + 1) * span + r])
    q_lo = request_start(q_tokens, prompt_lengths)
    info = jnp.stack(
        [
            q_lo[0] // KB,
            cg,
            q_lo[span] // KB,
            2 * groups - 1 - cg,
            (z_idx * nyh) % groups,
            jnp.asarray(groups, jnp.int32),
        ]
    ).astype(jnp.int32)
    out_head = attention(info, q_head, kv_all, q_tokens[:, None], q_lo[:, None])

    out_lower = out_head[:span].reshape(ncl, half_rows, HD)
    out_upper = out_head[span:].reshape(ncl, half_rows, HD)[::-1]
    out_send = jnp.stack([out_lower, out_upper], axis=1).reshape(ncl, tok_rows, HD)

    picked = kv_all.reshape(groups, 2, ncl, half_rows, 2 * HD)
    picked = lax.dynamic_slice_in_dim(picked, cg * ncl, ncl, axis=3)
    doubled = jnp.concatenate([picked, picked], axis=0)
    natural = lax.dynamic_slice_in_dim(doubled, (groups - (z_idx * nyh) % groups) % groups, groups, axis=0)
    cache_lower = natural[:, 0].reshape(groups * ncl, ncl, 2 * HD)
    cache_upper = natural[::-1, 1].reshape(groups * ncl, ncl, 2 * HD)
    cache = jnp.concatenate([cache_lower, cache_upper], axis=0).transpose(1, 0, 2)
    send = jnp.concatenate([out_send, cache], axis=2)
    recv = lax.all_to_all(send, CL, split_axis=0, concat_axis=0, tiled=True)
    recv = recv.transpose(1, 0, 2)
    attn_out = recv[:, :, :HD].reshape(tok_rows, local_width)
    key_cache = recv[:, :, HD : 2 * HD].reshape(tok_rows, local_width)
    value_cache = recv[:, :, 2 * HD :].reshape(tok_rows, local_width)
    return attn_out, key_cache, value_cache


def solution(mesh):
    ctx_size = mesh.shape["ctx"]
    tp_size = mesh.shape["tp"]
    nz = 8
    split = Mesh(
        mesh.devices.reshape(nz, 2, 2, ctx_size // (nz * 4), tp_size // 2, 2),
        ("z", "yhi", "ylo", "xlo", "xhi", "core"),
    )
    rows = P(CTX, TP)
    placed = (rows, P(None, TP), P(None, TP), P(None, TP), P(TP), P(TP), P())
    return jax.shard_map(
        per_device,
        mesh=split,
        in_specs=placed,
        out_specs=(rows, rows, rows),
        check_vma=False,
    )
```

```python
import functools

import jax
import jax.numpy as jnp
from jax import lax
from jax.experimental import pallas as pl
from jax.experimental.pallas import tpu as pltpu
from jax.sharding import Mesh
from jax.sharding import PartitionSpec as P

HD = 128
KB = 256
CL = ("ylo", "xlo")
CTX = ("z", "yhi", "ylo", "xlo")
TP = ("xhi", "core")


def rotate(matrix, position):
    row_count, columns = matrix.shape
    head_count = columns // HD
    rot_half = HD // 2
    shaped = matrix.reshape(row_count, head_count, HD)
    inverse_freq = 500000.0 ** (-2.0 * jnp.arange(rot_half, dtype=jnp.float32) / HD)
    angles = position.astype(jnp.float32)[:, None] * inverse_freq[None, :]
    cosine = jnp.cos(angles)[:, None, :]
    sine_part = jnp.sin(angles)[:, None, :]
    first_part = shaped[..., :rot_half]
    second_part = shaped[..., rot_half:]
    turned = jnp.concatenate(
        [
            first_part * cosine - second_part * sine_part,
            second_part * cosine + first_part * sine_part,
        ],
        axis=-1,
    )
    return turned.reshape(row_count, columns).astype(jnp.bfloat16)


def request_start(token_ids, prompt_lengths):
    req_ends = jnp.cumsum(prompt_lengths)
    starts = req_ends - prompt_lengths
    request = jnp.sum((token_ids[:, None] >= req_ends[None, :]).astype(jnp.int32), axis=1)
    onehot = request[:, None] == jnp.arange(prompt_lengths.shape[0], dtype=jnp.int32)[None, :]
    return jnp.sum(jnp.where(onehot, starts[None, :], 0), axis=1)


def part_kernel(nb, info_ref, q_ref, kv_ref, qtok_ref, qlo_ref, m_in, l_in, acc_in, m_out, l_out, acc_out):
    blk = pl.program_id(0)
    lo = info_ref[nb + 2 * blk]
    hi = info_ref[nb + 2 * blk + 1]
    m_out[...] = m_in[...]
    l_out[...] = l_in[...]
    acc_out[...] = acc_in[...]
    scale = HD ** (-0.5)
    for j in range(nb):
        kb = info_ref[j]

        @pl.when((kb >= lo) & (kb <= hi))
        def _():
            block = kv_ref[j * KB : (j + 1) * KB, :]
            keys = block[:, :HD]
            vals = block[:, HD:]
            scores = (
                lax.dot_general(q_ref[...], keys, (((1,), (1,)), ((), ())), preferred_element_type=jnp.float32)
                * scale
            )
            ktok = kb * KB + lax.broadcasted_iota(jnp.int32, (1, KB), 1)
            visible = (ktok >= qlo_ref[...]) & (ktok <= qtok_ref[...])
            masked = jnp.where(visible, scores, -1e30)
            peak = m_out[...]
            new_peak = jnp.maximum(peak, jnp.max(masked, axis=1, keepdims=True))
            weights = jnp.where(visible, jnp.exp(masked - new_peak), 0.0)
            factor = jnp.exp(peak - new_peak)
            l_out[...] = l_out[...] * factor + jnp.sum(weights, axis=1, keepdims=True)
            acc_out[...] = acc_out[...] * factor + jnp.dot(
                weights.astype(jnp.bfloat16), vals, preferred_element_type=jnp.float32
            )
            m_out[...] = new_peak


def attend_part(info, q, kv, qtok, qlo, state):
    rows = q.shape[0]
    half = rows // 2
    nb = kv.shape[0] // KB
    row_spec = lambda width: pl.BlockSpec((half, width), lambda i, info: (i, 0))
    return pl.pallas_call(
        functools.partial(part_kernel, nb),
        out_shape=(
            jax.ShapeDtypeStruct((rows, 1), jnp.float32),
            jax.ShapeDtypeStruct((rows, 1), jnp.float32),
            jax.ShapeDtypeStruct((rows, HD), jnp.float32),
        ),
        grid_spec=pltpu.PrefetchScalarGridSpec(
            num_scalar_prefetch=1,
            grid=(2,),
            in_specs=[
                row_spec(HD),
                pl.BlockSpec(kv.shape, lambda i, info: (0, 0)),
                row_spec(1),
                row_spec(1),
                row_spec(1),
                row_spec(1),
                row_spec(HD),
            ],
            out_specs=(row_spec(1), row_spec(1), row_spec(HD)),
        ),
    )(info, q, kv, qtok, qlo, *state)


def z_ring(part, n):
    fwd = [part]
    bwd = [part]
    steps = n // 2
    arrived = [(0, part)]
    for step in range(1, steps + 1):
        if step < steps:
            bwd.append(lax.ppermute(bwd[-1], "z", [(i, (i - 1) % n) for i in range(n)]))
            fwd.append(lax.ppermute(fwd[-1], "z", [(i, (i + 1) % n) for i in range(n)]))
            arrived.append((step, bwd[-1]))
            arrived.append((n - step, fwd[-1]))
        else:
            cut = part.shape[0] // 2
            arrived.append((steps, lax.ppermute(fwd[-1][:cut], "z", [(i, (i + 1) % n) for i in range(n)])))
            arrived.append((steps, lax.ppermute(bwd[-1][cut:], "z", [(i, (i - 1) % n) for i in range(n)])))
    return arrived


def per_device(hidden_in, w_query, w_key, w_value, query_gain, key_gain, prompt_lengths):
    tok_rows = hidden_in.shape[0]
    half_rows = tok_rows // 2
    local_width = w_query.shape[1]
    head_count = local_width // HD
    nz = lax.axis_size("z")
    nyh = lax.axis_size("yhi")
    ncl = lax.axis_size("ylo") * lax.axis_size("xlo")
    z_idx = lax.axis_index("z")
    cg = z_idx * nyh + lax.axis_index("yhi")
    cl = lax.axis_index("ylo") * lax.axis_size("xlo") + lax.axis_index("xlo")
    groups = nz * nyh
    ctx_count = groups * ncl
    own = cg * ncl + cl

    xh = lax.axis_index("xhi")
    core = lax.axis_index("core")
    swap = [(0, 1), (1, 0)]
    across = lax.ppermute(hidden_in, "xhi", swap)
    pair = jnp.where(xh == 0, jnp.concatenate([hidden_in, across], axis=1), jnp.concatenate([across, hidden_in], axis=1))
    other = lax.ppermute(pair, "core", swap)
    width = hidden_in.shape[1]
    mine_first = jnp.concatenate([pair[:, :width], other[:, :width], pair[:, width:], other[:, width:]], axis=1)
    theirs_first = jnp.concatenate([other[:, :width], pair[:, :width], other[:, width:], pair[:, width:]], axis=1)
    pieces = jnp.where(core == 0, mine_first, theirs_first)
    queries = jnp.dot(pieces, w_query, preferred_element_type=jnp.float32)
    keys_proj = jnp.dot(pieces, w_key, preferred_element_type=jnp.float32)
    values = jnp.dot(pieces, w_value, preferred_element_type=jnp.float32).astype(jnp.bfloat16)
    squares = jnp.stack([jnp.sum(queries * queries, axis=1), jnp.sum(keys_proj * keys_proj, axis=1)])
    squares = squares + lax.ppermute(squares, "xhi", swap)
    squares = squares + lax.ppermute(squares, "core", swap)
    query_sq = squares[0]
    key_sq = squares[1]
    full_width = local_width * lax.axis_size("xhi") * lax.axis_size("core")
    query_normed = queries * lax.rsqrt(query_sq[:, None] / full_width + 1e-06) * query_gain
    key_normed = keys_proj * lax.rsqrt(key_sq[:, None] / full_width + 1e-06) * key_gain
    local_rows = jnp.arange(tok_rows, dtype=jnp.int32)
    block_of = jnp.where(local_rows < half_rows, own, 2 * ctx_count - 1 - own)
    token_ids = block_of * half_rows + local_rows % half_rows
    position = token_ids - request_start(token_ids, prompt_lengths)
    query_rot = rotate(query_normed, position)
    key_rot = rotate(key_normed, position)

    packed = jnp.concatenate(
        [
            query_rot.reshape(tok_rows, head_count, HD),
            key_rot.reshape(tok_rows, head_count, HD),
            values.reshape(tok_rows, head_count, HD),
        ],
        axis=2,
    )
    got = lax.all_to_all(packed, CL, split_axis=1, concat_axis=0, tiled=True)
    got = got.reshape(ncl, tok_rows, 3 * HD)
    lower = got[:, :half_rows].reshape(ncl * half_rows, 3 * HD)
    upper = got[::-1, half_rows:].reshape(ncl * half_rows, 3 * HD)
    mine = jnp.concatenate([lower, upper], axis=0)
    q_head = mine[:, :HD]
    kv_mine = mine[:, HD:]

    yh = lax.axis_index("yhi")
    kv_other = lax.ppermute(kv_mine, "yhi", swap)
    kv_pair = jnp.where(yh == 0, jnp.concatenate([kv_mine, kv_other], axis=0), jnp.concatenate([kv_other, kv_mine], axis=0))
    arrived = z_ring(kv_pair, nz)

    span = ncl * half_rows
    total_tokens = 2 * ctx_count * half_rows
    r = jnp.arange(span, dtype=jnp.int32)
    q_tokens = jnp.concatenate([cg * span + r, total_tokens - (cg + 1) * span + r])
    q_lo = request_start(q_tokens, prompt_lengths)
    bounds = jnp.stack([q_lo[0] // KB, cg, q_lo[span] // KB, 2 * groups - 1 - cg]).astype(jnp.int32)
    rows_q = 2 * span
    state = (
        jnp.full((rows_q, 1), -1e30, jnp.float32),
        jnp.zeros((rows_q, 1), jnp.float32),
        jnp.zeros((rows_q, HD), jnp.float32),
    )
    picked_parts = {}
    seen = {}
    for dist, part in arrived:
        first = seen.get(dist, 0)
        chunks = part.shape[0] // span
        seen[dist] = first + chunks // 2
        ids = []
        for j in range(chunks):
            group_j = (2 * ((z_idx + dist) % nz) + first + j // 2) % groups
            ids.append(group_j if j % 2 == 0 else 2 * groups - 1 - group_j)
        info = jnp.concatenate([jnp.stack(ids).astype(jnp.int32), bounds])
        state = attend_part(info, q_head, part, q_tokens[:, None], q_lo[:, None], state)
        sub = part.reshape(chunks // 2, 2, ncl, half_rows, 2 * HD)
        picked_parts.setdefault(dist, []).append(lax.dynamic_slice_in_dim(sub, cg * ncl, ncl, axis=3))
    _, total, acc = state
    out_head = (acc / total).astype(jnp.bfloat16)

    out_lower = out_head[:span].reshape(ncl, half_rows, HD)
    out_upper = out_head[span:].reshape(ncl, half_rows, HD)[::-1]
    out_send = jnp.stack([out_lower, out_upper], axis=1).reshape(ncl, tok_rows, HD)

    picked = jnp.concatenate([p for dist in range(nz) for p in picked_parts[dist]], axis=0)
    doubled = jnp.concatenate([picked, picked], axis=0)
    natural = lax.dynamic_slice_in_dim(doubled, (groups - (z_idx * nyh) % groups) % groups, groups, axis=0)
    cache_lower = natural[:, 0].reshape(groups * ncl, ncl, 2 * HD)
    cache_upper = natural[::-1, 1].reshape(groups * ncl, ncl, 2 * HD)
    cache = jnp.concatenate([cache_lower, cache_upper], axis=0).transpose(1, 0, 2)
    send = jnp.concatenate([out_send, cache], axis=2)
    recv = lax.all_to_all(send, CL, split_axis=0, concat_axis=0, tiled=True)
    recv = recv.transpose(1, 0, 2)
    attn_out = recv[:, :, :HD].reshape(tok_rows, local_width)
    key_cache = recv[:, :, HD : 2 * HD].reshape(tok_rows, local_width)
    value_cache = recv[:, :, 2 * HD :].reshape(tok_rows, local_width)
    return attn_out, key_cache, value_cache


def solution(mesh):
    ctx_size = mesh.shape["ctx"]
    tp_size = mesh.shape["tp"]
    nz = 8
    split = Mesh(
        mesh.devices.reshape(nz, 2, 2, ctx_size // (nz * 4), tp_size // 2, 2),
        ("z", "yhi", "ylo", "xlo", "xhi", "core"),
    )
    rows = P(CTX, TP)
    placed = (rows, P(None, TP), P(None, TP), P(None, TP), P(TP), P(TP), P())
    return jax.shard_map(
        per_device,
        mesh=split,
        in_specs=placed,
        out_specs=(rows, rows, rows),
        check_vma=False,
    )
```

```python
import functools

import jax
import jax.numpy as jnp
from jax import lax
from jax.experimental import pallas as pl
from jax.experimental.pallas import tpu as pltpu
from jax.sharding import Mesh
from jax.sharding import PartitionSpec as P

HD = 128
KB = 256
CL = ("ylo", "xlo")
CTX = ("z", "yhi", "ylo", "xlo")
TP = ("xhi", "core")


def rotate(matrix, position):
    row_count, columns = matrix.shape
    head_count = columns // HD
    rot_half = HD // 2
    shaped = matrix.reshape(row_count, head_count, HD)
    inverse_freq = 500000.0 ** (-2.0 * jnp.arange(rot_half, dtype=jnp.float32) / HD)
    angles = position.astype(jnp.float32)[:, None] * inverse_freq[None, :]
    cosine = jnp.cos(angles)[:, None, :]
    sine_part = jnp.sin(angles)[:, None, :]
    first_part = shaped[..., :rot_half]
    second_part = shaped[..., rot_half:]
    turned = jnp.concatenate(
        [
            first_part * cosine - second_part * sine_part,
            second_part * cosine + first_part * sine_part,
        ],
        axis=-1,
    )
    return turned.reshape(row_count, columns).astype(jnp.bfloat16)


def request_start(token_ids, prompt_lengths):
    req_ends = jnp.cumsum(prompt_lengths)
    starts = req_ends - prompt_lengths
    request = jnp.sum((token_ids[:, None] >= req_ends[None, :]).astype(jnp.int32), axis=1)
    onehot = request[:, None] == jnp.arange(prompt_lengths.shape[0], dtype=jnp.int32)[None, :]
    return jnp.sum(jnp.where(onehot, starts[None, :], 0), axis=1)


def attn_kernel(counts, info_ref, q_ref, qtok_ref, qlo_ref, *refs):
    parts = refs[: len(counts)]
    o_ref, m_ref, l_ref, acc_ref = refs[len(counts) :]
    blk = pl.program_id(0)
    total_blocks = sum(counts)
    lo = info_ref[total_blocks + 2 * blk]
    hi = info_ref[total_blocks + 2 * blk + 1]
    m_ref[...] = jnp.full(m_ref.shape, -1e30, jnp.float32)
    l_ref[...] = jnp.zeros(l_ref.shape, jnp.float32)
    acc_ref[...] = jnp.zeros(acc_ref.shape, jnp.float32)
    scale = HD ** (-0.5)
    slot = 0
    for part_ref, count in zip(parts, counts):
        for j in range(count):
            kb = info_ref[slot]
            slot += 1

            @pl.when((kb >= lo) & (kb <= hi))
            def _(kb=kb, part_ref=part_ref, j=j):
                block = part_ref[j * KB : (j + 1) * KB, :]
                keys = block[:, :HD]
                vals = block[:, HD:]
                scores = (
                    lax.dot_general(q_ref[...], keys, (((1,), (1,)), ((), ())), preferred_element_type=jnp.float32)
                    * scale
                )
                ktok = kb * KB + lax.broadcasted_iota(jnp.int32, (1, KB), 1)
                visible = (ktok >= qlo_ref[...]) & (ktok <= qtok_ref[...])
                masked = jnp.where(visible, scores, -1e30)
                peak = m_ref[...]
                new_peak = jnp.maximum(peak, jnp.max(masked, axis=1, keepdims=True))
                weights = jnp.where(visible, jnp.exp(masked - new_peak), 0.0)
                factor = jnp.exp(peak - new_peak)
                l_ref[...] = l_ref[...] * factor + jnp.sum(weights, axis=1, keepdims=True)
                acc_ref[...] = acc_ref[...] * factor + jnp.dot(
                    weights.astype(jnp.bfloat16), vals, preferred_element_type=jnp.float32
                )
                m_ref[...] = new_peak

    o_ref[...] = (acc_ref[...] / l_ref[...]).astype(o_ref.dtype)


def attention(info, q, qtok, qlo, parts):
    rows = q.shape[0]
    half = rows // 2
    counts = tuple(part.shape[0] // KB for part in parts)
    row_spec = lambda width: pl.BlockSpec((half, width), lambda i, info: (i, 0))
    return pl.pallas_call(
        functools.partial(attn_kernel, counts),
        out_shape=jax.ShapeDtypeStruct((rows, HD), jnp.bfloat16),
        grid_spec=pltpu.PrefetchScalarGridSpec(
            num_scalar_prefetch=1,
            grid=(2,),
            in_specs=[row_spec(HD), row_spec(1), row_spec(1)]
            + [pl.BlockSpec(part.shape, lambda i, info: (0, 0)) for part in parts],
            out_specs=row_spec(HD),
            scratch_shapes=[
                pltpu.VMEM((half, 1), jnp.float32),
                pltpu.VMEM((half, 1), jnp.float32),
                pltpu.VMEM((half, HD), jnp.float32),
            ],
        ),
    )(info, q, qtok, qlo, *parts)


def z_ring(part, n):
    fwd = [part]
    bwd = [part]
    steps = n // 2
    for step in range(1, steps + 1):
        if step < steps:
            fwd.append(lax.ppermute(fwd[-1], "z", [(i, (i + 1) % n) for i in range(n)]))
            bwd.append(lax.ppermute(bwd[-1], "z", [(i, (i - 1) % n) for i in range(n)]))
        else:
            cut = part.shape[0] // 2
            far_a = lax.ppermute(fwd[-1][:cut], "z", [(i, (i + 1) % n) for i in range(n)])
            far_b = lax.ppermute(bwd[-1][cut:], "z", [(i, (i - 1) % n) for i in range(n)])
    far = [(steps, far_a), (steps, far_b)]
    near = [(d, bwd[d]) for d in range(steps)]
    back = [(n - d, fwd[d]) for d in range(steps - 1, 0, -1)]
    return near + far + back


def per_device(hidden_in, w_query, w_key, w_value, query_gain, key_gain, prompt_lengths):
    tok_rows = hidden_in.shape[0]
    half_rows = tok_rows // 2
    local_width = w_query.shape[1]
    head_count = local_width // HD
    nz = lax.axis_size("z")
    nyh = lax.axis_size("yhi")
    ncl = lax.axis_size("ylo") * lax.axis_size("xlo")
    z_idx = lax.axis_index("z")
    cg = z_idx * nyh + lax.axis_index("yhi")
    cl = lax.axis_index("ylo") * lax.axis_size("xlo") + lax.axis_index("xlo")
    groups = nz * nyh
    ctx_count = groups * ncl
    own = cg * ncl + cl

    xh = lax.axis_index("xhi")
    core = lax.axis_index("core")
    swap = [(0, 1), (1, 0)]
    across = lax.ppermute(hidden_in, "xhi", swap)
    pair = jnp.where(xh == 0, jnp.concatenate([hidden_in, across], axis=1), jnp.concatenate([across, hidden_in], axis=1))
    other = lax.ppermute(pair, "core", swap)
    width = hidden_in.shape[1]
    mine_first = jnp.concatenate([pair[:, :width], other[:, :width], pair[:, width:], other[:, width:]], axis=1)
    theirs_first = jnp.concatenate([other[:, :width], pair[:, :width], other[:, width:], pair[:, width:]], axis=1)
    pieces = jnp.where(core == 0, mine_first, theirs_first)
    queries = jnp.dot(pieces, w_query, preferred_element_type=jnp.float32)
    keys_proj = jnp.dot(pieces, w_key, preferred_element_type=jnp.float32)
    values = jnp.dot(pieces, w_value, preferred_element_type=jnp.float32).astype(jnp.bfloat16)
    squares = jnp.stack([jnp.sum(queries * queries, axis=1), jnp.sum(keys_proj * keys_proj, axis=1)])
    squares = squares + lax.ppermute(squares, "xhi", swap)
    squares = squares + lax.ppermute(squares, "core", swap)
    query_sq = squares[0]
    key_sq = squares[1]
    full_width = local_width * lax.axis_size("xhi") * lax.axis_size("core")
    query_normed = queries * lax.rsqrt(query_sq[:, None] / full_width + 1e-06) * query_gain
    key_normed = keys_proj * lax.rsqrt(key_sq[:, None] / full_width + 1e-06) * key_gain
    local_rows = jnp.arange(tok_rows, dtype=jnp.int32)
    block_of = jnp.where(local_rows < half_rows, own, 2 * ctx_count - 1 - own)
    token_ids = block_of * half_rows + local_rows % half_rows
    position = token_ids - request_start(token_ids, prompt_lengths)
    query_rot = rotate(query_normed, position)
    key_rot = rotate(key_normed, position)

    packed = jnp.concatenate(
        [
            query_rot.reshape(tok_rows, head_count, HD),
            key_rot.reshape(tok_rows, head_count, HD),
            values.reshape(tok_rows, head_count, HD),
        ],
        axis=2,
    )
    got = lax.all_to_all(packed, CL, split_axis=1, concat_axis=0, tiled=True)
    got = got.reshape(ncl, tok_rows, 3 * HD)
    lower = got[:, :half_rows].reshape(ncl * half_rows, 3 * HD)
    upper = got[::-1, half_rows:].reshape(ncl * half_rows, 3 * HD)
    mine = jnp.concatenate([lower, upper], axis=0)
    q_head = mine[:, :HD]
    kv_mine = mine[:, HD:]

    yh = lax.axis_index("yhi")
    kv_other = lax.ppermute(kv_mine, "yhi", swap)
    kv_pair = jnp.where(yh == 0, jnp.concatenate([kv_mine, kv_other], axis=0), jnp.concatenate([kv_other, kv_mine], axis=0))
    arrived = z_ring(kv_pair, nz)

    span = ncl * half_rows
    total_tokens = 2 * ctx_count * half_rows
    r = jnp.arange(span, dtype=jnp.int32)
    q_tokens = jnp.concatenate([cg * span + r, total_tokens - (cg + 1) * span + r])
    q_lo = request_start(q_tokens, prompt_lengths)
    ids = []
    seen = {}
    for dist, part in arrived:
        first = seen.get(dist, 0)
        chunks = part.shape[0] // span
        seen[dist] = first + chunks // 2
        for j in range(chunks):
            group_j = (2 * ((z_idx + dist) % nz) + first + j // 2) % groups
            ids.append(group_j if j % 2 == 0 else 2 * groups - 1 - group_j)
    info = jnp.stack(ids + [q_lo[0] // KB, cg, q_lo[span] // KB, 2 * groups - 1 - cg]).astype(jnp.int32)
    parts = [part for _, part in arrived]
    out_head = attention(info, q_head, q_tokens[:, None], q_lo[:, None], parts)

    out_lower = out_head[:span].reshape(ncl, half_rows, HD)
    out_upper = out_head[span:].reshape(ncl, half_rows, HD)[::-1]
    out_send = jnp.stack([out_lower, out_upper], axis=1).reshape(ncl, tok_rows, HD)

    picked = jnp.concatenate(
        [
            lax.dynamic_slice_in_dim(
                part.reshape(part.shape[0] // (2 * span), 2, ncl, half_rows, 2 * HD), cg * ncl, ncl, axis=3
            )
            for part in parts
        ],
        axis=0,
    )
    doubled = jnp.concatenate([picked, picked], axis=0)
    natural = lax.dynamic_slice_in_dim(doubled, (groups - (z_idx * nyh) % groups) % groups, groups, axis=0)
    cache_lower = natural[:, 0].reshape(groups * ncl, ncl, 2 * HD)
    cache_upper = natural[::-1, 1].reshape(groups * ncl, ncl, 2 * HD)
    cache = jnp.concatenate([cache_lower, cache_upper], axis=0).transpose(1, 0, 2)
    send = jnp.concatenate([out_send, cache], axis=2)
    recv = lax.all_to_all(send, CL, split_axis=0, concat_axis=0, tiled=True)
    recv = recv.transpose(1, 0, 2)
    attn_out = recv[:, :, :HD].reshape(tok_rows, local_width)
    key_cache = recv[:, :, HD : 2 * HD].reshape(tok_rows, local_width)
    value_cache = recv[:, :, 2 * HD :].reshape(tok_rows, local_width)
    return attn_out, key_cache, value_cache


def solution(mesh):
    ctx_size = mesh.shape["ctx"]
    tp_size = mesh.shape["tp"]
    nz = 8
    split = Mesh(
        mesh.devices.reshape(nz, 2, 2, ctx_size // (nz * 4), tp_size // 2, 2),
        ("z", "yhi", "ylo", "xlo", "xhi", "core"),
    )
    rows = P(CTX, TP)
    placed = (rows, P(None, TP), P(None, TP), P(None, TP), P(TP), P(TP), P())
    return jax.shard_map(
        per_device,
        mesh=split,
        in_specs=placed,
        out_specs=(rows, rows, rows),
        check_vma=False,
    )
```

```python
import functools

import jax
import jax.numpy as jnp
from jax import lax
from jax.experimental import pallas as pl
from jax.experimental.pallas import tpu as pltpu
from jax.sharding import Mesh
from jax.sharding import PartitionSpec as P

HD = 128
KB = 256
CL = ("ylo", "xlo")
CTX = ("z", "yhi", "ylo", "xlo")
TP = ("xhi", "core")


def rotate(matrix, position):
    row_count, columns = matrix.shape
    head_count = columns // HD
    rot_half = HD // 2
    shaped = matrix.reshape(row_count, head_count, HD)
    inverse_freq = 500000.0 ** (-2.0 * jnp.arange(rot_half, dtype=jnp.float32) / HD)
    angles = position.astype(jnp.float32)[:, None] * inverse_freq[None, :]
    cosine = jnp.cos(angles)[:, None, :]
    sine_part = jnp.sin(angles)[:, None, :]
    first_part = shaped[..., :rot_half]
    second_part = shaped[..., rot_half:]
    turned = jnp.concatenate(
        [
            first_part * cosine - second_part * sine_part,
            second_part * cosine + first_part * sine_part,
        ],
        axis=-1,
    )
    return turned.reshape(row_count, columns).astype(jnp.bfloat16)


def request_start(token_ids, prompt_lengths):
    req_ends = jnp.cumsum(prompt_lengths)
    starts = req_ends - prompt_lengths
    request = jnp.sum((token_ids[:, None] >= req_ends[None, :]).astype(jnp.int32), axis=1)
    onehot = request[:, None] == jnp.arange(prompt_lengths.shape[0], dtype=jnp.int32)[None, :]
    return jnp.sum(jnp.where(onehot, starts[None, :], 0), axis=1)


def attn_kernel(info_ref, q_ref, kv_ref, qtok_ref, qlo_ref, o_ref):
    blk = pl.program_id(0)
    lo = info_ref[2 * blk]
    hi = info_ref[2 * blk + 1]
    z_own = info_ref[4]
    core_own = info_ref[5]
    nz = info_ref[6]
    groups = 2 * nz
    nblocks = 2 * groups
    q = q_ref[...]
    qtok = qtok_ref[...]
    qlo = qlo_ref[...]
    rows = q.shape[0]
    scale = HD ** (-0.5)

    def body(kb, carry):
        peak, total, acc = carry
        upper = kb >= groups
        group = jnp.where(upper, nblocks - 1 - kb, kb)
        dist = (group // 2 - z_own + nz) % nz
        other = (group % 2 != core_own).astype(jnp.int32)
        start = pl.multiple_of(((other * nz + dist) * 2 + upper.astype(jnp.int32)) * KB, KB)
        block = kv_ref[pl.ds(start, KB), :]
        keys = block[:, :HD]
        vals = block[:, HD:]
        scores = (
            lax.dot_general(q, keys, (((1,), (1,)), ((), ())), preferred_element_type=jnp.float32)
            * scale
        )
        ktok = kb * KB + lax.broadcasted_iota(jnp.int32, (1, KB), 1)
        visible = (ktok >= qlo) & (ktok <= qtok)
        masked = jnp.where(visible, scores, -1e30)
        new_peak = jnp.maximum(peak, jnp.max(masked, axis=1, keepdims=True))
        weights = jnp.where(visible, jnp.exp(masked - new_peak), 0.0)
        factor = jnp.exp(peak - new_peak)
        total = total * factor + jnp.sum(weights, axis=1, keepdims=True)
        acc = acc * factor + jnp.dot(
            weights.astype(jnp.bfloat16), vals, preferred_element_type=jnp.float32
        )
        return new_peak, total, acc

    start_state = (
        jnp.full((rows, 1), -1e30, jnp.float32),
        jnp.zeros((rows, 1), jnp.float32),
        jnp.zeros((rows, HD), jnp.float32),
    )
    _, total, acc = lax.fori_loop(lo, hi + 1, body, start_state)
    o_ref[...] = (acc / total).astype(o_ref.dtype)


def attention(info, q, kv, qtok, qlo):
    rows = q.shape[0]
    half = rows // 2
    return pl.pallas_call(
        attn_kernel,
        out_shape=jax.ShapeDtypeStruct((rows, HD), jnp.bfloat16),
        grid_spec=pltpu.PrefetchScalarGridSpec(
            num_scalar_prefetch=1,
            grid=(2,),
            in_specs=[
                pl.BlockSpec((half, HD), lambda i, info: (i, 0)),
                pl.BlockSpec(kv.shape, lambda i, info: (0, 0)),
                pl.BlockSpec((half, 1), lambda i, info: (i, 0)),
                pl.BlockSpec((half, 1), lambda i, info: (i, 0)),
            ],
            out_specs=pl.BlockSpec((half, HD), lambda i, info: (i, 0)),
        ),
    )(info, q, kv, qtok, qlo)


def z_ring(part, n):
    fwd = [part]
    bwd = [part]
    steps = n // 2
    for step in range(1, steps + 1):
        if step < steps:
            fwd.append(lax.ppermute(fwd[-1], "z", [(i, (i + 1) % n) for i in range(n)]))
            bwd.append(lax.ppermute(bwd[-1], "z", [(i, (i - 1) % n) for i in range(n)]))
        else:
            cut = part.shape[0] // 2
            far_a = lax.ppermute(fwd[-1][:cut], "z", [(i, (i + 1) % n) for i in range(n)])
            far_b = lax.ppermute(bwd[-1][cut:], "z", [(i, (i - 1) % n) for i in range(n)])
    ordered = bwd[: steps] + [far_a, far_b] + fwd[1:steps][::-1]
    return ordered


def per_device(hidden_in, w_query, w_key, w_value, query_gain, key_gain, prompt_lengths):
    tok_rows = hidden_in.shape[0]
    half_rows = tok_rows // 2
    local_width = w_query.shape[1]
    head_count = local_width // HD
    nz = lax.axis_size("z")
    nyh = lax.axis_size("yhi")
    ncl = lax.axis_size("ylo") * lax.axis_size("xlo")
    z_idx = lax.axis_index("z")
    cg = z_idx * nyh + lax.axis_index("yhi")
    cl = lax.axis_index("ylo") * lax.axis_size("xlo") + lax.axis_index("xlo")
    groups = nz * nyh
    ctx_count = groups * ncl
    own = cg * ncl + cl

    xh = lax.axis_index("xhi")
    core = lax.axis_index("core")
    swap = [(0, 1), (1, 0)]
    across = lax.ppermute(hidden_in, "xhi", swap)
    pair = jnp.where(xh == 0, jnp.concatenate([hidden_in, across], axis=1), jnp.concatenate([across, hidden_in], axis=1))
    other = lax.ppermute(pair, "core", swap)
    width = hidden_in.shape[1]
    mine_first = jnp.concatenate([pair[:, :width], other[:, :width], pair[:, width:], other[:, width:]], axis=1)
    theirs_first = jnp.concatenate([other[:, :width], pair[:, :width], other[:, width:], pair[:, width:]], axis=1)
    pieces = jnp.where(core == 0, mine_first, theirs_first)
    queries = jnp.dot(pieces, w_query, preferred_element_type=jnp.float32)
    keys_proj = jnp.dot(pieces, w_key, preferred_element_type=jnp.float32)
    values = jnp.dot(pieces, w_value, preferred_element_type=jnp.float32).astype(jnp.bfloat16)
    squares = jnp.stack([jnp.sum(queries * queries, axis=1), jnp.sum(keys_proj * keys_proj, axis=1)])
    squares = squares + lax.ppermute(squares, "xhi", swap)
    squares = squares + lax.ppermute(squares, "core", swap)
    query_sq = squares[0]
    key_sq = squares[1]
    full_width = local_width * lax.axis_size("xhi") * lax.axis_size("core")
    query_normed = queries * lax.rsqrt(query_sq[:, None] / full_width + 1e-06) * query_gain
    key_normed = keys_proj * lax.rsqrt(key_sq[:, None] / full_width + 1e-06) * key_gain
    local_rows = jnp.arange(tok_rows, dtype=jnp.int32)
    block_of = jnp.where(local_rows < half_rows, own, 2 * ctx_count - 1 - own)
    token_ids = block_of * half_rows + local_rows % half_rows
    position = token_ids - request_start(token_ids, prompt_lengths)
    query_rot = rotate(query_normed, position)
    key_rot = rotate(key_normed, position)

    packed = jnp.concatenate(
        [
            query_rot.reshape(tok_rows, head_count, HD),
            key_rot.reshape(tok_rows, head_count, HD),
            values.reshape(tok_rows, head_count, HD),
        ],
        axis=2,
    )
    got = lax.all_to_all(packed, CL, split_axis=1, concat_axis=0, tiled=True)
    got = got.reshape(ncl, tok_rows, 3 * HD)
    lower = got[:, :half_rows].reshape(ncl * half_rows, 3 * HD)
    upper = got[::-1, half_rows:].reshape(ncl * half_rows, 3 * HD)
    mine = jnp.concatenate([lower, upper], axis=0)
    q_head = mine[:, :HD]
    kv_mine = mine[:, HD:]

    yh = lax.axis_index("yhi")
    pair_axes = ("yhi", "core")
    crossed = lax.ppermute(mine, pair_axes, [(1, 2), (2, 1)])
    mine = jnp.where(yh == core, mine, crossed)
    q_head = mine[:, :HD]
    kv_mine = mine[:, HD:]
    ring_parts = z_ring(kv_mine, nz)
    sibling_parts = [lax.ppermute(p, "core", swap) for p in ring_parts]
    kv_all = jnp.concatenate(ring_parts + sibling_parts, axis=0)

    q_group = z_idx * nyh + core
    span = ncl * half_rows
    total_tokens = 2 * ctx_count * half_rows
    r = jnp.arange(span, dtype=jnp.int32)
    q_tokens = jnp.concatenate([q_group * span + r, total_tokens - (q_group + 1) * span + r])
    q_lo = request_start(q_tokens, prompt_lengths)
    info = jnp.stack(
        [
            q_lo[0] // KB,
            q_group,
            q_lo[span] // KB,
            2 * groups - 1 - q_group,
            z_idx,
            core,
            jnp.asarray(nz, jnp.int32),
        ]
    ).astype(jnp.int32)
    out_head = attention(info, q_head, kv_all, q_tokens[:, None], q_lo[:, None])

    out_lower = out_head[:span].reshape(ncl, half_rows, HD)
    out_upper = out_head[span:].reshape(ncl, half_rows, HD)[::-1]
    out_send = jnp.stack([out_lower, out_upper], axis=1).reshape(ncl, tok_rows, HD)

    picked = kv_all.reshape(2, nz, 2, ncl, half_rows, 2 * HD)
    picked = lax.dynamic_slice_in_dim(picked, q_group * ncl, ncl, axis=4)
    doubled = jnp.concatenate([picked, picked], axis=1)
    by_z = lax.dynamic_slice_in_dim(doubled, (nz - z_idx) % nz, nz, axis=1)
    by_half = jnp.where(core == 0, by_z, by_z[::-1])
    natural = by_half.transpose(1, 0, 2, 3, 4, 5).reshape(groups, 2, ncl, ncl, 2 * HD)
    cache_lower = natural[:, 0].reshape(groups * ncl, ncl, 2 * HD)
    cache_upper = natural[::-1, 1].reshape(groups * ncl, ncl, 2 * HD)
    cache = jnp.concatenate([cache_lower, cache_upper], axis=0).transpose(1, 0, 2)
    send = jnp.concatenate([out_send, cache], axis=2)
    crossed_back = lax.ppermute(send, pair_axes, [(1, 2), (2, 1)])
    send = jnp.where(yh == core, send, crossed_back)
    recv = lax.all_to_all(send, CL, split_axis=0, concat_axis=0, tiled=True)
    recv = recv.transpose(1, 0, 2)
    attn_out = recv[:, :, :HD].reshape(tok_rows, local_width)
    key_cache = recv[:, :, HD : 2 * HD].reshape(tok_rows, local_width)
    value_cache = recv[:, :, 2 * HD :].reshape(tok_rows, local_width)
    return attn_out, key_cache, value_cache


def solution(mesh):
    ctx_size = mesh.shape["ctx"]
    tp_size = mesh.shape["tp"]
    nz = 8
    split = Mesh(
        mesh.devices.reshape(nz, 2, 2, ctx_size // (nz * 4), tp_size // 2, 2),
        ("z", "yhi", "ylo", "xlo", "xhi", "core"),
    )
    rows = P(CTX, TP)
    placed = (rows, P(None, TP), P(None, TP), P(None, TP), P(TP), P(TP), P())
    return jax.shard_map(
        per_device,
        mesh=split,
        in_specs=placed,
        out_specs=(rows, rows, rows),
        check_vma=False,
    )
```

```python
import functools

import jax
import jax.numpy as jnp
from jax import lax
from jax.experimental import pallas as pl
from jax.experimental.pallas import tpu as pltpu
from jax.sharding import Mesh
from jax.sharding import PartitionSpec as P

HD = 128
KB = 256
CL = ("ylo", "xlo")
CTX = ("z", "yhi", "ylo", "xlo")
TP = ("xhi", "core")


def rotate(matrix, position):
    row_count, columns = matrix.shape
    head_count = columns // HD
    rot_half = HD // 2
    shaped = matrix.reshape(row_count, head_count, HD)
    inverse_freq = 500000.0 ** (-2.0 * jnp.arange(rot_half, dtype=jnp.float32) / HD)
    angles = position.astype(jnp.float32)[:, None] * inverse_freq[None, :]
    cosine = jnp.cos(angles)[:, None, :]
    sine_part = jnp.sin(angles)[:, None, :]
    first_part = shaped[..., :rot_half]
    second_part = shaped[..., rot_half:]
    turned = jnp.concatenate(
        [
            first_part * cosine - second_part * sine_part,
            second_part * cosine + first_part * sine_part,
        ],
        axis=-1,
    )
    return turned.reshape(row_count, columns).astype(jnp.bfloat16)


def request_start(token_ids, prompt_lengths):
    req_ends = jnp.cumsum(prompt_lengths)
    starts = req_ends - prompt_lengths
    request = jnp.sum((token_ids[:, None] >= req_ends[None, :]).astype(jnp.int32), axis=1)
    onehot = request[:, None] == jnp.arange(prompt_lengths.shape[0], dtype=jnp.int32)[None, :]
    return jnp.sum(jnp.where(onehot, starts[None, :], 0), axis=1)


def attn_kernel(info_ref, q_ref, kv_ref, qtok_ref, qlo_ref, m_ref, l_ref, acc_ref):
    blk = pl.program_id(0)
    lo = info_ref[2 * blk]
    hi = info_ref[2 * blk + 1]
    z_own = info_ref[8]
    core_own = info_ref[9]
    nz = info_ref[10]
    groups = 2 * nz
    nblocks = 2 * groups
    q = q_ref[...]
    qtok = qtok_ref[...]
    qlo = qlo_ref[...]
    rows = q.shape[0]
    scale = HD ** (-0.5)

    def update(kb, group, upper, carry):
        peak, total, acc = carry
        dist = (group // 2 - z_own + nz) % nz
        start = pl.multiple_of((dist * 2 + upper.astype(jnp.int32)) * KB, KB)
        block = kv_ref[pl.ds(start, KB), :]
        keys = block[:, :HD]
        vals = block[:, HD:]
        scores = (
            lax.dot_general(q, keys, (((1,), (1,)), ((), ())), preferred_element_type=jnp.float32)
            * scale
        )
        ktok = kb * KB + lax.broadcasted_iota(jnp.int32, (1, KB), 1)
        visible = (ktok >= qlo) & (ktok <= qtok)
        masked = jnp.where(visible, scores, -1e30)
        new_peak = jnp.maximum(peak, jnp.max(masked, axis=1, keepdims=True))
        weights = jnp.where(visible, jnp.exp(masked - new_peak), 0.0)
        factor = jnp.exp(peak - new_peak)
        total = total * factor + jnp.sum(weights, axis=1, keepdims=True)
        acc = acc * factor + jnp.dot(
            weights.astype(jnp.bfloat16), vals, preferred_element_type=jnp.float32
        )
        return new_peak, total, acc

    def body(kb, carry):
        upper = kb >= groups
        group = jnp.where(upper, nblocks - 1 - kb, kb)
        return lax.cond(
            group % 2 == core_own,
            lambda c: update(kb, group, upper, c),
            lambda c: c,
            carry,
        )

    start_state = (
        jnp.full((rows, 1), -1e30, jnp.float32),
        jnp.zeros((rows, 1), jnp.float32),
        jnp.zeros((rows, HD), jnp.float32),
    )
    peak, total, acc = lax.fori_loop(lo, hi + 1, body, start_state)
    m_ref[...] = peak
    l_ref[...] = total
    acc_ref[...] = acc


def attention(info, q, kv, qtok, qlo):
    rows = q.shape[0]
    block = rows // 4
    row_spec = lambda width: pl.BlockSpec((block, width), lambda i, info: (i, 0))
    return pl.pallas_call(
        attn_kernel,
        out_shape=(
            jax.ShapeDtypeStruct((rows, 1), jnp.float32),
            jax.ShapeDtypeStruct((rows, 1), jnp.float32),
            jax.ShapeDtypeStruct((rows, HD), jnp.float32),
        ),
        grid_spec=pltpu.PrefetchScalarGridSpec(
            num_scalar_prefetch=1,
            grid=(4,),
            in_specs=[
                row_spec(HD),
                pl.BlockSpec(kv.shape, lambda i, info: (0, 0)),
                row_spec(1),
                row_spec(1),
            ],
            out_specs=(row_spec(1), row_spec(1), row_spec(HD)),
        ),
    )(info, q, kv, qtok, qlo)


def z_ring(part, n):
    fwd = [part]
    bwd = [part]
    steps = n // 2
    for step in range(1, steps + 1):
        if step < steps:
            fwd.append(lax.ppermute(fwd[-1], "z", [(i, (i + 1) % n) for i in range(n)]))
            bwd.append(lax.ppermute(bwd[-1], "z", [(i, (i - 1) % n) for i in range(n)]))
        else:
            cut = part.shape[0] // 2
            far_a = lax.ppermute(fwd[-1][:cut], "z", [(i, (i + 1) % n) for i in range(n)])
            far_b = lax.ppermute(bwd[-1][cut:], "z", [(i, (i - 1) % n) for i in range(n)])
    ordered = bwd[: steps] + [far_a, far_b] + fwd[1:steps][::-1]
    return ordered


def per_device(hidden_in, w_query, w_key, w_value, query_gain, key_gain, prompt_lengths):
    tok_rows = hidden_in.shape[0]
    half_rows = tok_rows // 2
    local_width = w_query.shape[1]
    head_count = local_width // HD
    nz = lax.axis_size("z")
    nyh = lax.axis_size("yhi")
    ncl = lax.axis_size("ylo") * lax.axis_size("xlo")
    z_idx = lax.axis_index("z")
    cg = z_idx * nyh + lax.axis_index("yhi")
    cl = lax.axis_index("ylo") * lax.axis_size("xlo") + lax.axis_index("xlo")
    groups = nz * nyh
    ctx_count = groups * ncl
    own = cg * ncl + cl

    xh = lax.axis_index("xhi")
    core = lax.axis_index("core")
    swap = [(0, 1), (1, 0)]
    across = lax.ppermute(hidden_in, "xhi", swap)
    pair = jnp.where(xh == 0, jnp.concatenate([hidden_in, across], axis=1), jnp.concatenate([across, hidden_in], axis=1))
    other = lax.ppermute(pair, "core", swap)
    width = hidden_in.shape[1]
    mine_first = jnp.concatenate([pair[:, :width], other[:, :width], pair[:, width:], other[:, width:]], axis=1)
    theirs_first = jnp.concatenate([other[:, :width], pair[:, :width], other[:, width:], pair[:, width:]], axis=1)
    pieces = jnp.where(core == 0, mine_first, theirs_first)
    queries = jnp.dot(pieces, w_query, preferred_element_type=jnp.float32)
    keys_proj = jnp.dot(pieces, w_key, preferred_element_type=jnp.float32)
    values = jnp.dot(pieces, w_value, preferred_element_type=jnp.float32).astype(jnp.bfloat16)
    squares = jnp.stack([jnp.sum(queries * queries, axis=1), jnp.sum(keys_proj * keys_proj, axis=1)])
    squares = squares + lax.ppermute(squares, "xhi", swap)
    squares = squares + lax.ppermute(squares, "core", swap)
    query_sq = squares[0]
    key_sq = squares[1]
    full_width = local_width * lax.axis_size("xhi") * lax.axis_size("core")
    query_normed = queries * lax.rsqrt(query_sq[:, None] / full_width + 1e-06) * query_gain
    key_normed = keys_proj * lax.rsqrt(key_sq[:, None] / full_width + 1e-06) * key_gain
    local_rows = jnp.arange(tok_rows, dtype=jnp.int32)
    block_of = jnp.where(local_rows < half_rows, own, 2 * ctx_count - 1 - own)
    token_ids = block_of * half_rows + local_rows % half_rows
    position = token_ids - request_start(token_ids, prompt_lengths)
    query_rot = rotate(query_normed, position)
    key_rot = rotate(key_normed, position)

    packed = jnp.concatenate(
        [
            query_rot.reshape(tok_rows, head_count, HD),
            key_rot.reshape(tok_rows, head_count, HD),
            values.reshape(tok_rows, head_count, HD),
        ],
        axis=2,
    )
    got = lax.all_to_all(packed, CL, split_axis=1, concat_axis=0, tiled=True)
    got = got.reshape(ncl, tok_rows, 3 * HD)
    lower = got[:, :half_rows].reshape(ncl * half_rows, 3 * HD)
    upper = got[::-1, half_rows:].reshape(ncl * half_rows, 3 * HD)
    mine = jnp.concatenate([lower, upper], axis=0)
    q_head = mine[:, :HD]
    kv_mine = mine[:, HD:]

    yh = lax.axis_index("yhi")
    pair_axes = ("yhi", "core")
    crossed = lax.ppermute(mine, pair_axes, [(1, 2), (2, 1)])
    mine = jnp.where(yh == core, mine, crossed)
    q_head = mine[:, :HD]
    kv_mine = mine[:, HD:]
    q_sibling = lax.ppermute(q_head, "core", swap)
    ring_parts = z_ring(kv_mine, nz)
    kv_half = jnp.concatenate(ring_parts, axis=0)

    q_group = z_idx * nyh + core
    sib_group = z_idx * nyh + (1 - core)
    span = ncl * half_rows
    total_tokens = 2 * ctx_count * half_rows
    r = jnp.arange(span, dtype=jnp.int32)
    q_tokens = jnp.concatenate(
        [
            q_group * span + r,
            total_tokens - (q_group + 1) * span + r,
            sib_group * span + r,
            total_tokens - (sib_group + 1) * span + r,
        ]
    )
    q_lo = request_start(q_tokens, prompt_lengths)
    info = jnp.stack(
        [
            q_lo[0] // KB,
            q_group,
            q_lo[span] // KB,
            2 * groups - 1 - q_group,
            q_lo[2 * span] // KB,
            sib_group,
            q_lo[3 * span] // KB,
            2 * groups - 1 - sib_group,
            z_idx,
            core,
            jnp.asarray(nz, jnp.int32),
        ]
    ).astype(jnp.int32)
    q_both = jnp.concatenate([q_head, q_sibling], axis=0)
    peak, total, acc = attention(info, q_both, kv_half, q_tokens[:, None], q_lo[:, None])
    rows_q = 2 * span
    partial = jnp.concatenate([acc, peak, total], axis=1)
    theirs = lax.ppermute(partial[rows_q:], "core", swap)
    peak_b = theirs[:, HD : HD + 1]
    peak_a = peak[:rows_q]
    joint = jnp.maximum(peak_a, peak_b)
    scale_a = jnp.exp(peak_a - joint)
    scale_b = jnp.exp(peak_b - joint)
    joint_total = total[:rows_q] * scale_a + theirs[:, HD + 1 :] * scale_b
    joint_acc = acc[:rows_q] * scale_a + theirs[:, :HD] * scale_b
    out_head = (joint_acc / joint_total).astype(jnp.bfloat16)

    out_lower = out_head[:span].reshape(ncl, half_rows, HD)
    out_upper = out_head[span:].reshape(ncl, half_rows, HD)[::-1]
    out_send = jnp.stack([out_lower, out_upper], axis=1).reshape(ncl, tok_rows, HD)

    halves = kv_half.reshape(nz, 2, ncl, half_rows, 2 * HD)
    own_pick = lax.dynamic_slice_in_dim(halves, q_group * ncl, ncl, axis=3)
    sib_pick = lax.dynamic_slice_in_dim(halves, sib_group * ncl, ncl, axis=3)
    got_pick = lax.ppermute(sib_pick, "core", swap)
    picked = jnp.where(core == 0, jnp.stack([own_pick, got_pick]), jnp.stack([got_pick, own_pick]))
    doubled = jnp.concatenate([picked, picked], axis=1)
    by_z = lax.dynamic_slice_in_dim(doubled, (nz - z_idx) % nz, nz, axis=1)
    natural = by_z.transpose(1, 0, 2, 3, 4, 5).reshape(groups, 2, ncl, ncl, 2 * HD)
    cache_lower = natural[:, 0].reshape(groups * ncl, ncl, 2 * HD)
    cache_upper = natural[::-1, 1].reshape(groups * ncl, ncl, 2 * HD)
    cache = jnp.concatenate([cache_lower, cache_upper], axis=0).transpose(1, 0, 2)
    send = jnp.concatenate([out_send, cache], axis=2)
    crossed_back = lax.ppermute(send, pair_axes, [(1, 2), (2, 1)])
    send = jnp.where(yh == core, send, crossed_back)
    recv = lax.all_to_all(send, CL, split_axis=0, concat_axis=0, tiled=True)
    recv = recv.transpose(1, 0, 2)
    attn_out = recv[:, :, :HD].reshape(tok_rows, local_width)
    key_cache = recv[:, :, HD : 2 * HD].reshape(tok_rows, local_width)
    value_cache = recv[:, :, 2 * HD :].reshape(tok_rows, local_width)
    return attn_out, key_cache, value_cache


def solution(mesh):
    ctx_size = mesh.shape["ctx"]
    tp_size = mesh.shape["tp"]
    nz = 8
    split = Mesh(
        mesh.devices.reshape(nz, 2, 2, ctx_size // (nz * 4), tp_size // 2, 2),
        ("z", "yhi", "ylo", "xlo", "xhi", "core"),
    )
    rows = P(CTX, TP)
    placed = (rows, P(None, TP), P(None, TP), P(None, TP), P(TP), P(TP), P())
    return jax.shard_map(
        per_device,
        mesh=split,
        in_specs=placed,
        out_specs=(rows, rows, rows),
        check_vma=False,
    )
```

```python
import functools

import jax
import jax.numpy as jnp
from jax import lax
from jax.experimental import pallas as pl
from jax.experimental.pallas import tpu as pltpu
from jax.sharding import Mesh
from jax.sharding import PartitionSpec as P

HD = 128
KB = 256
CL = ("ylo", "xlo")
CTX = ("z", "yhi", "ylo", "xlo")
TP = ("xhi", "core")


def rotate(matrix, position):
    row_count, columns = matrix.shape
    head_count = columns // HD
    rot_half = HD // 2
    shaped = matrix.reshape(row_count, head_count, HD)
    inverse_freq = 500000.0 ** (-2.0 * jnp.arange(rot_half, dtype=jnp.float32) / HD)
    angles = position.astype(jnp.float32)[:, None] * inverse_freq[None, :]
    cosine = jnp.cos(angles)[:, None, :]
    sine_part = jnp.sin(angles)[:, None, :]
    first_part = shaped[..., :rot_half]
    second_part = shaped[..., rot_half:]
    turned = jnp.concatenate(
        [
            first_part * cosine - second_part * sine_part,
            second_part * cosine + first_part * sine_part,
        ],
        axis=-1,
    )
    return turned.reshape(row_count, columns).astype(jnp.bfloat16)


def request_start(token_ids, prompt_lengths):
    req_ends = jnp.cumsum(prompt_lengths)
    starts = req_ends - prompt_lengths
    request = jnp.sum((token_ids[:, None] >= req_ends[None, :]).astype(jnp.int32), axis=1)
    onehot = request[:, None] == jnp.arange(prompt_lengths.shape[0], dtype=jnp.int32)[None, :]
    return jnp.sum(jnp.where(onehot, starts[None, :], 0), axis=1)


def attn_kernel(info_ref, q_ref, kv_ref, qtok_ref, qlo_ref, m_ref, l_ref, acc_ref):
    blk = pl.program_id(0)
    lo = info_ref[2 * blk]
    hi = info_ref[2 * blk + 1]
    z_own = info_ref[8]
    core_own = info_ref[9]
    nz = info_ref[10]
    groups = 2 * nz
    nblocks = 2 * groups
    q = q_ref[...]
    qtok = qtok_ref[...]
    qlo = qlo_ref[...]
    rows = q.shape[0]
    scale = HD ** (-0.5)

    def update(kb, group, upper, carry):
        peak, total, acc = carry
        dist = (group // 2 - z_own + nz) % nz
        start = pl.multiple_of((dist * 2 + upper.astype(jnp.int32)) * KB, KB)
        block = kv_ref[pl.ds(start, KB), :]
        keys = block[:, :HD]
        vals = block[:, HD:]
        scores = (
            lax.dot_general(q, keys, (((1,), (1,)), ((), ())), preferred_element_type=jnp.float32)
            * scale
        )
        ktok = kb * KB + lax.broadcasted_iota(jnp.int32, (1, KB), 1)
        visible = (ktok >= qlo) & (ktok <= qtok)
        masked = jnp.where(visible, scores, -1e30)
        new_peak = jnp.maximum(peak, jnp.max(masked, axis=1, keepdims=True))
        weights = jnp.where(visible, jnp.exp(masked - new_peak), 0.0)
        factor = jnp.exp(peak - new_peak)
        total = total * factor + jnp.sum(weights, axis=1, keepdims=True)
        acc = acc * factor + jnp.dot(
            weights.astype(jnp.bfloat16), vals, preferred_element_type=jnp.float32
        )
        return new_peak, total, acc

    def body(kb, carry):
        upper = kb >= groups
        group = jnp.where(upper, nblocks - 1 - kb, kb)
        return lax.cond(
            group % 2 == core_own,
            lambda c: update(kb, group, upper, c),
            lambda c: c,
            carry,
        )

    start_state = (
        jnp.full((rows, 1), -1e30, jnp.float32),
        jnp.zeros((rows, 1), jnp.float32),
        jnp.zeros((rows, HD), jnp.float32),
    )
    peak, total, acc = lax.fori_loop(lo, hi + 1, body, start_state)
    m_ref[...] = peak
    l_ref[...] = total
    acc_ref[...] = acc


def attention(info, q, kv, qtok, qlo):
    rows = q.shape[0]
    block = rows // 4
    row_spec = lambda width: pl.BlockSpec((block, width), lambda i, info: (i, 0))
    return pl.pallas_call(
        attn_kernel,
        out_shape=(
            jax.ShapeDtypeStruct((rows, 1), jnp.float32),
            jax.ShapeDtypeStruct((rows, 1), jnp.float32),
            jax.ShapeDtypeStruct((rows, HD), jnp.float32),
        ),
        grid_spec=pltpu.PrefetchScalarGridSpec(
            num_scalar_prefetch=1,
            grid=(4,),
            in_specs=[
                row_spec(HD),
                pl.BlockSpec(kv.shape, lambda i, info: (0, 0)),
                row_spec(1),
                row_spec(1),
            ],
            out_specs=(row_spec(1), row_spec(1), row_spec(HD)),
        ),
    )(info, q, kv, qtok, qlo)


def z_ring(part, n):
    fwd = [part]
    bwd = [part]
    steps = n // 2
    for step in range(1, steps + 1):
        if step < steps:
            fwd.append(lax.ppermute(fwd[-1], "z", [(i, (i + 1) % n) for i in range(n)]))
            bwd.append(lax.ppermute(bwd[-1], "z", [(i, (i - 1) % n) for i in range(n)]))
        else:
            cut = part.shape[0] // 2
            far_a = lax.ppermute(fwd[-1][:cut], "z", [(i, (i + 1) % n) for i in range(n)])
            far_b = lax.ppermute(bwd[-1][cut:], "z", [(i, (i - 1) % n) for i in range(n)])
    ordered = bwd[: steps] + [far_a, far_b] + fwd[1:steps][::-1]
    return ordered


def per_device(hidden_in, w_query, w_key, w_value, query_gain, key_gain, prompt_lengths):
    tok_rows = hidden_in.shape[0]
    half_rows = tok_rows // 2
    local_width = w_query.shape[1]
    head_count = local_width // HD
    nz = lax.axis_size("z")
    nyh = lax.axis_size("yhi")
    ncl = lax.axis_size("ylo") * lax.axis_size("xlo")
    z_idx = lax.axis_index("z")
    cg = z_idx * nyh + lax.axis_index("yhi")
    cl = lax.axis_index("ylo") * lax.axis_size("xlo") + lax.axis_index("xlo")
    groups = nz * nyh
    ctx_count = groups * ncl
    own = cg * ncl + cl

    xh = lax.axis_index("xhi")
    core = lax.axis_index("core")
    swap = [(0, 1), (1, 0)]
    across = lax.ppermute(hidden_in, "xhi", swap)
    pair = jnp.where(xh == 0, jnp.concatenate([hidden_in, across], axis=1), jnp.concatenate([across, hidden_in], axis=1))
    other = lax.ppermute(pair, "core", swap)
    width = hidden_in.shape[1]
    mine_first = jnp.concatenate([pair[:, :width], other[:, :width], pair[:, width:], other[:, width:]], axis=1)
    theirs_first = jnp.concatenate([other[:, :width], pair[:, :width], other[:, width:], pair[:, width:]], axis=1)
    pieces = jnp.where(core == 0, mine_first, theirs_first)
    queries = jnp.dot(pieces, w_query, preferred_element_type=jnp.float32)
    keys_proj = jnp.dot(pieces, w_key, preferred_element_type=jnp.float32)
    values = jnp.dot(pieces, w_value, preferred_element_type=jnp.float32).astype(jnp.bfloat16)
    squares = jnp.stack([jnp.sum(queries * queries, axis=1), jnp.sum(keys_proj * keys_proj, axis=1)])
    squares = squares + lax.ppermute(squares, "xhi", swap)
    squares = squares + lax.ppermute(squares, "core", swap)
    query_sq = squares[0]
    key_sq = squares[1]
    full_width = local_width * lax.axis_size("xhi") * lax.axis_size("core")
    query_normed = queries * lax.rsqrt(query_sq[:, None] / full_width + 1e-06) * query_gain
    key_normed = keys_proj * lax.rsqrt(key_sq[:, None] / full_width + 1e-06) * key_gain
    local_rows = jnp.arange(tok_rows, dtype=jnp.int32)
    block_of = jnp.where(local_rows < half_rows, own, 2 * ctx_count - 1 - own)
    token_ids = block_of * half_rows + local_rows % half_rows
    position = token_ids - request_start(token_ids, prompt_lengths)
    query_rot = rotate(query_normed, position)
    key_rot = rotate(key_normed, position)

    packed = jnp.concatenate(
        [
            query_rot.reshape(tok_rows, head_count, HD),
            key_rot.reshape(tok_rows, head_count, HD),
            values.reshape(tok_rows, head_count, HD),
        ],
        axis=2,
    )
    got = lax.all_to_all(packed, CL, split_axis=1, concat_axis=0, tiled=True)
    got = got.reshape(ncl, tok_rows, 3 * HD)
    lower = got[:, :half_rows].reshape(ncl * half_rows, 3 * HD)
    upper = got[::-1, half_rows:].reshape(ncl * half_rows, 3 * HD)
    mine = jnp.concatenate([lower, upper], axis=0)
    q_head = mine[:, :HD]
    kv_mine = mine[:, HD:]

    yh = lax.axis_index("yhi")
    pair_axes = ("yhi", "core")
    crossed = lax.ppermute(mine, pair_axes, [(1, 2), (2, 1)])
    mine = jnp.where(yh == core, mine, crossed)
    q_head = mine[:, :HD]
    kv_mine = mine[:, HD:]
    q_sibling = lax.ppermute(q_head, "core", swap)
    q_sibling, kv_mine = lax.optimization_barrier((q_sibling, kv_mine))
    ring_parts = z_ring(kv_mine, nz)
    kv_half = jnp.concatenate(ring_parts, axis=0)

    q_group = z_idx * nyh + core
    sib_group = z_idx * nyh + (1 - core)
    span = ncl * half_rows
    total_tokens = 2 * ctx_count * half_rows
    r = jnp.arange(span, dtype=jnp.int32)
    q_tokens = jnp.concatenate(
        [
            q_group * span + r,
            total_tokens - (q_group + 1) * span + r,
            sib_group * span + r,
            total_tokens - (sib_group + 1) * span + r,
        ]
    )
    q_lo = request_start(q_tokens, prompt_lengths)
    info = jnp.stack(
        [
            q_lo[0] // KB,
            q_group,
            q_lo[span] // KB,
            2 * groups - 1 - q_group,
            q_lo[2 * span] // KB,
            sib_group,
            q_lo[3 * span] // KB,
            2 * groups - 1 - sib_group,
            z_idx,
            core,
            jnp.asarray(nz, jnp.int32),
        ]
    ).astype(jnp.int32)
    q_both = jnp.concatenate([q_head, q_sibling], axis=0)
    peak, total, acc = attention(info, q_both, kv_half, q_tokens[:, None], q_lo[:, None])
    rows_q = 2 * span
    partial = jnp.concatenate([acc, peak, total], axis=1)
    theirs = lax.ppermute(partial[rows_q:], "core", swap)
    peak_b = theirs[:, HD : HD + 1]
    peak_a = peak[:rows_q]
    joint = jnp.maximum(peak_a, peak_b)
    scale_a = jnp.exp(peak_a - joint)
    scale_b = jnp.exp(peak_b - joint)
    joint_total = total[:rows_q] * scale_a + theirs[:, HD + 1 :] * scale_b
    joint_acc = acc[:rows_q] * scale_a + theirs[:, :HD] * scale_b
    out_head = (joint_acc / joint_total).astype(jnp.bfloat16)

    out_lower = out_head[:span].reshape(ncl, half_rows, HD)
    out_upper = out_head[span:].reshape(ncl, half_rows, HD)[::-1]
    out_send = jnp.stack([out_lower, out_upper], axis=1).reshape(ncl, tok_rows, HD)

    halves = kv_half.reshape(nz, 2, ncl, half_rows, 2 * HD)
    own_pick = lax.dynamic_slice_in_dim(halves, q_group * ncl, ncl, axis=3)
    sib_pick = lax.dynamic_slice_in_dim(halves, sib_group * ncl, ncl, axis=3)
    got_pick = lax.ppermute(sib_pick, "core", swap)
    picked = jnp.where(core == 0, jnp.stack([own_pick, got_pick]), jnp.stack([got_pick, own_pick]))
    doubled = jnp.concatenate([picked, picked], axis=1)
    by_z = lax.dynamic_slice_in_dim(doubled, (nz - z_idx) % nz, nz, axis=1)
    natural = by_z.transpose(1, 0, 2, 3, 4, 5).reshape(groups, 2, ncl, ncl, 2 * HD)
    cache_lower = natural[:, 0].reshape(groups * ncl, ncl, 2 * HD)
    cache_upper = natural[::-1, 1].reshape(groups * ncl, ncl, 2 * HD)
    cache = jnp.concatenate([cache_lower, cache_upper], axis=0).transpose(1, 0, 2)
    send = jnp.concatenate([out_send, cache], axis=2)
    crossed_back = lax.ppermute(send, pair_axes, [(1, 2), (2, 1)])
    send = jnp.where(yh == core, send, crossed_back)
    recv = lax.all_to_all(send, CL, split_axis=0, concat_axis=0, tiled=True)
    recv = recv.transpose(1, 0, 2)
    attn_out = recv[:, :, :HD].reshape(tok_rows, local_width)
    key_cache = recv[:, :, HD : 2 * HD].reshape(tok_rows, local_width)
    value_cache = recv[:, :, 2 * HD :].reshape(tok_rows, local_width)
    return attn_out, key_cache, value_cache


def solution(mesh):
    ctx_size = mesh.shape["ctx"]
    tp_size = mesh.shape["tp"]
    nz = 8
    split = Mesh(
        mesh.devices.reshape(nz, 2, 2, ctx_size // (nz * 4), tp_size // 2, 2),
        ("z", "yhi", "ylo", "xlo", "xhi", "core"),
    )
    rows = P(CTX, TP)
    placed = (rows, P(None, TP), P(None, TP), P(None, TP), P(TP), P(TP), P())
    return jax.shard_map(
        per_device,
        mesh=split,
        in_specs=placed,
        out_specs=(rows, rows, rows),
        check_vma=False,
    )
```

```python
import functools

import jax
import jax.numpy as jnp
from jax import lax
from jax.experimental import pallas as pl
from jax.experimental.pallas import tpu as pltpu
from jax.sharding import Mesh
from jax.sharding import PartitionSpec as P

HD = 128
KB = 256
CL = ("ylo", "xlo")
CTX = ("z", "yhi", "ylo", "xlo")
TP = ("xhi", "core")


def rotate(matrix, position):
    row_count, columns = matrix.shape
    head_count = columns // HD
    rot_half = HD // 2
    shaped = matrix.reshape(row_count, head_count, HD)
    inverse_freq = 500000.0 ** (-2.0 * jnp.arange(rot_half, dtype=jnp.float32) / HD)
    angles = position.astype(jnp.float32)[:, None] * inverse_freq[None, :]
    cosine = jnp.cos(angles)[:, None, :]
    sine_part = jnp.sin(angles)[:, None, :]
    first_part = shaped[..., :rot_half]
    second_part = shaped[..., rot_half:]
    turned = jnp.concatenate(
        [
            first_part * cosine - second_part * sine_part,
            second_part * cosine + first_part * sine_part,
        ],
        axis=-1,
    )
    return turned.reshape(row_count, columns).astype(jnp.bfloat16)


def request_start(token_ids, prompt_lengths):
    req_ends = jnp.cumsum(prompt_lengths)
    starts = req_ends - prompt_lengths
    request = jnp.sum((token_ids[:, None] >= req_ends[None, :]).astype(jnp.int32), axis=1)
    onehot = request[:, None] == jnp.arange(prompt_lengths.shape[0], dtype=jnp.int32)[None, :]
    return jnp.sum(jnp.where(onehot, starts[None, :], 0), axis=1)


def attn_kernel(info_ref, q_ref, kv_ref, qtok_ref, qlo_ref, o_ref):
    blk = pl.program_id(0)
    lo = info_ref[2 * blk]
    hi = info_ref[2 * blk + 1]
    shift = info_ref[4]
    groups = info_ref[5]
    nblocks = 2 * groups
    q = q_ref[...]
    qtok = qtok_ref[...]
    qlo = qlo_ref[...]
    rows = q.shape[0]
    scale = HD ** (-0.5)

    def body(kb, carry):
        peak, total, acc = carry
        upper = kb >= groups
        group = jnp.where(upper, nblocks - 1 - kb, kb)
        slot = (group - shift + groups) % groups
        start = pl.multiple_of((slot * 2 + upper.astype(jnp.int32)) * KB, KB)
        block = kv_ref[pl.ds(start, KB), :]
        keys = block[:, :HD]
        vals = block[:, HD:]
        scores = (
            lax.dot_general(q, keys, (((1,), (1,)), ((), ())), preferred_element_type=jnp.float32)
            * scale
        )
        ktok = kb * KB + lax.broadcasted_iota(jnp.int32, (1, KB), 1)
        visible = (ktok >= qlo) & (ktok <= qtok)
        masked = jnp.where(visible, scores, -1e30)
        new_peak = jnp.maximum(peak, jnp.max(masked, axis=1, keepdims=True))
        weights = jnp.where(visible, jnp.exp(masked - new_peak), 0.0)
        factor = jnp.exp(peak - new_peak)
        total = total * factor + jnp.sum(weights, axis=1, keepdims=True)
        acc = acc * factor + jnp.dot(
            weights.astype(jnp.bfloat16), vals, preferred_element_type=jnp.float32
        )
        return new_peak, total, acc

    start_state = (
        jnp.full((rows, 1), -1e30, jnp.float32),
        jnp.zeros((rows, 1), jnp.float32),
        jnp.zeros((rows, HD), jnp.float32),
    )
    _, total, acc = lax.fori_loop(lo, hi + 1, body, start_state)
    o_ref[...] = (acc / total).astype(o_ref.dtype)


def attention(info, q, kv, qtok, qlo):
    rows = q.shape[0]
    half = rows // 2
    return pl.pallas_call(
        attn_kernel,
        out_shape=jax.ShapeDtypeStruct((rows, HD), jnp.bfloat16),
        grid_spec=pltpu.PrefetchScalarGridSpec(
            num_scalar_prefetch=1,
            grid=(2,),
            in_specs=[
                pl.BlockSpec((half, HD), lambda i, info: (i, 0)),
                pl.BlockSpec(kv.shape, lambda i, info: (0, 0)),
                pl.BlockSpec((half, 1), lambda i, info: (i, 0)),
                pl.BlockSpec((half, 1), lambda i, info: (i, 0)),
            ],
            out_specs=pl.BlockSpec((half, HD), lambda i, info: (i, 0)),
        ),
    )(info, q, kv, qtok, qlo)


def z_ring(part, n):
    fwd = [part]
    bwd = [part]
    steps = n // 2
    for step in range(1, steps + 1):
        if step < steps:
            fwd.append(lax.ppermute(fwd[-1], "z", [(i, (i + 1) % n) for i in range(n)]))
            bwd.append(lax.ppermute(bwd[-1], "z", [(i, (i - 1) % n) for i in range(n)]))
        else:
            cut = part.shape[0] // 2
            far_a = lax.ppermute(fwd[-1][:cut], "z", [(i, (i + 1) % n) for i in range(n)])
            far_b = lax.ppermute(bwd[-1][cut:], "z", [(i, (i - 1) % n) for i in range(n)])
    ordered = bwd[: steps] + [far_a, far_b] + fwd[1:steps][::-1]
    return jnp.concatenate(ordered, axis=0)


def per_device(hidden_in, w_query, w_key, w_value, query_gain, key_gain, prompt_lengths):
    tok_rows = hidden_in.shape[0]
    half_rows = tok_rows // 2
    local_width = w_query.shape[1]
    head_count = local_width // HD
    nz = lax.axis_size("z")
    nyh = lax.axis_size("yhi")
    ncl = lax.axis_size("ylo") * lax.axis_size("xlo")
    z_idx = lax.axis_index("z")
    cg = z_idx * nyh + lax.axis_index("yhi")
    cl = lax.axis_index("ylo") * lax.axis_size("xlo") + lax.axis_index("xlo")
    groups = nz * nyh
    ctx_count = groups * ncl
    own = cg * ncl + cl

    xh = lax.axis_index("xhi")
    core = lax.axis_index("core")
    swap = [(0, 1), (1, 0)]
    across = lax.ppermute(hidden_in, "xhi", swap)
    pair = jnp.where(xh == 0, jnp.concatenate([hidden_in, across], axis=1), jnp.concatenate([across, hidden_in], axis=1))
    other = lax.ppermute(pair, "core", swap)
    width = hidden_in.shape[1]
    mine_first = jnp.concatenate([pair[:, :width], other[:, :width], pair[:, width:], other[:, width:]], axis=1)
    theirs_first = jnp.concatenate([other[:, :width], pair[:, :width], other[:, width:], pair[:, width:]], axis=1)
    pieces = jnp.where(core == 0, mine_first, theirs_first)
    queries = jnp.dot(pieces, w_query, preferred_element_type=jnp.float32)
    keys_proj = jnp.dot(pieces, w_key, preferred_element_type=jnp.float32)
    values = jnp.dot(pieces, w_value, preferred_element_type=jnp.float32).astype(jnp.bfloat16)
    squares = jnp.stack([jnp.sum(queries * queries, axis=1), jnp.sum(keys_proj * keys_proj, axis=1)])
    squares = squares + lax.ppermute(squares, "xhi", swap)
    squares = squares + lax.ppermute(squares, "core", swap)
    query_sq = squares[0]
    key_sq = squares[1]
    full_width = local_width * lax.axis_size("xhi") * lax.axis_size("core")
    query_normed = queries * lax.rsqrt(query_sq[:, None] / full_width + 1e-06) * query_gain
    key_normed = keys_proj * lax.rsqrt(key_sq[:, None] / full_width + 1e-06) * key_gain
    local_rows = jnp.arange(tok_rows, dtype=jnp.int32)
    block_of = jnp.where(local_rows < half_rows, own, 2 * ctx_count - 1 - own)
    token_ids = block_of * half_rows + local_rows % half_rows
    position = token_ids - request_start(token_ids, prompt_lengths)
    query_rot = rotate(query_normed, position)
    key_rot = rotate(key_normed, position)

    packed = jnp.concatenate(
        [
            query_rot.reshape(tok_rows, head_count, HD),
            key_rot.reshape(tok_rows, head_count, HD),
            values.reshape(tok_rows, head_count, HD),
        ],
        axis=2,
    )
    got = lax.all_to_all(packed, CL, split_axis=1, concat_axis=0, tiled=True)
    got = got.reshape(ncl, tok_rows, 3 * HD)
    lower = got[:, :half_rows].reshape(ncl * half_rows, 3 * HD)
    upper = got[::-1, half_rows:].reshape(ncl * half_rows, 3 * HD)
    mine = jnp.concatenate([lower, upper], axis=0)
    q_head = mine[:, :HD]
    kv_mine = mine[:, HD:]

    yh = lax.axis_index("yhi")
    kv_other = lax.ppermute(kv_mine, "yhi", swap)
    kv_pair = jnp.where(yh == 0, jnp.concatenate([kv_mine, kv_other], axis=0), jnp.concatenate([kv_other, kv_mine], axis=0))
    kv_all = z_ring(kv_pair, nz)

    span = ncl * half_rows
    total_tokens = 2 * ctx_count * half_rows
    r = jnp.arange(span, dtype=jnp.int32)
    q_tokens = jnp.concatenate([cg * span + r, total_tokens - (cg + 1) * span + r])
    q_lo = request_start(q_tokens, prompt_lengths)
    info = jnp.stack(
        [
            q_lo[0] // KB,
            cg,
            q_lo[span] // KB,
            2 * groups - 1 - cg,
            (z_idx * nyh) % groups,
            jnp.asarray(groups, jnp.int32),
        ]
    ).astype(jnp.int32)
    out_head = attention(info, q_head, kv_all, q_tokens[:, None], q_lo[:, None])

    out_lower = out_head[:span].reshape(ncl, half_rows, HD)
    out_upper = out_head[span:].reshape(ncl, half_rows, HD)[::-1]
    out_send = jnp.stack([out_lower, out_upper], axis=1).reshape(ncl, tok_rows, HD)

    picked = kv_all.reshape(groups, 2, ncl, half_rows, 2 * HD)
    picked = lax.dynamic_slice_in_dim(picked, cg * ncl, ncl, axis=3)
    doubled = jnp.concatenate([picked, picked], axis=0)
    natural = lax.dynamic_slice_in_dim(doubled, (groups - (z_idx * nyh) % groups) % groups, groups, axis=0)
    cache_lower = natural[:, 0].reshape(groups * ncl, ncl, 2 * HD)
    cache_upper = natural[::-1, 1].reshape(groups * ncl, ncl, 2 * HD)
    cache = jnp.concatenate([cache_lower, cache_upper], axis=0).transpose(1, 0, 2)

    def exchange(outgoing):
        parts = [lax.dynamic_index_in_dim(outgoing, cl, axis=0, keepdims=False)]
        for shift in range(1, ncl):
            leaving = lax.dynamic_index_in_dim(outgoing, (cl + shift) % ncl, axis=0, keepdims=False)
            parts.append(lax.ppermute(leaving, CL, [(i, (i + shift) % ncl) for i in range(ncl)]))
        arrived = jnp.stack(parts)
        order = (cl - jnp.arange(ncl, dtype=jnp.int32)) % ncl
        return jnp.take(arrived, order, axis=0).transpose(1, 0, 2)

    cache_recv = exchange(cache)
    out_recv = exchange(out_send)
    attn_out = out_recv.reshape(tok_rows, local_width)
    key_cache = cache_recv[:, :, :HD].reshape(tok_rows, local_width)
    value_cache = cache_recv[:, :, HD:].reshape(tok_rows, local_width)
    return attn_out, key_cache, value_cache


def solution(mesh):
    ctx_size = mesh.shape["ctx"]
    tp_size = mesh.shape["tp"]
    nz = 8
    split = Mesh(
        mesh.devices.reshape(nz, 2, 2, ctx_size // (nz * 4), tp_size // 2, 2),
        ("z", "yhi", "ylo", "xlo", "xhi", "core"),
    )
    rows = P(CTX, TP)
    placed = (rows, P(None, TP), P(None, TP), P(None, TP), P(TP), P(TP), P())
    return jax.shard_map(
        per_device,
        mesh=split,
        in_specs=placed,
        out_specs=(rows, rows, rows),
        check_vma=False,
    )
```

```python
import functools

import jax
import jax.numpy as jnp
from jax import lax
from jax.experimental import pallas as pl
from jax.experimental.pallas import tpu as pltpu
from jax.sharding import Mesh
from jax.sharding import PartitionSpec as P

HD = 128
KB = 256
CL = ("ylo", "xlo")
CTX = ("z", "yhi", "ylo", "xlo")
TP = ("xhi", "core")


def rotate(matrix, position):
    row_count, columns = matrix.shape
    head_count = columns // HD
    rot_half = HD // 2
    shaped = matrix.reshape(row_count, head_count, HD)
    inverse_freq = 500000.0 ** (-2.0 * jnp.arange(rot_half, dtype=jnp.float32) / HD)
    angles = position.astype(jnp.float32)[:, None] * inverse_freq[None, :]
    cosine = jnp.cos(angles)[:, None, :]
    sine_part = jnp.sin(angles)[:, None, :]
    first_part = shaped[..., :rot_half]
    second_part = shaped[..., rot_half:]
    turned = jnp.concatenate(
        [
            first_part * cosine - second_part * sine_part,
            second_part * cosine + first_part * sine_part,
        ],
        axis=-1,
    )
    return turned.reshape(row_count, columns).astype(jnp.bfloat16)


def request_start(token_ids, prompt_lengths):
    req_ends = jnp.cumsum(prompt_lengths)
    starts = req_ends - prompt_lengths
    request = jnp.sum((token_ids[:, None] >= req_ends[None, :]).astype(jnp.int32), axis=1)
    onehot = request[:, None] == jnp.arange(prompt_lengths.shape[0], dtype=jnp.int32)[None, :]
    return jnp.sum(jnp.where(onehot, starts[None, :], 0), axis=1)


def attn_kernel(info_ref, q_ref, kv_ref, qtok_ref, qlo_ref, o_ref):
    blk = pl.program_id(0)
    lo = info_ref[2 * blk]
    hi = info_ref[2 * blk + 1]
    shift = info_ref[4]
    groups = info_ref[5]
    nblocks = 2 * groups
    q = q_ref[...]
    qtok = qtok_ref[...]
    qlo = qlo_ref[...]
    rows = q.shape[0]
    scale = HD ** (-0.5)

    first_tok = info_ref[6 + 2 * blk]
    last_lo = info_ref[7 + 2 * blk]

    def body(kb, carry):
        inside = (kb * KB >= last_lo) & (kb * KB + KB - 1 <= first_tok)
        return lax.cond(inside, lambda c: step(kb, c, False), lambda c: step(kb, c, True), carry)

    def step(kb, carry, masking):
        peak, total, acc = carry
        upper = kb >= groups
        group = jnp.where(upper, nblocks - 1 - kb, kb)
        slot = (group - shift + groups) % groups
        start = pl.multiple_of((slot * 2 + upper.astype(jnp.int32)) * KB, KB)
        block = kv_ref[pl.ds(start, KB), :]
        keys = block[:, :HD]
        vals = block[:, HD:]
        scores = (
            lax.dot_general(q, keys, (((1,), (1,)), ((), ())), preferred_element_type=jnp.float32)
            * scale
        )
        if masking:
            ktok = kb * KB + lax.broadcasted_iota(jnp.int32, (1, KB), 1)
            visible = (ktok >= qlo) & (ktok <= qtok)
            masked = jnp.where(visible, scores, -1e30)
            new_peak = jnp.maximum(peak, jnp.max(masked, axis=1, keepdims=True))
            weights = jnp.where(visible, jnp.exp(masked - new_peak), 0.0)
        else:
            new_peak = jnp.maximum(peak, jnp.max(scores, axis=1, keepdims=True))
            weights = jnp.exp(scores - new_peak)
        factor = jnp.exp(peak - new_peak)
        total = total * factor + jnp.sum(weights, axis=1, keepdims=True)
        acc = acc * factor + jnp.dot(
            weights.astype(jnp.bfloat16), vals, preferred_element_type=jnp.float32
        )
        return new_peak, total, acc

    start_state = (
        jnp.full((rows, 1), -1e30, jnp.float32),
        jnp.zeros((rows, 1), jnp.float32),
        jnp.zeros((rows, HD), jnp.float32),
    )
    _, total, acc = lax.fori_loop(lo, hi + 1, body, start_state)
    o_ref[...] = (acc / total).astype(o_ref.dtype)


def attention(info, q, kv, qtok, qlo):
    rows = q.shape[0]
    half = rows // 2
    return pl.pallas_call(
        attn_kernel,
        out_shape=jax.ShapeDtypeStruct((rows, HD), jnp.bfloat16),
        grid_spec=pltpu.PrefetchScalarGridSpec(
            num_scalar_prefetch=1,
            grid=(2,),
            in_specs=[
                pl.BlockSpec((half, HD), lambda i, info: (i, 0)),
                pl.BlockSpec(kv.shape, lambda i, info: (0, 0)),
                pl.BlockSpec((half, 1), lambda i, info: (i, 0)),
                pl.BlockSpec((half, 1), lambda i, info: (i, 0)),
            ],
            out_specs=pl.BlockSpec((half, HD), lambda i, info: (i, 0)),
        ),
    )(info, q, kv, qtok, qlo)


def z_ring(part, n):
    fwd = [part]
    bwd = [part]
    steps = n // 2
    for step in range(1, steps + 1):
        if step < steps:
            fwd.append(lax.ppermute(fwd[-1], "z", [(i, (i + 1) % n) for i in range(n)]))
            bwd.append(lax.ppermute(bwd[-1], "z", [(i, (i - 1) % n) for i in range(n)]))
        else:
            cut = part.shape[0] // 2
            far_a = lax.ppermute(fwd[-1][:cut], "z", [(i, (i + 1) % n) for i in range(n)])
            far_b = lax.ppermute(bwd[-1][cut:], "z", [(i, (i - 1) % n) for i in range(n)])
    ordered = bwd[: steps] + [far_a, far_b] + fwd[1:steps][::-1]
    return jnp.concatenate(ordered, axis=0)


def per_device(hidden_in, w_query, w_key, w_value, query_gain, key_gain, prompt_lengths):
    tok_rows = hidden_in.shape[0]
    half_rows = tok_rows // 2
    local_width = w_query.shape[1]
    head_count = local_width // HD
    nz = lax.axis_size("z")
    nyh = lax.axis_size("yhi")
    ncl = lax.axis_size("ylo") * lax.axis_size("xlo")
    z_idx = lax.axis_index("z")
    cg = z_idx * nyh + lax.axis_index("yhi")
    cl = lax.axis_index("ylo") * lax.axis_size("xlo") + lax.axis_index("xlo")
    groups = nz * nyh
    ctx_count = groups * ncl
    own = cg * ncl + cl

    xh = lax.axis_index("xhi")
    core = lax.axis_index("core")
    swap = [(0, 1), (1, 0)]
    across = lax.ppermute(hidden_in, "xhi", swap)
    pair = jnp.where(xh == 0, jnp.concatenate([hidden_in, across], axis=1), jnp.concatenate([across, hidden_in], axis=1))
    other = lax.ppermute(pair, "core", swap)
    width = hidden_in.shape[1]
    mine_first = jnp.concatenate([pair[:, :width], other[:, :width], pair[:, width:], other[:, width:]], axis=1)
    theirs_first = jnp.concatenate([other[:, :width], pair[:, :width], other[:, width:], pair[:, width:]], axis=1)
    pieces = jnp.where(core == 0, mine_first, theirs_first)
    queries = jnp.dot(pieces, w_query, preferred_element_type=jnp.float32)
    keys_proj = jnp.dot(pieces, w_key, preferred_element_type=jnp.float32)
    values = jnp.dot(pieces, w_value, preferred_element_type=jnp.float32).astype(jnp.bfloat16)
    squares = jnp.stack([jnp.sum(queries * queries, axis=1), jnp.sum(keys_proj * keys_proj, axis=1)])
    squares = squares + lax.ppermute(squares, "xhi", swap)
    squares = squares + lax.ppermute(squares, "core", swap)
    query_sq = squares[0]
    key_sq = squares[1]
    full_width = local_width * lax.axis_size("xhi") * lax.axis_size("core")
    query_normed = queries * lax.rsqrt(query_sq[:, None] / full_width + 1e-06) * query_gain
    key_normed = keys_proj * lax.rsqrt(key_sq[:, None] / full_width + 1e-06) * key_gain
    local_rows = jnp.arange(tok_rows, dtype=jnp.int32)
    block_of = jnp.where(local_rows < half_rows, own, 2 * ctx_count - 1 - own)
    token_ids = block_of * half_rows + local_rows % half_rows
    position = token_ids - request_start(token_ids, prompt_lengths)
    query_rot = rotate(query_normed, position)
    key_rot = rotate(key_normed, position)

    packed = jnp.concatenate(
        [
            query_rot.reshape(tok_rows, head_count, HD),
            key_rot.reshape(tok_rows, head_count, HD),
            values.reshape(tok_rows, head_count, HD),
        ],
        axis=2,
    )
    got = lax.all_to_all(packed, CL, split_axis=1, concat_axis=0, tiled=True)
    got = got.reshape(ncl, tok_rows, 3 * HD)
    lower = got[:, :half_rows].reshape(ncl * half_rows, 3 * HD)
    upper = got[::-1, half_rows:].reshape(ncl * half_rows, 3 * HD)
    mine = jnp.concatenate([lower, upper], axis=0)
    q_head = mine[:, :HD]
    kv_mine = mine[:, HD:]

    yh = lax.axis_index("yhi")
    kv_other = lax.ppermute(kv_mine, "yhi", swap)
    kv_pair = jnp.where(yh == 0, jnp.concatenate([kv_mine, kv_other], axis=0), jnp.concatenate([kv_other, kv_mine], axis=0))
    kv_all = z_ring(kv_pair, nz)

    span = ncl * half_rows
    total_tokens = 2 * ctx_count * half_rows
    r = jnp.arange(span, dtype=jnp.int32)
    q_tokens = jnp.concatenate([cg * span + r, total_tokens - (cg + 1) * span + r])
    q_lo = request_start(q_tokens, prompt_lengths)
    info = jnp.stack(
        [
            q_lo[0] // KB,
            cg,
            q_lo[span] // KB,
            2 * groups - 1 - cg,
            (z_idx * nyh) % groups,
            jnp.asarray(groups, jnp.int32),
            q_tokens[0],
            q_lo[span - 1],
            q_tokens[span],
            q_lo[2 * span - 1],
        ]
    ).astype(jnp.int32)
    out_head = attention(info, q_head, kv_all, q_tokens[:, None], q_lo[:, None])

    out_lower = out_head[:span].reshape(ncl, half_rows, HD)
    out_upper = out_head[span:].reshape(ncl, half_rows, HD)[::-1]
    out_send = jnp.stack([out_lower, out_upper], axis=1).reshape(ncl, tok_rows, HD)

    picked = kv_all.reshape(groups, 2, ncl, half_rows, 2 * HD)
    picked = lax.dynamic_slice_in_dim(picked, cg * ncl, ncl, axis=3)
    doubled = jnp.concatenate([picked, picked], axis=0)
    natural = lax.dynamic_slice_in_dim(doubled, (groups - (z_idx * nyh) % groups) % groups, groups, axis=0)
    cache_lower = natural[:, 0].reshape(groups * ncl, ncl, 2 * HD)
    cache_upper = natural[::-1, 1].reshape(groups * ncl, ncl, 2 * HD)
    cache = jnp.concatenate([cache_lower, cache_upper], axis=0).transpose(1, 0, 2)
    send = jnp.concatenate([out_send, cache], axis=2)
    recv = lax.all_to_all(send, CL, split_axis=0, concat_axis=0, tiled=True)
    recv = recv.transpose(1, 0, 2)
    attn_out = recv[:, :, :HD].reshape(tok_rows, local_width)
    key_cache = recv[:, :, HD : 2 * HD].reshape(tok_rows, local_width)
    value_cache = recv[:, :, 2 * HD :].reshape(tok_rows, local_width)
    return attn_out, key_cache, value_cache


def solution(mesh):
    ctx_size = mesh.shape["ctx"]
    tp_size = mesh.shape["tp"]
    nz = 8
    split = Mesh(
        mesh.devices.reshape(nz, 2, 2, ctx_size // (nz * 4), tp_size // 2, 2),
        ("z", "yhi", "ylo", "xlo", "xhi", "core"),
    )
    rows = P(CTX, TP)
    placed = (rows, P(None, TP), P(None, TP), P(None, TP), P(TP), P(TP), P())
    return jax.shard_map(
        per_device,
        mesh=split,
        in_specs=placed,
        out_specs=(rows, rows, rows),
        check_vma=False,
    )
```

```python
import functools

import jax
import jax.numpy as jnp
from jax import lax
from jax.experimental import pallas as pl
from jax.experimental.pallas import tpu as pltpu
from jax.sharding import Mesh
from jax.sharding import PartitionSpec as P

HD = 128
KB = 256
CL = ("ylo", "xlo")
CTX = ("z", "yhi", "ylo", "xlo")
TP = ("xhi", "core")


def rotate(matrix, position):
    row_count, columns = matrix.shape
    head_count = columns // HD
    rot_half = HD // 2
    shaped = matrix.reshape(row_count, head_count, HD)
    inverse_freq = 500000.0 ** (-2.0 * jnp.arange(rot_half, dtype=jnp.float32) / HD)
    angles = position.astype(jnp.float32)[:, None] * inverse_freq[None, :]
    cosine = jnp.cos(angles)[:, None, :]
    sine_part = jnp.sin(angles)[:, None, :]
    first_part = shaped[..., :rot_half]
    second_part = shaped[..., rot_half:]
    turned = jnp.concatenate(
        [
            first_part * cosine - second_part * sine_part,
            second_part * cosine + first_part * sine_part,
        ],
        axis=-1,
    )
    return turned.reshape(row_count, columns).astype(jnp.bfloat16)


def request_start(token_ids, prompt_lengths):
    req_ends = jnp.cumsum(prompt_lengths)
    starts = req_ends - prompt_lengths
    request = jnp.sum((token_ids[:, None] >= req_ends[None, :]).astype(jnp.int32), axis=1)
    onehot = request[:, None] == jnp.arange(prompt_lengths.shape[0], dtype=jnp.int32)[None, :]
    return jnp.sum(jnp.where(onehot, starts[None, :], 0), axis=1)


def attn_kernel(info_ref, q_ref, kv_ref, qtok_ref, qlo_ref, o_ref):
    blk = pl.program_id(0)
    lo = info_ref[2 * blk]
    hi = info_ref[2 * blk + 1]
    shift = info_ref[4]
    groups = info_ref[5]
    nblocks = 2 * groups
    q = q_ref[...]
    qtok = qtok_ref[...]
    qlo = qlo_ref[...]
    rows = q.shape[0]
    scale = HD ** (-0.5)

    first_tok = info_ref[6 + 2 * blk]
    last_lo = info_ref[7 + 2 * blk]

    def body(kb, carry):
        inside = (kb * KB >= last_lo) & (kb * KB + KB - 1 <= first_tok)
        return lax.cond(inside, lambda c: step(kb, c, False), lambda c: step(kb, c, True), carry)

    def step(kb, carry, masking):
        peak, total, acc = carry
        upper = kb >= groups
        group = jnp.where(upper, nblocks - 1 - kb, kb)
        slot = (group - shift + groups) % groups
        start = pl.multiple_of((slot * 2 + upper.astype(jnp.int32)) * KB, KB)
        block = kv_ref[pl.ds(start, KB), :]
        keys = block[:, :HD]
        vals = block[:, HD:]
        scores = (
            lax.dot_general(q, keys, (((1,), (1,)), ((), ())), preferred_element_type=jnp.float32)
            * scale
        )
        if masking:
            ktok = kb * KB + lax.broadcasted_iota(jnp.int32, (1, KB), 1)
            visible = (ktok >= qlo) & (ktok <= qtok)
            masked = jnp.where(visible, scores, -1e30)
            new_peak = jnp.maximum(peak, jnp.max(masked, axis=1, keepdims=True))
            weights = jnp.where(visible, jnp.exp(masked - new_peak), 0.0)
        else:
            new_peak = jnp.maximum(peak, jnp.max(scores, axis=1, keepdims=True))
            weights = jnp.exp(scores - new_peak)
        factor = jnp.exp(peak - new_peak)
        total = total * factor + jnp.sum(weights, axis=1, keepdims=True)
        acc = acc * factor + jnp.dot(
            weights.astype(jnp.bfloat16), vals, preferred_element_type=jnp.float32
        )
        return new_peak, total, acc

    start_state = (
        jnp.full((rows, 1), -1e30, jnp.float32),
        jnp.zeros((rows, 1), jnp.float32),
        jnp.zeros((rows, HD), jnp.float32),
    )
    _, total, acc = lax.fori_loop(lo, hi + 1, body, start_state)
    o_ref[...] = (acc / total).astype(o_ref.dtype)


def attention(info, q, kv, qtok, qlo):
    rows = q.shape[0]
    half = rows // 2
    return pl.pallas_call(
        attn_kernel,
        out_shape=jax.ShapeDtypeStruct((rows, HD), jnp.bfloat16),
        grid_spec=pltpu.PrefetchScalarGridSpec(
            num_scalar_prefetch=1,
            grid=(2,),
            in_specs=[
                pl.BlockSpec((half, HD), lambda i, info: (i, 0)),
                pl.BlockSpec(kv.shape, lambda i, info: (0, 0)),
                pl.BlockSpec((half, 1), lambda i, info: (i, 0)),
                pl.BlockSpec((half, 1), lambda i, info: (i, 0)),
            ],
            out_specs=pl.BlockSpec((half, HD), lambda i, info: (i, 0)),
        ),
    )(info, q, kv, qtok, qlo)


def z_ring(part, n):
    fwd = [part]
    bwd = [part]
    steps = n // 2
    for step in range(1, steps + 1):
        if step < steps:
            fwd.append(lax.ppermute(fwd[-1], "z", [(i, (i + 1) % n) for i in range(n)]))
            bwd.append(lax.ppermute(bwd[-1], "z", [(i, (i - 1) % n) for i in range(n)]))
        else:
            cut = part.shape[0] // 2
            far_a = lax.ppermute(fwd[-1][:cut], "z", [(i, (i + 1) % n) for i in range(n)])
            far_b = lax.ppermute(bwd[-1][cut:], "z", [(i, (i - 1) % n) for i in range(n)])
    ordered = bwd[: steps] + [far_a, far_b] + fwd[1:steps][::-1]
    return ordered


def per_device(hidden_in, w_query, w_key, w_value, query_gain, key_gain, prompt_lengths):
    tok_rows = hidden_in.shape[0]
    half_rows = tok_rows // 2
    local_width = w_query.shape[1]
    head_count = local_width // HD
    nz = lax.axis_size("z")
    nyh = lax.axis_size("yhi")
    ncl = lax.axis_size("ylo") * lax.axis_size("xlo")
    z_idx = lax.axis_index("z")
    cg = z_idx * nyh + lax.axis_index("yhi")
    cl = lax.axis_index("ylo") * lax.axis_size("xlo") + lax.axis_index("xlo")
    groups = nz * nyh
    ctx_count = groups * ncl
    own = cg * ncl + cl

    xh = lax.axis_index("xhi")
    core = lax.axis_index("core")
    swap = [(0, 1), (1, 0)]
    across = lax.ppermute(hidden_in, "xhi", swap)
    pair = jnp.where(xh == 0, jnp.concatenate([hidden_in, across], axis=1), jnp.concatenate([across, hidden_in], axis=1))
    other = lax.ppermute(pair, "core", swap)
    width = hidden_in.shape[1]
    mine_first = jnp.concatenate([pair[:, :width], other[:, :width], pair[:, width:], other[:, width:]], axis=1)
    theirs_first = jnp.concatenate([other[:, :width], pair[:, :width], other[:, width:], pair[:, width:]], axis=1)
    pieces = jnp.where(core == 0, mine_first, theirs_first)
    queries = jnp.dot(pieces, w_query, preferred_element_type=jnp.float32)
    keys_proj = jnp.dot(pieces, w_key, preferred_element_type=jnp.float32)
    values = jnp.dot(pieces, w_value, preferred_element_type=jnp.float32).astype(jnp.bfloat16)
    squares = jnp.stack([jnp.sum(queries * queries, axis=1), jnp.sum(keys_proj * keys_proj, axis=1)])
    squares = squares + lax.ppermute(squares, "xhi", swap)
    squares = squares + lax.ppermute(squares, "core", swap)
    query_sq = squares[0]
    key_sq = squares[1]
    full_width = local_width * lax.axis_size("xhi") * lax.axis_size("core")
    query_normed = queries * lax.rsqrt(query_sq[:, None] / full_width + 1e-06) * query_gain
    key_normed = keys_proj * lax.rsqrt(key_sq[:, None] / full_width + 1e-06) * key_gain
    local_rows = jnp.arange(tok_rows, dtype=jnp.int32)
    block_of = jnp.where(local_rows < half_rows, own, 2 * ctx_count - 1 - own)
    token_ids = block_of * half_rows + local_rows % half_rows
    position = token_ids - request_start(token_ids, prompt_lengths)
    query_rot = rotate(query_normed, position)
    key_rot = rotate(key_normed, position)

    packed = jnp.concatenate(
        [key_rot.reshape(tok_rows, head_count, HD), values.reshape(tok_rows, head_count, HD)], axis=2
    )

    def head_split(per_head):
        width = per_head.shape[2]
        got = lax.all_to_all(per_head, CL, split_axis=1, concat_axis=0, tiled=True)
        got = got.reshape(ncl, tok_rows, width)
        lower = got[:, :half_rows].reshape(ncl * half_rows, width)
        upper = got[::-1, half_rows:].reshape(ncl * half_rows, width)
        return jnp.concatenate([lower, upper], axis=0)

    kv_mine = head_split(packed)

    yh = lax.axis_index("yhi")
    kv_other = lax.ppermute(kv_mine, "yhi", swap)
    kv_pair = jnp.where(yh == 0, jnp.concatenate([kv_mine, kv_other], axis=0), jnp.concatenate([kv_other, kv_mine], axis=0))
    ring_parts = z_ring(kv_pair, nz)
    q_late, _ = lax.optimization_barrier((query_rot, ring_parts[1]))
    q_head = head_split(q_late.reshape(tok_rows, head_count, HD))
    kv_all = jnp.concatenate(ring_parts, axis=0)

    span = ncl * half_rows
    total_tokens = 2 * ctx_count * half_rows
    r = jnp.arange(span, dtype=jnp.int32)
    q_tokens = jnp.concatenate([cg * span + r, total_tokens - (cg + 1) * span + r])
    q_lo = request_start(q_tokens, prompt_lengths)
    info = jnp.stack(
        [
            q_lo[0] // KB,
            cg,
            q_lo[span] // KB,
            2 * groups - 1 - cg,
            (z_idx * nyh) % groups,
            jnp.asarray(groups, jnp.int32),
            q_tokens[0],
            q_lo[span - 1],
            q_tokens[span],
            q_lo[2 * span - 1],
        ]
    ).astype(jnp.int32)
    out_head = attention(info, q_head, kv_all, q_tokens[:, None], q_lo[:, None])

    out_lower = out_head[:span].reshape(ncl, half_rows, HD)
    out_upper = out_head[span:].reshape(ncl, half_rows, HD)[::-1]
    out_send = jnp.stack([out_lower, out_upper], axis=1).reshape(ncl, tok_rows, HD)

    picked = kv_all.reshape(groups, 2, ncl, half_rows, 2 * HD)
    picked = lax.dynamic_slice_in_dim(picked, cg * ncl, ncl, axis=3)
    doubled = jnp.concatenate([picked, picked], axis=0)
    natural = lax.dynamic_slice_in_dim(doubled, (groups - (z_idx * nyh) % groups) % groups, groups, axis=0)
    cache_lower = natural[:, 0].reshape(groups * ncl, ncl, 2 * HD)
    cache_upper = natural[::-1, 1].reshape(groups * ncl, ncl, 2 * HD)
    cache = jnp.concatenate([cache_lower, cache_upper], axis=0).transpose(1, 0, 2)
    send = jnp.concatenate([out_send, cache], axis=2)
    recv = lax.all_to_all(send, CL, split_axis=0, concat_axis=0, tiled=True)
    recv = recv.transpose(1, 0, 2)
    attn_out = recv[:, :, :HD].reshape(tok_rows, local_width)
    key_cache = recv[:, :, HD : 2 * HD].reshape(tok_rows, local_width)
    value_cache = recv[:, :, 2 * HD :].reshape(tok_rows, local_width)
    return attn_out, key_cache, value_cache


def solution(mesh):
    ctx_size = mesh.shape["ctx"]
    tp_size = mesh.shape["tp"]
    nz = 8
    split = Mesh(
        mesh.devices.reshape(nz, 2, 2, ctx_size // (nz * 4), tp_size // 2, 2),
        ("z", "yhi", "ylo", "xlo", "xhi", "core"),
    )
    rows = P(CTX, TP)
    placed = (rows, P(None, TP), P(None, TP), P(None, TP), P(TP), P(TP), P())
    return jax.shard_map(
        per_device,
        mesh=split,
        in_specs=placed,
        out_specs=(rows, rows, rows),
        check_vma=False,
    )
```

```python
import functools

import jax
import jax.numpy as jnp
from jax import lax
from jax.experimental import pallas as pl
from jax.experimental.pallas import tpu as pltpu
from jax.sharding import Mesh
from jax.sharding import PartitionSpec as P

HD = 128
KB = 256
CL = ("ylo", "xlo")
CTX = ("z", "yhi", "ylo", "xlo")
TP = ("xhi", "core")


def rotate(matrix, position):
    row_count, columns = matrix.shape
    head_count = columns // HD
    rot_half = HD // 2
    shaped = matrix.reshape(row_count, head_count, HD)
    inverse_freq = 500000.0 ** (-2.0 * jnp.arange(rot_half, dtype=jnp.float32) / HD)
    angles = position.astype(jnp.float32)[:, None] * inverse_freq[None, :]
    cosine = jnp.cos(angles)[:, None, :]
    sine_part = jnp.sin(angles)[:, None, :]
    first_part = shaped[..., :rot_half]
    second_part = shaped[..., rot_half:]
    turned = jnp.concatenate(
        [
            first_part * cosine - second_part * sine_part,
            second_part * cosine + first_part * sine_part,
        ],
        axis=-1,
    )
    return turned.reshape(row_count, columns).astype(jnp.bfloat16)


def request_start(token_ids, prompt_lengths):
    req_ends = jnp.cumsum(prompt_lengths)
    starts = req_ends - prompt_lengths
    request = jnp.sum((token_ids[:, None] >= req_ends[None, :]).astype(jnp.int32), axis=1)
    onehot = request[:, None] == jnp.arange(prompt_lengths.shape[0], dtype=jnp.int32)[None, :]
    return jnp.sum(jnp.where(onehot, starts[None, :], 0), axis=1)


def attn_kernel(info_ref, q_ref, kv_ref, qtok_ref, qlo_ref, o_ref):
    blk = pl.program_id(0)
    lo = info_ref[2 * blk]
    hi = info_ref[2 * blk + 1]
    shift = info_ref[4]
    groups = info_ref[5]
    nblocks = 2 * groups
    q = q_ref[...]
    qtok = qtok_ref[...]
    qlo = qlo_ref[...]
    rows = q.shape[0]
    scale = HD ** (-0.5)

    first_tok = info_ref[6 + 2 * blk]
    last_lo = info_ref[7 + 2 * blk]

    def body(kb, carry):
        inside = (kb * KB >= last_lo) & (kb * KB + KB - 1 <= first_tok)
        return lax.cond(inside, lambda c: step(kb, c, False), lambda c: step(kb, c, True), carry)

    def step(kb, carry, masking):
        peak, total, acc = carry
        upper = kb >= groups
        group = jnp.where(upper, nblocks - 1 - kb, kb)
        slot = (group - shift + groups) % groups
        start = pl.multiple_of((slot * 2 + upper.astype(jnp.int32)) * KB, KB)
        block = kv_ref[pl.ds(start, KB), :]
        keys = block[:, :HD]
        vals = block[:, HD:]
        scores = (
            lax.dot_general(q, keys, (((1,), (1,)), ((), ())), preferred_element_type=jnp.float32)
            * scale
        )
        if masking:
            ktok = kb * KB + lax.broadcasted_iota(jnp.int32, (1, KB), 1)
            visible = (ktok >= qlo) & (ktok <= qtok)
            masked = jnp.where(visible, scores, -1e30)
            new_peak = jnp.maximum(peak, jnp.max(masked, axis=1, keepdims=True))
            weights = jnp.where(visible, jnp.exp(masked - new_peak), 0.0)
        else:
            new_peak = jnp.maximum(peak, jnp.max(scores, axis=1, keepdims=True))
            weights = jnp.exp(scores - new_peak)
        factor = jnp.exp(peak - new_peak)
        total = total * factor + jnp.sum(weights, axis=1, keepdims=True)
        acc = acc * factor + jnp.dot(
            weights.astype(jnp.bfloat16), vals, preferred_element_type=jnp.float32
        )
        return new_peak, total, acc

    start_state = (
        jnp.full((rows, 1), -1e30, jnp.float32),
        jnp.zeros((rows, 1), jnp.float32),
        jnp.zeros((rows, HD), jnp.float32),
    )
    _, total, acc = lax.fori_loop(lo, hi + 1, body, start_state)
    o_ref[...] = (acc / total).astype(o_ref.dtype)


def attention(info, q, kv, qtok, qlo):
    rows = q.shape[0]
    half = rows // 2
    return pl.pallas_call(
        attn_kernel,
        out_shape=jax.ShapeDtypeStruct((rows, HD), jnp.bfloat16),
        grid_spec=pltpu.PrefetchScalarGridSpec(
            num_scalar_prefetch=1,
            grid=(2,),
            in_specs=[
                pl.BlockSpec((half, HD), lambda i, info: (i, 0)),
                pl.BlockSpec(kv.shape, lambda i, info: (0, 0)),
                pl.BlockSpec((half, 1), lambda i, info: (i, 0)),
                pl.BlockSpec((half, 1), lambda i, info: (i, 0)),
            ],
            out_specs=pl.BlockSpec((half, HD), lambda i, info: (i, 0)),
        ),
    )(info, q, kv, qtok, qlo)


def z_ring(part, n):
    fwd = [part]
    bwd = [part]
    steps = n // 2
    for step in range(1, steps + 1):
        if step < steps:
            fwd.append(lax.ppermute(fwd[-1], "z", [(i, (i + 1) % n) for i in range(n)]))
            bwd.append(lax.ppermute(bwd[-1], "z", [(i, (i - 1) % n) for i in range(n)]))
        else:
            cut = part.shape[0] // 2
            far_a = lax.ppermute(fwd[-1][:cut], "z", [(i, (i + 1) % n) for i in range(n)])
            far_b = lax.ppermute(bwd[-1][cut:], "z", [(i, (i - 1) % n) for i in range(n)])
    ordered = bwd[: steps] + [far_a, far_b] + fwd[1:steps][::-1]
    return jnp.concatenate(ordered, axis=0)


def per_device(hidden_in, w_query, w_key, w_value, query_gain, key_gain, prompt_lengths):
    tok_rows = hidden_in.shape[0]
    half_rows = tok_rows // 2
    local_width = w_query.shape[1]
    head_count = local_width // HD
    nz = lax.axis_size("z")
    nyh = lax.axis_size("yhi")
    ncl = lax.axis_size("ylo") * lax.axis_size("xlo")
    z_idx = lax.axis_index("z")
    cg = z_idx * nyh + lax.axis_index("yhi")
    cl = lax.axis_index("ylo") * lax.axis_size("xlo") + lax.axis_index("xlo")
    groups = nz * nyh
    ctx_count = groups * ncl
    own = cg * ncl + cl

    xh = lax.axis_index("xhi")
    core = lax.axis_index("core")
    swap = [(0, 1), (1, 0)]
    ntp = lax.axis_size("xhi") * lax.axis_size("core")
    tp_idx = xh * lax.axis_size("core") + core
    order = (tp_idx - jnp.arange(ntp, dtype=jnp.int32)) % ntp

    def tp_gather(piece):
        got = [piece] + [lax.ppermute(piece, TP, [(i, (i + k) % ntp) for i in range(ntp)]) for k in range(1, ntp)]
        return jnp.take(jnp.stack(got), order, axis=0)

    pieces = tp_gather(hidden_in).transpose(1, 0, 2).reshape(tok_rows, ntp * hidden_in.shape[1])
    queries = jnp.dot(pieces, w_query, preferred_element_type=jnp.float32)
    keys_proj = jnp.dot(pieces, w_key, preferred_element_type=jnp.float32)
    values = jnp.dot(pieces, w_value, preferred_element_type=jnp.float32).astype(jnp.bfloat16)
    squares = jnp.stack([jnp.sum(queries * queries, axis=1), jnp.sum(keys_proj * keys_proj, axis=1)])
    squares = jnp.sum(tp_gather(squares), axis=0)
    query_sq = squares[0]
    key_sq = squares[1]
    full_width = local_width * lax.axis_size("xhi") * lax.axis_size("core")
    query_normed = queries * lax.rsqrt(query_sq[:, None] / full_width + 1e-06) * query_gain
    key_normed = keys_proj * lax.rsqrt(key_sq[:, None] / full_width + 1e-06) * key_gain
    local_rows = jnp.arange(tok_rows, dtype=jnp.int32)
    block_of = jnp.where(local_rows < half_rows, own, 2 * ctx_count - 1 - own)
    token_ids = block_of * half_rows + local_rows % half_rows
    position = token_ids - request_start(token_ids, prompt_lengths)
    query_rot = rotate(query_normed, position)
    key_rot = rotate(key_normed, position)

    packed = jnp.concatenate(
        [
            query_rot.reshape(tok_rows, head_count, HD),
            key_rot.reshape(tok_rows, head_count, HD),
            values.reshape(tok_rows, head_count, HD),
        ],
        axis=2,
    )
    got = lax.all_to_all(packed, CL, split_axis=1, concat_axis=0, tiled=True)
    got = got.reshape(ncl, tok_rows, 3 * HD)
    lower = got[:, :half_rows].reshape(ncl * half_rows, 3 * HD)
    upper = got[::-1, half_rows:].reshape(ncl * half_rows, 3 * HD)
    mine = jnp.concatenate([lower, upper], axis=0)
    q_head = mine[:, :HD]
    kv_mine = mine[:, HD:]

    yh = lax.axis_index("yhi")
    kv_other = lax.ppermute(kv_mine, "yhi", swap)
    kv_pair = jnp.where(yh == 0, jnp.concatenate([kv_mine, kv_other], axis=0), jnp.concatenate([kv_other, kv_mine], axis=0))
    kv_all = z_ring(kv_pair, nz)

    span = ncl * half_rows
    total_tokens = 2 * ctx_count * half_rows
    r = jnp.arange(span, dtype=jnp.int32)
    q_tokens = jnp.concatenate([cg * span + r, total_tokens - (cg + 1) * span + r])
    q_lo = request_start(q_tokens, prompt_lengths)
    info = jnp.stack(
        [
            q_lo[0] // KB,
            cg,
            q_lo[span] // KB,
            2 * groups - 1 - cg,
            (z_idx * nyh) % groups,
            jnp.asarray(groups, jnp.int32),
            q_tokens[0],
            q_lo[span - 1],
            q_tokens[span],
            q_lo[2 * span - 1],
        ]
    ).astype(jnp.int32)
    out_head = attention(info, q_head, kv_all, q_tokens[:, None], q_lo[:, None])

    out_lower = out_head[:span].reshape(ncl, half_rows, HD)
    out_upper = out_head[span:].reshape(ncl, half_rows, HD)[::-1]
    out_send = jnp.stack([out_lower, out_upper], axis=1).reshape(ncl, tok_rows, HD)

    picked = kv_all.reshape(groups, 2, ncl, half_rows, 2 * HD)
    picked = lax.dynamic_slice_in_dim(picked, cg * ncl, ncl, axis=3)
    doubled = jnp.concatenate([picked, picked], axis=0)
    natural = lax.dynamic_slice_in_dim(doubled, (groups - (z_idx * nyh) % groups) % groups, groups, axis=0)
    cache_lower = natural[:, 0].reshape(groups * ncl, ncl, 2 * HD)
    cache_upper = natural[::-1, 1].reshape(groups * ncl, ncl, 2 * HD)
    cache = jnp.concatenate([cache_lower, cache_upper], axis=0).transpose(1, 0, 2)
    send = jnp.concatenate([out_send, cache], axis=2)
    recv = lax.all_to_all(send, CL, split_axis=0, concat_axis=0, tiled=True)
    recv = recv.transpose(1, 0, 2)
    attn_out = recv[:, :, :HD].reshape(tok_rows, local_width)
    key_cache = recv[:, :, HD : 2 * HD].reshape(tok_rows, local_width)
    value_cache = recv[:, :, 2 * HD :].reshape(tok_rows, local_width)
    return attn_out, key_cache, value_cache


def solution(mesh):
    ctx_size = mesh.shape["ctx"]
    tp_size = mesh.shape["tp"]
    nz = 8
    split = Mesh(
        mesh.devices.reshape(nz, 2, 2, ctx_size // (nz * 4), tp_size // 2, 2),
        ("z", "yhi", "ylo", "xlo", "xhi", "core"),
    )
    rows = P(CTX, TP)
    placed = (rows, P(None, TP), P(None, TP), P(None, TP), P(TP), P(TP), P())
    return jax.shard_map(
        per_device,
        mesh=split,
        in_specs=placed,
        out_specs=(rows, rows, rows),
        check_vma=False,
    )
```

```python
import functools

import jax
import jax.numpy as jnp
from jax import lax
from jax.experimental import pallas as pl
from jax.experimental.pallas import tpu as pltpu
from jax.sharding import Mesh
from jax.sharding import PartitionSpec as P

HD = 128
KB = 256
CL = ("ylo", "xlo")
CTX = ("z", "yhi", "ylo", "xlo")
TP = ("xhi", "core")


def rotate(matrix, position):
    row_count, columns = matrix.shape
    head_count = columns // HD
    rot_half = HD // 2
    shaped = matrix.reshape(row_count, head_count, HD)
    inverse_freq = 500000.0 ** (-2.0 * jnp.arange(rot_half, dtype=jnp.float32) / HD)
    angles = position.astype(jnp.float32)[:, None] * inverse_freq[None, :]
    cosine = jnp.cos(angles)[:, None, :]
    sine_part = jnp.sin(angles)[:, None, :]
    first_part = shaped[..., :rot_half]
    second_part = shaped[..., rot_half:]
    turned = jnp.concatenate(
        [
            first_part * cosine - second_part * sine_part,
            second_part * cosine + first_part * sine_part,
        ],
        axis=-1,
    )
    return turned.reshape(row_count, columns).astype(jnp.bfloat16)


def request_start(token_ids, prompt_lengths):
    req_ends = jnp.cumsum(prompt_lengths)
    starts = req_ends - prompt_lengths
    request = jnp.sum((token_ids[:, None] >= req_ends[None, :]).astype(jnp.int32), axis=1)
    onehot = request[:, None] == jnp.arange(prompt_lengths.shape[0], dtype=jnp.int32)[None, :]
    return jnp.sum(jnp.where(onehot, starts[None, :], 0), axis=1)


def attn_kernel(info_ref, q_ref, kv_ref, qtok_ref, qlo_ref, o_ref):
    blk = pl.program_id(0)
    lo = info_ref[2 * blk]
    hi = info_ref[2 * blk + 1]
    shift = info_ref[4]
    groups = info_ref[5]
    nblocks = 2 * groups
    q = q_ref[...]
    qtok = qtok_ref[...]
    qlo = qlo_ref[...]
    rows = q.shape[0]
    scale = HD ** (-0.5)

    def body(kb, carry):
        peak, total, acc = carry
        upper = kb >= groups
        group = jnp.where(upper, nblocks - 1 - kb, kb)
        slot = (group - shift + groups) % groups
        start = pl.multiple_of((slot * 2 + upper.astype(jnp.int32)) * KB, KB)
        block = kv_ref[pl.ds(start, KB), :]
        keys = block[:, :HD]
        vals = block[:, HD:]
        scores = (
            lax.dot_general(q, keys, (((1,), (1,)), ((), ())), preferred_element_type=jnp.float32)
            * scale
        )
        ktok = kb * KB + lax.broadcasted_iota(jnp.int32, (1, KB), 1)
        visible = (ktok >= qlo) & (ktok <= qtok)
        masked = jnp.where(visible, scores, -1e30)
        new_peak = jnp.maximum(peak, jnp.max(masked, axis=1, keepdims=True))
        weights = jnp.where(visible, jnp.exp(masked - new_peak), 0.0)
        factor = jnp.exp(peak - new_peak)
        total = total * factor + jnp.sum(weights, axis=1, keepdims=True)
        acc = acc * factor + jnp.dot(
            weights.astype(jnp.bfloat16), vals, preferred_element_type=jnp.float32
        )
        return new_peak, total, acc

    start_state = (
        jnp.full((rows, 1), -1e30, jnp.float32),
        jnp.zeros((rows, 1), jnp.float32),
        jnp.zeros((rows, HD), jnp.float32),
    )
    _, total, acc = lax.fori_loop(lo, hi + 1, body, start_state)
    o_ref[...] = (acc / total).astype(o_ref.dtype)


def attention(info, q, kv, qtok, qlo):
    rows = q.shape[0]
    half = rows // 2
    return pl.pallas_call(
        attn_kernel,
        out_shape=jax.ShapeDtypeStruct((rows, HD), jnp.bfloat16),
        grid_spec=pltpu.PrefetchScalarGridSpec(
            num_scalar_prefetch=1,
            grid=(2,),
            in_specs=[
                pl.BlockSpec((half, HD), lambda i, info: (i, 0)),
                pl.BlockSpec(kv.shape, lambda i, info: (0, 0)),
                pl.BlockSpec((half, 1), lambda i, info: (i, 0)),
                pl.BlockSpec((half, 1), lambda i, info: (i, 0)),
            ],
            out_specs=pl.BlockSpec((half, HD), lambda i, info: (i, 0)),
        ),
    )(info, q, kv, qtok, qlo)


def z_ring(part, n):
    fwd = [part]
    bwd = [part]
    steps = n // 2
    for step in range(1, steps + 1):
        if step < steps:
            fwd.append(lax.ppermute(fwd[-1], "z", [(i, (i + 1) % n) for i in range(n)]))
            bwd.append(lax.ppermute(bwd[-1], "z", [(i, (i - 1) % n) for i in range(n)]))
        else:
            cut = part.shape[0] // 2
            far_a = lax.ppermute(fwd[-1][:cut], "z", [(i, (i + 1) % n) for i in range(n)])
            far_b = lax.ppermute(bwd[-1][cut:], "z", [(i, (i - 1) % n) for i in range(n)])
    ordered = bwd[: steps] + [far_a, far_b] + fwd[1:steps][::-1]
    return jnp.concatenate(ordered, axis=0)


def span_rows(ncl, half_rows):
    return ncl * half_rows


def per_device(hidden_in, w_query, w_key, w_value, query_gain, key_gain, prompt_lengths):
    tok_rows = hidden_in.shape[0]
    half_rows = tok_rows // 2
    local_width = w_query.shape[1]
    head_count = local_width // HD
    nz = lax.axis_size("z")
    nyh = lax.axis_size("yhi")
    ncl = lax.axis_size("ylo") * lax.axis_size("xlo")
    z_idx = lax.axis_index("z")
    cg = z_idx * nyh + lax.axis_index("yhi")
    cl = lax.axis_index("ylo") * lax.axis_size("xlo") + lax.axis_index("xlo")
    groups = nz * nyh
    ctx_count = groups * ncl
    own = cg * ncl + cl

    xh = lax.axis_index("xhi")
    core = lax.axis_index("core")
    swap = [(0, 1), (1, 0)]
    across = lax.ppermute(hidden_in, "xhi", swap)
    pair = jnp.where(xh == 0, jnp.concatenate([hidden_in, across], axis=1), jnp.concatenate([across, hidden_in], axis=1))
    other = lax.ppermute(pair, "core", swap)
    width = hidden_in.shape[1]
    mine_first = jnp.concatenate([pair[:, :width], other[:, :width], pair[:, width:], other[:, width:]], axis=1)
    theirs_first = jnp.concatenate([other[:, :width], pair[:, :width], other[:, width:], pair[:, width:]], axis=1)
    pieces = jnp.where(core == 0, mine_first, theirs_first)
    queries = jnp.dot(pieces, w_query, preferred_element_type=jnp.float32)
    keys_proj = jnp.dot(pieces, w_key, preferred_element_type=jnp.float32)
    values = jnp.dot(pieces, w_value, preferred_element_type=jnp.float32).astype(jnp.bfloat16)
    squares = jnp.stack([jnp.sum(queries * queries, axis=1), jnp.sum(keys_proj * keys_proj, axis=1)])
    squares = squares + lax.ppermute(squares, "xhi", swap)
    squares = squares + lax.ppermute(squares, "core", swap)
    query_sq = squares[0]
    key_sq = squares[1]
    full_width = local_width * lax.axis_size("xhi") * lax.axis_size("core")
    query_normed = queries * lax.rsqrt(query_sq[:, None] / full_width + 1e-06) * query_gain
    key_normed = keys_proj * lax.rsqrt(key_sq[:, None] / full_width + 1e-06) * key_gain
    local_rows = jnp.arange(tok_rows, dtype=jnp.int32)
    block_of = jnp.where(local_rows < half_rows, own, 2 * ctx_count - 1 - own)
    token_ids = block_of * half_rows + local_rows % half_rows
    position = token_ids - request_start(token_ids, prompt_lengths)
    query_rot = rotate(query_normed, position)
    key_rot = rotate(key_normed, position)

    packed = jnp.concatenate(
        [
            query_rot.reshape(tok_rows, head_count, HD),
            key_rot.reshape(tok_rows, head_count, HD),
            values.reshape(tok_rows, head_count, HD),
        ],
        axis=2,
    )
    spread = jnp.broadcast_to(packed[:, None], (tok_rows, nyh, head_count, 3 * HD))
    spread = spread.reshape(tok_rows, nyh * head_count, 3 * HD)
    got = lax.all_to_all(spread, ("yhi",) + CL, split_axis=1, concat_axis=0, tiled=True)
    got = got.reshape(nyh, ncl, tok_rows, 3 * HD)
    lower = got[:, :, :half_rows].reshape(nyh, ncl * half_rows, 3 * HD)
    upper = got[:, ::-1, half_rows:].reshape(nyh, ncl * half_rows, 3 * HD)
    both = jnp.concatenate([lower, upper], axis=1)
    yh = lax.axis_index("yhi")
    q_head = lax.dynamic_index_in_dim(both, yh, axis=0, keepdims=False)[:, :HD]
    kv_pair = both[:, :, HD:].reshape(nyh * 2 * span_rows(ncl, half_rows), 2 * HD)
    kv_all = z_ring(kv_pair, nz)

    span = ncl * half_rows
    total_tokens = 2 * ctx_count * half_rows
    r = jnp.arange(span, dtype=jnp.int32)
    q_tokens = jnp.concatenate([cg * span + r, total_tokens - (cg + 1) * span + r])
    q_lo = request_start(q_tokens, prompt_lengths)
    info = jnp.stack(
        [
            q_lo[0] // KB,
            cg,
            q_lo[span] // KB,
            2 * groups - 1 - cg,
            (z_idx * nyh) % groups,
            jnp.asarray(groups, jnp.int32),
        ]
    ).astype(jnp.int32)
    out_head = attention(info, q_head, kv_all, q_tokens[:, None], q_lo[:, None])

    out_lower = out_head[:span].reshape(ncl, half_rows, HD)
    out_upper = out_head[span:].reshape(ncl, half_rows, HD)[::-1]
    out_send = jnp.stack([out_lower, out_upper], axis=1).reshape(ncl, tok_rows, HD)

    picked = kv_all.reshape(groups, 2, ncl, half_rows, 2 * HD)
    picked = lax.dynamic_slice_in_dim(picked, cg * ncl, ncl, axis=3)
    doubled = jnp.concatenate([picked, picked], axis=0)
    natural = lax.dynamic_slice_in_dim(doubled, (groups - (z_idx * nyh) % groups) % groups, groups, axis=0)
    cache_lower = natural[:, 0].reshape(groups * ncl, ncl, 2 * HD)
    cache_upper = natural[::-1, 1].reshape(groups * ncl, ncl, 2 * HD)
    cache = jnp.concatenate([cache_lower, cache_upper], axis=0).transpose(1, 0, 2)
    send = jnp.concatenate([out_send, cache], axis=2)
    recv = lax.all_to_all(send, CL, split_axis=0, concat_axis=0, tiled=True)
    recv = recv.transpose(1, 0, 2)
    attn_out = recv[:, :, :HD].reshape(tok_rows, local_width)
    key_cache = recv[:, :, HD : 2 * HD].reshape(tok_rows, local_width)
    value_cache = recv[:, :, 2 * HD :].reshape(tok_rows, local_width)
    return attn_out, key_cache, value_cache


def solution(mesh):
    ctx_size = mesh.shape["ctx"]
    tp_size = mesh.shape["tp"]
    nz = 8
    split = Mesh(
        mesh.devices.reshape(nz, 2, 2, ctx_size // (nz * 4), tp_size // 2, 2),
        ("z", "yhi", "ylo", "xlo", "xhi", "core"),
    )
    rows = P(CTX, TP)
    placed = (rows, P(None, TP), P(None, TP), P(None, TP), P(TP), P(TP), P())
    return jax.shard_map(
        per_device,
        mesh=split,
        in_specs=placed,
        out_specs=(rows, rows, rows),
        check_vma=False,
    )
```

```python
import functools

import jax
import jax.numpy as jnp
from jax import lax
from jax.experimental import pallas as pl
from jax.experimental.pallas import tpu as pltpu
from jax.sharding import Mesh
from jax.sharding import PartitionSpec as P

HD = 128
KB = 256
CL = ("ylo", "xlo")
CTX = ("z", "yhi", "ylo", "xlo")
TP = ("xhi", "core")


def rotate(matrix, position):
    row_count, columns = matrix.shape
    head_count = columns // HD
    rot_half = HD // 2
    shaped = matrix.reshape(row_count, head_count, HD)
    inverse_freq = 500000.0 ** (-2.0 * jnp.arange(rot_half, dtype=jnp.float32) / HD)
    angles = position.astype(jnp.float32)[:, None] * inverse_freq[None, :]
    cosine = jnp.cos(angles)[:, None, :]
    sine_part = jnp.sin(angles)[:, None, :]
    first_part = shaped[..., :rot_half]
    second_part = shaped[..., rot_half:]
    turned = jnp.concatenate(
        [
            first_part * cosine - second_part * sine_part,
            second_part * cosine + first_part * sine_part,
        ],
        axis=-1,
    )
    return turned.reshape(row_count, columns).astype(jnp.bfloat16)


def request_start(token_ids, prompt_lengths):
    req_ends = jnp.cumsum(prompt_lengths)
    starts = req_ends - prompt_lengths
    request = jnp.sum((token_ids[:, None] >= req_ends[None, :]).astype(jnp.int32), axis=1)
    onehot = request[:, None] == jnp.arange(prompt_lengths.shape[0], dtype=jnp.int32)[None, :]
    return jnp.sum(jnp.where(onehot, starts[None, :], 0), axis=1)


def attn_kernel(info_ref, q_ref, kv_ref, qtok_ref, qlo_ref, o_ref):
    blk = pl.program_id(0)
    lo = info_ref[2 * blk]
    hi = info_ref[2 * blk + 1]
    shift = info_ref[4]
    groups = info_ref[5]
    nblocks = 2 * groups
    q = q_ref[...]
    qtok = qtok_ref[...]
    qlo = qlo_ref[...]
    rows = q.shape[0]
    scale = HD ** (-0.5)

    def body(kb, carry):
        peak, total, acc = carry
        upper = kb >= groups
        group = jnp.where(upper, nblocks - 1 - kb, kb)
        slot = (group - shift + groups) % groups
        start = pl.multiple_of((slot * 2 + upper.astype(jnp.int32)) * KB, KB)
        block = kv_ref[pl.ds(start, KB), :]
        keys = block[:, :HD]
        vals = block[:, HD:]
        scores = (
            lax.dot_general(q, keys, (((1,), (1,)), ((), ())), preferred_element_type=jnp.float32)
            * scale
        )
        ktok = kb * KB + lax.broadcasted_iota(jnp.int32, (1, KB), 1)
        visible = (ktok >= qlo) & (ktok <= qtok)
        masked = jnp.where(visible, scores, -1e30)
        new_peak = jnp.maximum(peak, jnp.max(masked, axis=1, keepdims=True))
        weights = jnp.where(visible, jnp.exp(masked - new_peak), 0.0)
        factor = jnp.exp(peak - new_peak)
        total = total * factor + jnp.sum(weights, axis=1, keepdims=True)
        acc = acc * factor + jnp.dot(
            weights.astype(jnp.bfloat16), vals, preferred_element_type=jnp.float32
        )
        return new_peak, total, acc

    start_state = (
        jnp.full((rows, 1), -1e30, jnp.float32),
        jnp.zeros((rows, 1), jnp.float32),
        jnp.zeros((rows, HD), jnp.float32),
    )
    _, total, acc = lax.fori_loop(lo, hi + 1, body, start_state)
    o_ref[...] = (acc / total).astype(o_ref.dtype)


def attention(info, q, kv, qtok, qlo):
    rows = q.shape[0]
    half = rows // 2
    return pl.pallas_call(
        attn_kernel,
        out_shape=jax.ShapeDtypeStruct((rows, HD), jnp.bfloat16),
        grid_spec=pltpu.PrefetchScalarGridSpec(
            num_scalar_prefetch=1,
            grid=(2,),
            in_specs=[
                pl.BlockSpec((half, HD), lambda i, info: (i, 0)),
                pl.BlockSpec(kv.shape, lambda i, info: (0, 0)),
                pl.BlockSpec((half, 1), lambda i, info: (i, 0)),
                pl.BlockSpec((half, 1), lambda i, info: (i, 0)),
            ],
            out_specs=pl.BlockSpec((half, HD), lambda i, info: (i, 0)),
        ),
    )(info, q, kv, qtok, qlo)


def z_ring(part, n):
    fwd = [part]
    bwd = [part]
    steps = n // 2
    for step in range(1, steps + 1):
        if step < steps:
            fwd.append(lax.ppermute(fwd[-1], "z", [(i, (i + 1) % n) for i in range(n)]))
            bwd.append(lax.ppermute(bwd[-1], "z", [(i, (i - 1) % n) for i in range(n)]))
        else:
            cut = part.shape[0] // 2
            far_a = lax.ppermute(fwd[-1][:cut], "z", [(i, (i + 1) % n) for i in range(n)])
            far_b = lax.ppermute(bwd[-1][cut:], "z", [(i, (i - 1) % n) for i in range(n)])
    ordered = bwd[: steps] + [far_a, far_b] + fwd[1:steps][::-1]
    return jnp.concatenate(ordered, axis=0)


def per_device(hidden_in, w_query, w_key, w_value, query_gain, key_gain, prompt_lengths):
    tok_rows = hidden_in.shape[0]
    half_rows = tok_rows // 2
    local_width = w_query.shape[1]
    head_count = local_width // HD
    nz = lax.axis_size("z")
    nyh = lax.axis_size("yhi")
    ncl = lax.axis_size("ylo") * lax.axis_size("xlo")
    z_idx = lax.axis_index("z")
    cg = z_idx * nyh + lax.axis_index("yhi")
    cl = lax.axis_index("ylo") * lax.axis_size("xlo") + lax.axis_index("xlo")
    groups = nz * nyh
    ctx_count = groups * ncl
    own = cg * ncl + cl

    xh = lax.axis_index("xhi")
    core = lax.axis_index("core")
    swap = [(0, 1), (1, 0)]
    width = hidden_in.shape[1]
    ncore = lax.axis_size("core")
    own_t = xh * ncore + core
    far_t = (1 - xh) * ncore + core
    across = lax.ppermute(hidden_in, "xhi", swap)
    pair = jnp.concatenate([hidden_in, across], axis=0)
    other = lax.ppermute(pair, "core", swap)

    def project(weight):
        rows_of = lambda t: lax.dynamic_slice_in_dim(weight, t * width, width, axis=0)
        total = jnp.dot(hidden_in, rows_of(own_t), preferred_element_type=jnp.float32)
        total = total + jnp.dot(across, rows_of(far_t), preferred_element_type=jnp.float32)
        total = total + jnp.dot(other[:tok_rows], rows_of(xh * ncore + 1 - core), preferred_element_type=jnp.float32)
        return total + jnp.dot(other[tok_rows:], rows_of((1 - xh) * ncore + 1 - core), preferred_element_type=jnp.float32)

    queries = project(w_query)
    keys_proj = project(w_key)
    values = project(w_value).astype(jnp.bfloat16)
    squares = jnp.stack([jnp.sum(queries * queries, axis=1), jnp.sum(keys_proj * keys_proj, axis=1)])
    squares = squares + lax.ppermute(squares, "xhi", swap)
    squares = squares + lax.ppermute(squares, "core", swap)
    query_sq = squares[0]
    key_sq = squares[1]
    full_width = local_width * lax.axis_size("xhi") * lax.axis_size("core")
    query_normed = queries * lax.rsqrt(query_sq[:, None] / full_width + 1e-06) * query_gain
    key_normed = keys_proj * lax.rsqrt(key_sq[:, None] / full_width + 1e-06) * key_gain
    local_rows = jnp.arange(tok_rows, dtype=jnp.int32)
    block_of = jnp.where(local_rows < half_rows, own, 2 * ctx_count - 1 - own)
    token_ids = block_of * half_rows + local_rows % half_rows
    position = token_ids - request_start(token_ids, prompt_lengths)
    query_rot = rotate(query_normed, position)
    key_rot = rotate(key_normed, position)

    packed = jnp.concatenate(
        [
            query_rot.reshape(tok_rows, head_count, HD),
            key_rot.reshape(tok_rows, head_count, HD),
            values.reshape(tok_rows, head_count, HD),
        ],
        axis=2,
    )
    got = lax.all_to_all(packed, CL, split_axis=1, concat_axis=0, tiled=True)
    got = got.reshape(ncl, tok_rows, 3 * HD)
    lower = got[:, :half_rows].reshape(ncl * half_rows, 3 * HD)
    upper = got[::-1, half_rows:].reshape(ncl * half_rows, 3 * HD)
    mine = jnp.concatenate([lower, upper], axis=0)
    q_head = mine[:, :HD]
    kv_mine = mine[:, HD:]

    yh = lax.axis_index("yhi")
    kv_other = lax.ppermute(kv_mine, "yhi", swap)
    kv_pair = jnp.where(yh == 0, jnp.concatenate([kv_mine, kv_other], axis=0), jnp.concatenate([kv_other, kv_mine], axis=0))
    kv_all = z_ring(kv_pair, nz)

    span = ncl * half_rows
    total_tokens = 2 * ctx_count * half_rows
    r = jnp.arange(span, dtype=jnp.int32)
    q_tokens = jnp.concatenate([cg * span + r, total_tokens - (cg + 1) * span + r])
    q_lo = request_start(q_tokens, prompt_lengths)
    info = jnp.stack(
        [
            q_lo[0] // KB,
            cg,
            q_lo[span] // KB,
            2 * groups - 1 - cg,
            (z_idx * nyh) % groups,
            jnp.asarray(groups, jnp.int32),
        ]
    ).astype(jnp.int32)
    out_head = attention(info, q_head, kv_all, q_tokens[:, None], q_lo[:, None])

    out_lower = out_head[:span].reshape(ncl, half_rows, HD)
    out_upper = out_head[span:].reshape(ncl, half_rows, HD)[::-1]
    out_send = jnp.stack([out_lower, out_upper], axis=1).reshape(ncl, tok_rows, HD)

    picked = kv_all.reshape(groups, 2, ncl, half_rows, 2 * HD)
    picked = lax.dynamic_slice_in_dim(picked, cg * ncl, ncl, axis=3)
    doubled = jnp.concatenate([picked, picked], axis=0)
    natural = lax.dynamic_slice_in_dim(doubled, (groups - (z_idx * nyh) % groups) % groups, groups, axis=0)
    cache_lower = natural[:, 0].reshape(groups * ncl, ncl, 2 * HD)
    cache_upper = natural[::-1, 1].reshape(groups * ncl, ncl, 2 * HD)
    cache = jnp.concatenate([cache_lower, cache_upper], axis=0).transpose(1, 0, 2)
    send = jnp.concatenate([out_send, cache], axis=2)
    recv = lax.all_to_all(send, CL, split_axis=0, concat_axis=0, tiled=True)
    recv = recv.transpose(1, 0, 2)
    attn_out = recv[:, :, :HD].reshape(tok_rows, local_width)
    key_cache = recv[:, :, HD : 2 * HD].reshape(tok_rows, local_width)
    value_cache = recv[:, :, 2 * HD :].reshape(tok_rows, local_width)
    return attn_out, key_cache, value_cache


def solution(mesh):
    ctx_size = mesh.shape["ctx"]
    tp_size = mesh.shape["tp"]
    nz = 8
    split = Mesh(
        mesh.devices.reshape(nz, 2, 2, ctx_size // (nz * 4), tp_size // 2, 2),
        ("z", "yhi", "ylo", "xlo", "xhi", "core"),
    )
    rows = P(CTX, TP)
    placed = (rows, P(None, TP), P(None, TP), P(None, TP), P(TP), P(TP), P())
    return jax.shard_map(
        per_device,
        mesh=split,
        in_specs=placed,
        out_specs=(rows, rows, rows),
        check_vma=False,
    )
```

```python
import functools

import jax
import jax.numpy as jnp
from jax import lax
from jax.experimental import pallas as pl
from jax.experimental.pallas import tpu as pltpu
from jax.sharding import Mesh
from jax.sharding import PartitionSpec as P

HD = 128
KB = 256
CL = ("ylo", "xlo")
CTX = ("z", "yhi", "ylo", "xlo")
TP = ("xhi", "core")


def rotate(matrix, position):
    row_count, columns = matrix.shape
    head_count = columns // HD
    rot_half = HD // 2
    shaped = matrix.reshape(row_count, head_count, HD)
    inverse_freq = 500000.0 ** (-2.0 * jnp.arange(rot_half, dtype=jnp.float32) / HD)
    angles = position.astype(jnp.float32)[:, None] * inverse_freq[None, :]
    cosine = jnp.cos(angles)[:, None, :]
    sine_part = jnp.sin(angles)[:, None, :]
    first_part = shaped[..., :rot_half]
    second_part = shaped[..., rot_half:]
    turned = jnp.concatenate(
        [
            first_part * cosine - second_part * sine_part,
            second_part * cosine + first_part * sine_part,
        ],
        axis=-1,
    )
    return turned.reshape(row_count, columns).astype(jnp.bfloat16)


def request_start(token_ids, prompt_lengths):
    req_ends = jnp.cumsum(prompt_lengths)
    starts = req_ends - prompt_lengths
    request = jnp.sum((token_ids[:, None] >= req_ends[None, :]).astype(jnp.int32), axis=1)
    onehot = request[:, None] == jnp.arange(prompt_lengths.shape[0], dtype=jnp.int32)[None, :]
    return jnp.sum(jnp.where(onehot, starts[None, :], 0), axis=1)


def attn_kernel(info_ref, q_ref, kv_ref, qtok_ref, qlo_ref, o_ref, buf, sem):
    blk = pl.program_id(0)
    lo = info_ref[2 * blk]
    hi = info_ref[2 * blk + 1]
    shift = info_ref[4]
    groups = info_ref[5]
    nblocks = 2 * groups
    q = q_ref[...]
    qtok = qtok_ref[...]
    qlo = qlo_ref[...]
    rows = q.shape[0]
    scale = HD ** (-0.5)

    def fetch(kb, slot):
        upper = kb >= groups
        group = jnp.where(upper, nblocks - 1 - kb, kb)
        place = (group - shift + groups) % groups
        start = pl.multiple_of((place * 2 + upper.astype(jnp.int32)) * KB, KB)
        return pltpu.make_async_copy(kv_ref.at[pl.ds(start, KB)], buf.at[slot], sem.at[slot])

    fetch(lo, 0).start()

    def body(kb, carry):
        peak, total, acc = carry
        slot = (kb - lo) % 2

        @pl.when(kb < hi)
        def _():
            fetch(kb + 1, 1 - slot).start()

        fetch(kb, slot).wait()
        block = buf[slot]
        keys = block[:, :HD]
        vals = block[:, HD:]
        scores = (
            lax.dot_general(q, keys, (((1,), (1,)), ((), ())), preferred_element_type=jnp.float32)
            * scale
        )
        ktok = kb * KB + lax.broadcasted_iota(jnp.int32, (1, KB), 1)
        visible = (ktok >= qlo) & (ktok <= qtok)
        masked = jnp.where(visible, scores, -1e30)
        new_peak = jnp.maximum(peak, jnp.max(masked, axis=1, keepdims=True))
        weights = jnp.where(visible, jnp.exp(masked - new_peak), 0.0)
        factor = jnp.exp(peak - new_peak)
        total = total * factor + jnp.sum(weights, axis=1, keepdims=True)
        acc = acc * factor + jnp.dot(
            weights.astype(jnp.bfloat16), vals, preferred_element_type=jnp.float32
        )
        return new_peak, total, acc

    start_state = (
        jnp.full((rows, 1), -1e30, jnp.float32),
        jnp.zeros((rows, 1), jnp.float32),
        jnp.zeros((rows, HD), jnp.float32),
    )
    _, total, acc = lax.fori_loop(lo, hi + 1, body, start_state)
    o_ref[...] = (acc / total).astype(o_ref.dtype)


def attention(info, q, kv, qtok, qlo):
    rows = q.shape[0]
    half = rows // 2
    return pl.pallas_call(
        attn_kernel,
        out_shape=jax.ShapeDtypeStruct((rows, HD), jnp.bfloat16),
        grid_spec=pltpu.PrefetchScalarGridSpec(
            num_scalar_prefetch=1,
            grid=(2,),
            in_specs=[
                pl.BlockSpec((half, HD), lambda i, info: (i, 0)),
                pl.BlockSpec(memory_space=pl.ANY),
                pl.BlockSpec((half, 1), lambda i, info: (i, 0)),
                pl.BlockSpec((half, 1), lambda i, info: (i, 0)),
            ],
            out_specs=pl.BlockSpec((half, HD), lambda i, info: (i, 0)),
            scratch_shapes=[pltpu.VMEM((2, KB, kv.shape[1]), kv.dtype), pltpu.SemaphoreType.DMA((2,))],
        ),
    )(info, q, kv, qtok, qlo)


def z_ring(part, n):
    fwd = [part]
    bwd = [part]
    steps = n // 2
    for step in range(1, steps + 1):
        if step < steps:
            fwd.append(lax.ppermute(fwd[-1], "z", [(i, (i + 1) % n) for i in range(n)]))
            bwd.append(lax.ppermute(bwd[-1], "z", [(i, (i - 1) % n) for i in range(n)]))
        else:
            cut = part.shape[0] // 2
            far_a = lax.ppermute(fwd[-1][:cut], "z", [(i, (i + 1) % n) for i in range(n)])
            far_b = lax.ppermute(bwd[-1][cut:], "z", [(i, (i - 1) % n) for i in range(n)])
    ordered = bwd[: steps] + [far_a, far_b] + fwd[1:steps][::-1]
    return jnp.concatenate(ordered, axis=0)


def per_device(hidden_in, w_query, w_key, w_value, query_gain, key_gain, prompt_lengths):
    tok_rows = hidden_in.shape[0]
    half_rows = tok_rows // 2
    local_width = w_query.shape[1]
    head_count = local_width // HD
    nz = lax.axis_size("z")
    nyh = lax.axis_size("yhi")
    ncl = lax.axis_size("ylo") * lax.axis_size("xlo")
    z_idx = lax.axis_index("z")
    cg = z_idx * nyh + lax.axis_index("yhi")
    cl = lax.axis_index("ylo") * lax.axis_size("xlo") + lax.axis_index("xlo")
    groups = nz * nyh
    ctx_count = groups * ncl
    own = cg * ncl + cl

    xh = lax.axis_index("xhi")
    core = lax.axis_index("core")
    swap = [(0, 1), (1, 0)]
    across = lax.ppermute(hidden_in, "xhi", swap)
    pair = jnp.where(xh == 0, jnp.concatenate([hidden_in, across], axis=1), jnp.concatenate([across, hidden_in], axis=1))
    other = lax.ppermute(pair, "core", swap)
    width = hidden_in.shape[1]
    mine_first = jnp.concatenate([pair[:, :width], other[:, :width], pair[:, width:], other[:, width:]], axis=1)
    theirs_first = jnp.concatenate([other[:, :width], pair[:, :width], other[:, width:], pair[:, width:]], axis=1)
    pieces = jnp.where(core == 0, mine_first, theirs_first)
    queries = jnp.dot(pieces, w_query, preferred_element_type=jnp.float32)
    keys_proj = jnp.dot(pieces, w_key, preferred_element_type=jnp.float32)
    values = jnp.dot(pieces, w_value, preferred_element_type=jnp.float32).astype(jnp.bfloat16)
    squares = jnp.stack([jnp.sum(queries * queries, axis=1), jnp.sum(keys_proj * keys_proj, axis=1)])
    squares = squares + lax.ppermute(squares, "xhi", swap)
    squares = squares + lax.ppermute(squares, "core", swap)
    query_sq = squares[0]
    key_sq = squares[1]
    full_width = local_width * lax.axis_size("xhi") * lax.axis_size("core")
    query_normed = queries * lax.rsqrt(query_sq[:, None] / full_width + 1e-06) * query_gain
    key_normed = keys_proj * lax.rsqrt(key_sq[:, None] / full_width + 1e-06) * key_gain
    local_rows = jnp.arange(tok_rows, dtype=jnp.int32)
    block_of = jnp.where(local_rows < half_rows, own, 2 * ctx_count - 1 - own)
    token_ids = block_of * half_rows + local_rows % half_rows
    position = token_ids - request_start(token_ids, prompt_lengths)
    query_rot = rotate(query_normed, position)
    key_rot = rotate(key_normed, position)

    packed = jnp.concatenate(
        [
            query_rot.reshape(tok_rows, head_count, HD),
            key_rot.reshape(tok_rows, head_count, HD),
            values.reshape(tok_rows, head_count, HD),
        ],
        axis=2,
    )
    got = lax.all_to_all(packed, CL, split_axis=1, concat_axis=0, tiled=True)
    got = got.reshape(ncl, tok_rows, 3 * HD)
    lower = got[:, :half_rows].reshape(ncl * half_rows, 3 * HD)
    upper = got[::-1, half_rows:].reshape(ncl * half_rows, 3 * HD)
    mine = jnp.concatenate([lower, upper], axis=0)
    q_head = mine[:, :HD]
    kv_mine = mine[:, HD:]

    yh = lax.axis_index("yhi")
    kv_other = lax.ppermute(kv_mine, "yhi", swap)
    kv_pair = jnp.where(yh == 0, jnp.concatenate([kv_mine, kv_other], axis=0), jnp.concatenate([kv_other, kv_mine], axis=0))
    kv_all = z_ring(kv_pair, nz)

    span = ncl * half_rows
    total_tokens = 2 * ctx_count * half_rows
    r = jnp.arange(span, dtype=jnp.int32)
    q_tokens = jnp.concatenate([cg * span + r, total_tokens - (cg + 1) * span + r])
    q_lo = request_start(q_tokens, prompt_lengths)
    info = jnp.stack(
        [
            q_lo[0] // KB,
            cg,
            q_lo[span] // KB,
            2 * groups - 1 - cg,
            (z_idx * nyh) % groups,
            jnp.asarray(groups, jnp.int32),
        ]
    ).astype(jnp.int32)
    out_head = attention(info, q_head, kv_all, q_tokens[:, None], q_lo[:, None])

    out_lower = out_head[:span].reshape(ncl, half_rows, HD)
    out_upper = out_head[span:].reshape(ncl, half_rows, HD)[::-1]
    out_send = jnp.stack([out_lower, out_upper], axis=1).reshape(ncl, tok_rows, HD)

    picked = kv_all.reshape(groups, 2, ncl, half_rows, 2 * HD)
    picked = lax.dynamic_slice_in_dim(picked, cg * ncl, ncl, axis=3)
    doubled = jnp.concatenate([picked, picked], axis=0)
    natural = lax.dynamic_slice_in_dim(doubled, (groups - (z_idx * nyh) % groups) % groups, groups, axis=0)
    cache_lower = natural[:, 0].reshape(groups * ncl, ncl, 2 * HD)
    cache_upper = natural[::-1, 1].reshape(groups * ncl, ncl, 2 * HD)
    cache = jnp.concatenate([cache_lower, cache_upper], axis=0).transpose(1, 0, 2)
    send = jnp.concatenate([out_send, cache], axis=2)
    recv = lax.all_to_all(send, CL, split_axis=0, concat_axis=0, tiled=True)
    recv = recv.transpose(1, 0, 2)
    attn_out = recv[:, :, :HD].reshape(tok_rows, local_width)
    key_cache = recv[:, :, HD : 2 * HD].reshape(tok_rows, local_width)
    value_cache = recv[:, :, 2 * HD :].reshape(tok_rows, local_width)
    return attn_out, key_cache, value_cache


def solution(mesh):
    ctx_size = mesh.shape["ctx"]
    tp_size = mesh.shape["tp"]
    nz = 8
    split = Mesh(
        mesh.devices.reshape(nz, 2, 2, ctx_size // (nz * 4), tp_size // 2, 2),
        ("z", "yhi", "ylo", "xlo", "xhi", "core"),
    )
    rows = P(CTX, TP)
    placed = (rows, P(None, TP), P(None, TP), P(None, TP), P(TP), P(TP), P())
    return jax.shard_map(
        per_device,
        mesh=split,
        in_specs=placed,
        out_specs=(rows, rows, rows),
        check_vma=False,
    )
```

```python
import functools

import jax
import jax.numpy as jnp
from jax import lax
from jax.experimental import pallas as pl
from jax.experimental.pallas import tpu as pltpu
from jax.sharding import Mesh
from jax.sharding import PartitionSpec as P

HD = 128
KB = 256
CL = ("ylo", "xlo")
CTX = ("z", "yhi", "ylo", "xlo")
TP = ("xhi", "core")


def rotate(matrix, position):
    row_count, columns = matrix.shape
    head_count = columns // HD
    rot_half = HD // 2
    shaped = matrix.reshape(row_count, head_count, HD)
    inverse_freq = 500000.0 ** (-2.0 * jnp.arange(rot_half, dtype=jnp.float32) / HD)
    angles = position.astype(jnp.float32)[:, None] * inverse_freq[None, :]
    cosine = jnp.cos(angles)[:, None, :]
    sine_part = jnp.sin(angles)[:, None, :]
    first_part = shaped[..., :rot_half]
    second_part = shaped[..., rot_half:]
    turned = jnp.concatenate(
        [
            first_part * cosine - second_part * sine_part,
            second_part * cosine + first_part * sine_part,
        ],
        axis=-1,
    )
    return turned.reshape(row_count, columns).astype(jnp.bfloat16)


def request_start(token_ids, prompt_lengths):
    req_ends = jnp.cumsum(prompt_lengths)
    starts = req_ends - prompt_lengths
    request = jnp.sum((token_ids[:, None] >= req_ends[None, :]).astype(jnp.int32), axis=1)
    onehot = request[:, None] == jnp.arange(prompt_lengths.shape[0], dtype=jnp.int32)[None, :]
    return jnp.sum(jnp.where(onehot, starts[None, :], 0), axis=1)


def attn_kernel(info_ref, q_ref, kv_ref, qtok_ref, qlo_ref, o_ref):
    blk = pl.program_id(0)
    lo = info_ref[2 * blk]
    hi = info_ref[2 * blk + 1]
    shift = info_ref[4]
    groups = info_ref[5]
    flip = info_ref[6]
    nblocks = 2 * groups
    q = q_ref[...]
    qtok = qtok_ref[...]
    qlo = qlo_ref[...]
    rows = q.shape[0]
    scale = HD ** (-0.5)

    def body(kb, carry):
        peak, total, acc = carry
        upper = kb >= groups
        group = jnp.where(upper, nblocks - 1 - kb, kb)
        place = (group - shift + groups) % groups
        slot = (place // 2) * 2 + (place % 2 + flip) % 2
        start = pl.multiple_of((slot * 2 + upper.astype(jnp.int32)) * KB, KB)
        block = kv_ref[pl.ds(start, KB), :]
        keys = block[:, :HD]
        vals = block[:, HD:]
        scores = (
            lax.dot_general(q, keys, (((1,), (1,)), ((), ())), preferred_element_type=jnp.float32)
            * scale
        )
        ktok = kb * KB + lax.broadcasted_iota(jnp.int32, (1, KB), 1)
        visible = (ktok >= qlo) & (ktok <= qtok)
        masked = jnp.where(visible, scores, -1e30)
        new_peak = jnp.maximum(peak, jnp.max(masked, axis=1, keepdims=True))
        weights = jnp.where(visible, jnp.exp(masked - new_peak), 0.0)
        factor = jnp.exp(peak - new_peak)
        total = total * factor + jnp.sum(weights, axis=1, keepdims=True)
        acc = acc * factor + jnp.dot(
            weights.astype(jnp.bfloat16), vals, preferred_element_type=jnp.float32
        )
        return new_peak, total, acc

    start_state = (
        jnp.full((rows, 1), -1e30, jnp.float32),
        jnp.zeros((rows, 1), jnp.float32),
        jnp.zeros((rows, HD), jnp.float32),
    )
    _, total, acc = lax.fori_loop(lo, hi + 1, body, start_state)
    o_ref[...] = (acc / total).astype(o_ref.dtype)


def attention(info, q, kv, qtok, qlo):
    rows = q.shape[0]
    half = rows // 2
    return pl.pallas_call(
        attn_kernel,
        out_shape=jax.ShapeDtypeStruct((rows, HD), jnp.bfloat16),
        grid_spec=pltpu.PrefetchScalarGridSpec(
            num_scalar_prefetch=1,
            grid=(2,),
            in_specs=[
                pl.BlockSpec((half, HD), lambda i, info: (i, 0)),
                pl.BlockSpec(kv.shape, lambda i, info: (0, 0)),
                pl.BlockSpec((half, 1), lambda i, info: (i, 0)),
                pl.BlockSpec((half, 1), lambda i, info: (i, 0)),
            ],
            out_specs=pl.BlockSpec((half, HD), lambda i, info: (i, 0)),
        ),
    )(info, q, kv, qtok, qlo)


def z_ring(part, n):
    fwd = [part]
    bwd = [part]
    steps = n // 2
    for step in range(1, steps + 1):
        if step < steps:
            fwd.append(lax.ppermute(fwd[-1], "z", [(i, (i + 1) % n) for i in range(n)]))
            bwd.append(lax.ppermute(bwd[-1], "z", [(i, (i - 1) % n) for i in range(n)]))
        else:
            cut = part.shape[0] // 2
            far_a = lax.ppermute(fwd[-1][:cut], "z", [(i, (i + 1) % n) for i in range(n)])
            far_b = lax.ppermute(bwd[-1][cut:], "z", [(i, (i - 1) % n) for i in range(n)])
    ordered = bwd[: steps] + [far_a, far_b] + fwd[1:steps][::-1]
    return jnp.concatenate(ordered, axis=0)


def per_device(hidden_in, w_query, w_key, w_value, query_gain, key_gain, prompt_lengths):
    tok_rows = hidden_in.shape[0]
    half_rows = tok_rows // 2
    local_width = w_query.shape[1]
    head_count = local_width // HD
    nz = lax.axis_size("z")
    nyh = lax.axis_size("yhi")
    ncl = lax.axis_size("ylo") * lax.axis_size("xlo")
    z_idx = lax.axis_index("z")
    cg = z_idx * nyh + lax.axis_index("yhi")
    cl = lax.axis_index("ylo") * lax.axis_size("xlo") + lax.axis_index("xlo")
    groups = nz * nyh
    ctx_count = groups * ncl
    own = cg * ncl + cl

    xh = lax.axis_index("xhi")
    core = lax.axis_index("core")
    swap = [(0, 1), (1, 0)]
    across = lax.ppermute(hidden_in, "xhi", swap)
    pair = jnp.where(xh == 0, jnp.concatenate([hidden_in, across], axis=1), jnp.concatenate([across, hidden_in], axis=1))
    other = lax.ppermute(pair, "core", swap)
    width = hidden_in.shape[1]
    mine_first = jnp.concatenate([pair[:, :width], other[:, :width], pair[:, width:], other[:, width:]], axis=1)
    theirs_first = jnp.concatenate([other[:, :width], pair[:, :width], other[:, width:], pair[:, width:]], axis=1)
    pieces = jnp.where(core == 0, mine_first, theirs_first)
    queries = jnp.dot(pieces, w_query, preferred_element_type=jnp.float32)
    keys_proj = jnp.dot(pieces, w_key, preferred_element_type=jnp.float32)
    values = jnp.dot(pieces, w_value, preferred_element_type=jnp.float32).astype(jnp.bfloat16)
    squares = jnp.stack([jnp.sum(queries * queries, axis=1), jnp.sum(keys_proj * keys_proj, axis=1)])
    squares = squares + lax.ppermute(squares, "xhi", swap)
    squares = squares + lax.ppermute(squares, "core", swap)
    query_sq = squares[0]
    key_sq = squares[1]
    full_width = local_width * lax.axis_size("xhi") * lax.axis_size("core")
    query_normed = queries * lax.rsqrt(query_sq[:, None] / full_width + 1e-06) * query_gain
    key_normed = keys_proj * lax.rsqrt(key_sq[:, None] / full_width + 1e-06) * key_gain
    local_rows = jnp.arange(tok_rows, dtype=jnp.int32)
    block_of = jnp.where(local_rows < half_rows, own, 2 * ctx_count - 1 - own)
    token_ids = block_of * half_rows + local_rows % half_rows
    position = token_ids - request_start(token_ids, prompt_lengths)
    query_rot = rotate(query_normed, position)
    key_rot = rotate(key_normed, position)

    packed = jnp.concatenate(
        [
            query_rot.reshape(tok_rows, head_count, HD),
            key_rot.reshape(tok_rows, head_count, HD),
            values.reshape(tok_rows, head_count, HD),
        ],
        axis=2,
    )
    got = lax.all_to_all(packed, CL, split_axis=1, concat_axis=0, tiled=True)
    got = got.reshape(ncl, tok_rows, 3 * HD)
    lower = got[:, :half_rows].reshape(ncl * half_rows, 3 * HD)
    upper = got[::-1, half_rows:].reshape(ncl * half_rows, 3 * HD)
    mine = jnp.concatenate([lower, upper], axis=0)
    q_head = mine[:, :HD]
    kv_mine = mine[:, HD:]

    yh = lax.axis_index("yhi")
    kv_other = lax.ppermute(kv_mine, "yhi", swap)
    kv_pair = jnp.concatenate([kv_mine, kv_other], axis=0)
    kv_all = z_ring(kv_pair, nz)

    span = ncl * half_rows
    total_tokens = 2 * ctx_count * half_rows
    r = jnp.arange(span, dtype=jnp.int32)
    q_tokens = jnp.concatenate([cg * span + r, total_tokens - (cg + 1) * span + r])
    q_lo = request_start(q_tokens, prompt_lengths)
    info = jnp.stack(
        [
            q_lo[0] // KB,
            cg,
            q_lo[span] // KB,
            2 * groups - 1 - cg,
            (z_idx * nyh) % groups,
            jnp.asarray(groups, jnp.int32),
            yh,
        ]
    ).astype(jnp.int32)
    out_head = attention(info, q_head, kv_all, q_tokens[:, None], q_lo[:, None])

    out_lower = out_head[:span].reshape(ncl, half_rows, HD)
    out_upper = out_head[span:].reshape(ncl, half_rows, HD)[::-1]
    out_send = jnp.stack([out_lower, out_upper], axis=1).reshape(ncl, tok_rows, HD)

    picked = kv_all.reshape(groups, 2, ncl, half_rows, 2 * HD)
    picked = lax.dynamic_slice_in_dim(picked, cg * ncl, ncl, axis=3)
    paired = picked.reshape(nz, nyh, 2, ncl, ncl, 2 * HD)
    picked = jnp.where(yh == 0, paired, paired[:, ::-1]).reshape(groups, 2, ncl, ncl, 2 * HD)
    doubled = jnp.concatenate([picked, picked], axis=0)
    natural = lax.dynamic_slice_in_dim(doubled, (groups - (z_idx * nyh) % groups) % groups, groups, axis=0)
    cache_lower = natural[:, 0].reshape(groups * ncl, ncl, 2 * HD)
    cache_upper = natural[::-1, 1].reshape(groups * ncl, ncl, 2 * HD)
    cache = jnp.concatenate([cache_lower, cache_upper], axis=0).transpose(1, 0, 2)
    send = jnp.concatenate([out_send, cache], axis=2)
    recv = lax.all_to_all(send, CL, split_axis=0, concat_axis=0, tiled=True)
    recv = recv.transpose(1, 0, 2)
    attn_out = recv[:, :, :HD].reshape(tok_rows, local_width)
    key_cache = recv[:, :, HD : 2 * HD].reshape(tok_rows, local_width)
    value_cache = recv[:, :, 2 * HD :].reshape(tok_rows, local_width)
    return attn_out, key_cache, value_cache


def solution(mesh):
    ctx_size = mesh.shape["ctx"]
    tp_size = mesh.shape["tp"]
    nz = 8
    split = Mesh(
        mesh.devices.reshape(nz, 2, 2, ctx_size // (nz * 4), tp_size // 2, 2),
        ("z", "yhi", "ylo", "xlo", "xhi", "core"),
    )
    rows = P(CTX, TP)
    placed = (rows, P(None, TP), P(None, TP), P(None, TP), P(TP), P(TP), P())
    return jax.shard_map(
        per_device,
        mesh=split,
        in_specs=placed,
        out_specs=(rows, rows, rows),
        check_vma=False,
    )
```

```python
import functools

import jax
import jax.numpy as jnp
from jax import lax
from jax.experimental import pallas as pl
from jax.experimental.pallas import tpu as pltpu
from jax.sharding import Mesh
from jax.sharding import PartitionSpec as P

HD = 128
KB = 256
CL = ("ylo", "xlo")
CTX = ("z", "yhi", "ylo", "xlo")
TP = ("xhi", "core")


def rotate(matrix, position):
    row_count, columns = matrix.shape
    head_count = columns // HD
    rot_half = HD // 2
    shaped = matrix.reshape(row_count, head_count, HD)
    inverse_freq = 500000.0 ** (-2.0 * jnp.arange(rot_half, dtype=jnp.float32) / HD)
    angles = position.astype(jnp.float32)[:, None] * inverse_freq[None, :]
    cosine = jnp.cos(angles)[:, None, :]
    sine_part = jnp.sin(angles)[:, None, :]
    first_part = shaped[..., :rot_half]
    second_part = shaped[..., rot_half:]
    turned = jnp.concatenate(
        [
            first_part * cosine - second_part * sine_part,
            second_part * cosine + first_part * sine_part,
        ],
        axis=-1,
    )
    return turned.reshape(row_count, columns).astype(jnp.bfloat16)


def request_start(token_ids, prompt_lengths):
    req_ends = jnp.cumsum(prompt_lengths)
    starts = req_ends - prompt_lengths
    request = jnp.sum((token_ids[:, None] >= req_ends[None, :]).astype(jnp.int32), axis=1)
    onehot = request[:, None] == jnp.arange(prompt_lengths.shape[0], dtype=jnp.int32)[None, :]
    return jnp.sum(jnp.where(onehot, starts[None, :], 0), axis=1)


def attn_kernel(info_ref, q_ref, kv_ref, qtok_ref, qlo_ref, o_ref, buf, sem):
    blk = pl.program_id(0)
    lo = info_ref[2 * blk]
    hi = info_ref[2 * blk + 1]
    shift = info_ref[4]
    groups = info_ref[5]
    flip = info_ref[6]
    nblocks = 2 * groups
    q = q_ref[...]
    qtok = qtok_ref[...]
    qlo = qlo_ref[...]
    rows = q.shape[0]
    scale = HD ** (-0.5)

    def fetch(kb, slot):
        upper = kb >= groups
        group = jnp.where(upper, nblocks - 1 - kb, kb)
        place = (group - shift + groups) % groups
        place = (place // 2) * 2 + (place % 2 + flip) % 2
        start = pl.multiple_of((place * 2 + upper.astype(jnp.int32)) * KB, KB)
        return pltpu.make_async_copy(kv_ref.at[pl.ds(start, KB)], buf.at[slot], sem.at[slot])

    fetch(lo, 0).start()

    def body(kb, carry):
        peak, total, acc = carry
        slot = (kb - lo) % 2

        @pl.when(kb < hi)
        def _():
            fetch(kb + 1, 1 - slot).start()

        fetch(kb, slot).wait()
        block = buf[slot]
        keys = block[:, :HD]
        vals = block[:, HD:]
        scores = (
            lax.dot_general(q, keys, (((1,), (1,)), ((), ())), preferred_element_type=jnp.float32)
            * scale
        )
        ktok = kb * KB + lax.broadcasted_iota(jnp.int32, (1, KB), 1)
        visible = (ktok >= qlo) & (ktok <= qtok)
        masked = jnp.where(visible, scores, -1e30)
        new_peak = jnp.maximum(peak, jnp.max(masked, axis=1, keepdims=True))
        weights = jnp.where(visible, jnp.exp(masked - new_peak), 0.0)
        factor = jnp.exp(peak - new_peak)
        total = total * factor + jnp.sum(weights, axis=1, keepdims=True)
        acc = acc * factor + jnp.dot(
            weights.astype(jnp.bfloat16), vals, preferred_element_type=jnp.float32
        )
        return new_peak, total, acc

    start_state = (
        jnp.full((rows, 1), -1e30, jnp.float32),
        jnp.zeros((rows, 1), jnp.float32),
        jnp.zeros((rows, HD), jnp.float32),
    )
    _, total, acc = lax.fori_loop(lo, hi + 1, body, start_state)
    o_ref[...] = (acc / total).astype(o_ref.dtype)


def attention(info, q, kv, qtok, qlo):
    rows = q.shape[0]
    half = rows // 2
    return pl.pallas_call(
        attn_kernel,
        out_shape=jax.ShapeDtypeStruct((rows, HD), jnp.bfloat16),
        grid_spec=pltpu.PrefetchScalarGridSpec(
            num_scalar_prefetch=1,
            grid=(2,),
            in_specs=[
                pl.BlockSpec((half, HD), lambda i, info: (i, 0)),
                pl.BlockSpec(memory_space=pl.ANY),
                pl.BlockSpec((half, 1), lambda i, info: (i, 0)),
                pl.BlockSpec((half, 1), lambda i, info: (i, 0)),
            ],
            out_specs=pl.BlockSpec((half, HD), lambda i, info: (i, 0)),
            scratch_shapes=[pltpu.VMEM((2, KB, kv.shape[1]), kv.dtype), pltpu.SemaphoreType.DMA((2,))],
        ),
    )(info, q, kv, qtok, qlo)


def z_ring(part, n):
    fwd = [part]
    bwd = [part]
    steps = n // 2
    for step in range(1, steps + 1):
        if step < steps:
            fwd.append(lax.ppermute(fwd[-1], "z", [(i, (i + 1) % n) for i in range(n)]))
            bwd.append(lax.ppermute(bwd[-1], "z", [(i, (i - 1) % n) for i in range(n)]))
        else:
            cut = part.shape[0] // 2
            far_a = lax.ppermute(fwd[-1][:cut], "z", [(i, (i + 1) % n) for i in range(n)])
            far_b = lax.ppermute(bwd[-1][cut:], "z", [(i, (i - 1) % n) for i in range(n)])
    ordered = bwd[: steps] + [far_a, far_b] + fwd[1:steps][::-1]
    return jnp.concatenate(ordered, axis=0)


def per_device(hidden_in, w_query, w_key, w_value, query_gain, key_gain, prompt_lengths):
    tok_rows = hidden_in.shape[0]
    half_rows = tok_rows // 2
    local_width = w_query.shape[1]
    head_count = local_width // HD
    nz = lax.axis_size("z")
    nyh = lax.axis_size("yhi")
    ncl = lax.axis_size("ylo") * lax.axis_size("xlo")
    z_idx = lax.axis_index("z")
    cg = z_idx * nyh + lax.axis_index("yhi")
    cl = lax.axis_index("ylo") * lax.axis_size("xlo") + lax.axis_index("xlo")
    groups = nz * nyh
    ctx_count = groups * ncl
    own = cg * ncl + cl

    xh = lax.axis_index("xhi")
    core = lax.axis_index("core")
    swap = [(0, 1), (1, 0)]
    across = lax.ppermute(hidden_in, "xhi", swap)
    pair = jnp.where(xh == 0, jnp.concatenate([hidden_in, across], axis=1), jnp.concatenate([across, hidden_in], axis=1))
    other = lax.ppermute(pair, "core", swap)
    width = hidden_in.shape[1]
    mine_first = jnp.concatenate([pair[:, :width], other[:, :width], pair[:, width:], other[:, width:]], axis=1)
    theirs_first = jnp.concatenate([other[:, :width], pair[:, :width], other[:, width:], pair[:, width:]], axis=1)
    pieces = jnp.where(core == 0, mine_first, theirs_first)
    queries = jnp.dot(pieces, w_query, preferred_element_type=jnp.float32)
    keys_proj = jnp.dot(pieces, w_key, preferred_element_type=jnp.float32)
    values = jnp.dot(pieces, w_value, preferred_element_type=jnp.float32).astype(jnp.bfloat16)
    squares = jnp.stack([jnp.sum(queries * queries, axis=1), jnp.sum(keys_proj * keys_proj, axis=1)])
    squares = squares + lax.ppermute(squares, "xhi", swap)
    squares = squares + lax.ppermute(squares, "core", swap)
    query_sq = squares[0]
    key_sq = squares[1]
    full_width = local_width * lax.axis_size("xhi") * lax.axis_size("core")
    query_normed = queries * lax.rsqrt(query_sq[:, None] / full_width + 1e-06) * query_gain
    key_normed = keys_proj * lax.rsqrt(key_sq[:, None] / full_width + 1e-06) * key_gain
    local_rows = jnp.arange(tok_rows, dtype=jnp.int32)
    block_of = jnp.where(local_rows < half_rows, own, 2 * ctx_count - 1 - own)
    token_ids = block_of * half_rows + local_rows % half_rows
    position = token_ids - request_start(token_ids, prompt_lengths)
    query_rot = rotate(query_normed, position)
    key_rot = rotate(key_normed, position)

    packed = jnp.concatenate(
        [
            query_rot.reshape(tok_rows, head_count, HD),
            key_rot.reshape(tok_rows, head_count, HD),
            values.reshape(tok_rows, head_count, HD),
        ],
        axis=2,
    )
    got = lax.all_to_all(packed, CL, split_axis=1, concat_axis=0, tiled=True)
    got = got.reshape(ncl, tok_rows, 3 * HD)
    lower = got[:, :half_rows].reshape(ncl * half_rows, 3 * HD)
    upper = got[::-1, half_rows:].reshape(ncl * half_rows, 3 * HD)
    mine = jnp.concatenate([lower, upper], axis=0)
    q_head = mine[:, :HD]
    kv_mine = mine[:, HD:]

    yh = lax.axis_index("yhi")
    kv_other = lax.ppermute(kv_mine, "yhi", swap)
    kv_pair = jnp.concatenate([kv_mine, kv_other], axis=0)
    kv_all = z_ring(kv_pair, nz)

    span = ncl * half_rows
    total_tokens = 2 * ctx_count * half_rows
    r = jnp.arange(span, dtype=jnp.int32)
    q_tokens = jnp.concatenate([cg * span + r, total_tokens - (cg + 1) * span + r])
    q_lo = request_start(q_tokens, prompt_lengths)
    info = jnp.stack(
        [
            q_lo[0] // KB,
            cg,
            q_lo[span] // KB,
            2 * groups - 1 - cg,
            (z_idx * nyh) % groups,
            jnp.asarray(groups, jnp.int32),
            yh,
        ]
    ).astype(jnp.int32)
    out_head = attention(info, q_head, kv_all, q_tokens[:, None], q_lo[:, None])

    out_lower = out_head[:span].reshape(ncl, half_rows, HD)
    out_upper = out_head[span:].reshape(ncl, half_rows, HD)[::-1]
    out_send = jnp.stack([out_lower, out_upper], axis=1).reshape(ncl, tok_rows, HD)

    picked = kv_all.reshape(groups, 2, ncl, half_rows, 2 * HD)
    picked = lax.dynamic_slice_in_dim(picked, cg * ncl, ncl, axis=3)
    paired = picked.reshape(nz, nyh, 2, ncl, ncl, 2 * HD)
    picked = jnp.where(yh == 0, paired, paired[:, ::-1]).reshape(groups, 2, ncl, ncl, 2 * HD)
    doubled = jnp.concatenate([picked, picked], axis=0)
    natural = lax.dynamic_slice_in_dim(doubled, (groups - (z_idx * nyh) % groups) % groups, groups, axis=0)
    cache_lower = natural[:, 0].reshape(groups * ncl, ncl, 2 * HD)
    cache_upper = natural[::-1, 1].reshape(groups * ncl, ncl, 2 * HD)
    cache = jnp.concatenate([cache_lower, cache_upper], axis=0).transpose(1, 0, 2)
    send = jnp.concatenate([out_send, cache], axis=2)
    recv = lax.all_to_all(send, CL, split_axis=0, concat_axis=0, tiled=True)
    recv = recv.transpose(1, 0, 2)
    attn_out = recv[:, :, :HD].reshape(tok_rows, local_width)
    key_cache = recv[:, :, HD : 2 * HD].reshape(tok_rows, local_width)
    value_cache = recv[:, :, 2 * HD :].reshape(tok_rows, local_width)
    return attn_out, key_cache, value_cache


def solution(mesh):
    ctx_size = mesh.shape["ctx"]
    tp_size = mesh.shape["tp"]
    nz = 8
    split = Mesh(
        mesh.devices.reshape(nz, 2, 2, ctx_size // (nz * 4), tp_size // 2, 2),
        ("z", "yhi", "ylo", "xlo", "xhi", "core"),
    )
    rows = P(CTX, TP)
    placed = (rows, P(None, TP), P(None, TP), P(None, TP), P(TP), P(TP), P())
    return jax.shard_map(
        per_device,
        mesh=split,
        in_specs=placed,
        out_specs=(rows, rows, rows),
        check_vma=False,
    )
```
